32 devices in a mesh: seq: 8 (over y, x, core), dec: 4 (over z).
Axes of the slice: x: 2, y: 2, z: 4, core: 2. Of those that a mesh axis runs over, the one named last changes fastest.
Arguments:
- tokens: bfloat16 [512, 8, 1536], P('dec', 'seq'), may hold values from -400 to 400
- norm_gain: float32 [1536], replicated, may hold values from 0.1 to 1.9
- lengths: int32 [8], replicated, may hold values from 0 to 1536
- w_query: bfloat16 [1536, 1536], P(None, 'dec'), may hold values from -0.3125 to 0.3125
- w_keyval: bfloat16 [1536, 1024], P(None, 'dec'), may hold values from -0.15625 to 0.15625
- w_out: bfloat16 [1536, 1536], P('dec'), may hold values from -0.75 to 0.75
- kv_cache: bfloat16 [8, 8, 1536, 128], P('seq', 'dec'), may hold values from -60 to 60
- prior_kv: bfloat16 [8, 2, 8, 2048, 128], P('seq', None, 'dec'), may hold values from -4 to 4
- owners: int32 [8, 3, 8, 16, 1], P('seq', None, 'dec'), may hold values from 0 to 7; in each aligned block of 32 rows (0 to 31, 32 to 63, ..., all dimensions but the last counted through in order) at most 4 rows name the same one
Outputs:
- attention_out: bfloat16 [512, 8, 1536], P('dec', 'seq')
- decode_pool: bfloat16 [8, 4, 3, 8, 4, 128, 128], P('seq', 'dec')
The draws below stay inside these ranges and needn't reach their ends.
Inputs may be any that keep to these rules, and one draw needn't show every extreme that they name: `owners`: for one request, one layer and the 2 KV heads of one decode group (32 blocks, consecutive in the array), no owner is named more than 4 times.
All inputs are finite; a program needn't handle non-finite values.
Results may differ from the reference program's by a relative error of at most 0.012.
The reference program's roundings to bfloat16 on the way count: a program that leaves them out, or rounds other values in their place, can miss the bound.
Values may be sent and summed in bfloat16 or wider, within the bound.
No kernel may reach another device: no remote copies, remote signals or barrier semaphores. Data moves between devices by JAX's collectives and lax.ppermute only.
A program may use at most 128 MiB of HBM per device.

```python
import math
import jax
import jax.numpy as jnp
import numpy as np
from jax import lax

D = 1536
QH = 24
KVH = 8
HD = 64
NEW_TOK = 512
BLK = 128
HL = 3
REQS = 8
OWNERS = 8
CTX = 1536
NB = 16
GH = 2
CAP = 4
N_DEC = 4


def draw_tokens(key, part):
    base_key, row_key, column_key = jax.random.split(key, 3)
    full_shape = (NEW_TOK, REQS, D)
    base_values = jnp.clip(jax.random.normal(base_key, full_shape, jnp.float32), -4.0, 4.0)
    row_scale = jnp.exp(jax.random.uniform(row_key, (NEW_TOK, REQS, 1), jnp.float32, 0.0, math.log(10.0)))
    column_scale = jnp.exp(jax.random.uniform(column_key, (D,), jnp.float32, 0.0, math.log(10.0)))
    return (base_values * row_scale * column_scale).astype(jnp.bfloat16)


def draw_kv_cache(key, part):
    base_key = jax.random.fold_in(key, 0)
    full_shape = (REQS, KVH, CTX, 2 * HD)
    result_values = jnp.clip(jax.random.normal(base_key, full_shape, jnp.float32), -4.0, 4.0)
    return result_values.astype(jnp.bfloat16)


def with_ends(entries, key, low, largest):
    spot = [jax.random.randint(jax.random.fold_in(key, axis), (), 0, length) for axis, length in enumerate(entries.shape)]
    widest = entries.shape.index(max(entries.shape))
    neighbour = spot[:widest] + [(spot[widest] + 1) % entries.shape[widest]] + spot[widest + 1:]
    return entries.at[tuple(spot)].set(low).at[tuple(neighbour)].set(largest)


def shard_levels(rng, shape, shards, low, top_value):
    loudness = 1.0
    for axis_at, shards_of in shards:
        draws = jax.random.uniform(jax.random.fold_in(jax.random.fold_in(rng, 6), axis_at), (shards_of,), jnp.float32, low / len(shards), top_value / len(shards))
        loudness = loudness * jnp.repeat(jnp.exp(draws), shape[axis_at] // shards_of).reshape((-1,) + (1,) * (len(shape) - 1 - axis_at))
    return loudness


def assign_block(rng, own, number, rows, number_of, top, bound, slope):
    sequence = jax.random.permutation(rng, number_of)
    packed, usual = load_shares(number_of, rows * top, bound, slope, True), load_shares(number_of, rows * top, bound, slope, False)
    places = jnp.arange(number_of)

    def named(tallies, turn):
        used = int((tallies > 0).sum())
        fixed = max(1, used // 4)
        shifted = fixed + (places - fixed + turn * (used - fixed)) % max(1, number_of - fixed)
        return jnp.zeros((number_of,), jnp.int32).at[sequence[jnp.where(places < fixed, places, shifted)]].set(jnp.asarray(tallies, jnp.int32))

    tallies = jnp.where(number % 4 == 0, named(packed, number // 4), named(usual, number - number // 4 - 1))
    mixed = jax.random.permutation(jax.random.fold_in(own, 3), number_of)
    giver, receiver = mixed[0:number_of // 2 * 2:2], mixed[1:number_of // 2 * 2:2]
    slack = jnp.minimum(tallies[giver] - 1, bound - tallies[receiver]) // 2
    slack = jnp.where((giver == sequence[0]) | (receiver == sequence[0]) | (tallies[receiver] == 0), 0, jnp.maximum(slack, 0))
    shifted = jax.random.randint(jax.random.fold_in(own, 4), (number_of // 2,), 0, 1 << 20) % (slack + 1)
    tallies = tallies.at[giver].add(-shifted).at[receiver].add(shifted)
    labels = jnp.searchsorted(jnp.cumsum(tallies), jnp.arange(rows * top), side="right").astype(jnp.int32)
    table = labels.reshape(top, rows).T
    table = table[jax.random.permutation(jax.random.fold_in(own, 1), rows)]
    turn = jax.random.randint(jax.random.fold_in(own, 2), (rows, 1), 0, top)
    return jnp.take_along_axis(table, (jnp.arange(top)[None, :] + turn) % top, axis=1)


def load_shares(number_of, total, limit, slope, full):
    portions = [(1 << 20) // math.isqrt(standing ** slope) + 1 for standing in range(1, number_of + 1)]
    largest = limit if full else min(limit, max(-(-total // number_of), total * portions[0] // sum(portions)))
    least = 1 if total - largest >= number_of - 1 else 0
    counts, surplus = [largest] + [least] * (number_of - 1), total - largest - least * (number_of - 1)
    while surplus > 0:
        movable = [i for i in range(1, number_of) if counts[i] < largest] or [i for i in range(1, number_of) if counts[i] < limit]
        whole, left = sum([portions[i] for i in movable]), surplus
        for i in movable:
            extra = min(limit - counts[i], max(1, left * portions[i] // whole), surplus)
            counts[i] = counts[i] + extra
            surplus = surplus - extra
    return np.array(counts)


def gaussian(own_key, dims, spread, reach, cuts=(), kind=jnp.bfloat16):
    result = spread * jax.random.normal(own_key, dims, jnp.float32)
    if cuts:
        result = result * shard_levels(own_key, dims, cuts, -0.22, 0.18)
    return jnp.clip(result, -reach, reach).astype(kind)


def setup_inputs(seed: int = 0) -> dict:
    seeds = jax.random.split(jax.random.key(seed), 10)
    tokens = draw_tokens(jax.random.fold_in(seeds[9], 71), 0)
    norm_gain = jnp.clip(1.0 + 0.18 * jax.random.normal(seeds[1], (D,), jnp.float32), 0.1, 1.9)
    lengths = with_ends(jax.random.randint(seeds[2], (REQS,), 0, CTX + 1), jax.random.fold_in(seeds[2], 1), 0, CTX).astype(jnp.int32)
    w_query = gaussian(seeds[3], (D, QH * HD), (D // 4) ** -0.5, 0.3125, ((1, 4),))
    w_keyval = gaussian(seeds[4], (D, KVH * 2 * HD), D ** -0.5, 0.15625, ((1, 4),))
    w_out = gaussian(seeds[5], (QH * HD, D), HD ** -0.5, 0.75, ((0, 4),))
    kv_cache = draw_kv_cache(jax.random.fold_in(seeds[9], 71), 0)
    prior_kv = gaussian(seeds[7], (REQS, HL - 1, KVH, NB * BLK, 2 * HD), 1.0, 4.0, ((0, 8), (2, 4)))
    owners_keys = jax.random.split(jax.random.fold_in(seeds[8], 1), REQS * HL * KVH * NB // (GH * NB))
    owners_turns = jax.random.permutation(jax.random.fold_in(seeds[8], 3), REQS * HL * KVH * NB // (GH * NB))
    owners = jax.vmap(lambda own, number: assign_block(jax.random.fold_in(seeds[8], 2), own, number, GH * NB, OWNERS, 1, CAP, 2))(owners_keys, owners_turns).reshape((REQS, HL, KVH, NB, 1))
    return dict(tokens=tokens, norm_gain=norm_gain, lengths=lengths, w_query=w_query, w_keyval=w_keyval, w_out=w_out, kv_cache=kv_cache, prior_kv=prior_kv, owners=owners)


EPSILON = 1e-06
ROPE_BASE = 10000.0

def rotate(values, angles):
    half_dim = values.shape[-1] // 2
    first_half = values[..., :half_dim]
    second_half = values[..., half_dim:]
    cosine = jnp.cos(angles)
    sine_part = jnp.sin(angles)
    return jnp.concatenate([first_half * cosine - second_half * sine_part, second_half * cosine + first_half * sine_part], axis=-1)

def reference(tokens, norm_gain, lengths, w_query, w_keyval, w_out, kv_cache, prior_kv, owners):
    widened = tokens.astype(jnp.float32)
    normed = (widened * lax.rsqrt(lax.optimization_barrier(jnp.mean(widened * widened, axis=-1, keepdims=True)) + EPSILON) * norm_gain).astype(jnp.bfloat16)
    flattened = normed.reshape(NEW_TOK * REQS, D)
    queries = jnp.dot(flattened, w_query, preferred_element_type=jnp.float32).reshape(NEW_TOK, REQS, QH, HD)
    key_value = jnp.dot(flattened, w_keyval, preferred_element_type=jnp.float32).reshape(NEW_TOK, REQS, KVH, 2 * HD)
    positions = (jnp.arange(NEW_TOK, dtype=jnp.int32)[:, None] + lengths[None, :]).astype(jnp.float32)
    inverse_freq = ROPE_BASE ** (-(jnp.arange(0, HD, 2, dtype=jnp.float32) / HD))
    angles = positions[:, :, None, None] * inverse_freq
    queries = rotate(queries, angles).astype(jnp.bfloat16)
    key_value = jnp.concatenate([rotate(key_value[..., :HD], angles), key_value[..., HD:]], axis=-1).astype(jnp.bfloat16)
    span_len = NB * BLK
    slot_ids = jnp.arange(span_len, dtype=jnp.int32)
    token_ids = jnp.arange(NEW_TOK, dtype=jnp.int32)
    score_scale = HD ** (-0.5)
    zero_index = jnp.zeros((), jnp.int32)

    def per_request(inputs):
        req_length, query_rows, fresh_rows, cached, earlier = inputs
        req_length = req_length.astype(jnp.int32)
        padded = jnp.pad(cached, ((0, 0), (0, span_len - CTX), (0, 0)))
        kept_cache = jnp.where((slot_ids < req_length)[None, :, None], padded, jnp.zeros_like(padded))
        assembled = lax.dynamic_update_slice(kept_cache, jnp.transpose(fresh_rows, (1, 0, 2)), (zero_index, req_length, zero_index))
        grouped = query_rows.reshape(NEW_TOK, KVH, QH // KVH, HD).astype(jnp.float32)
        key_part = assembled[..., :HD].astype(jnp.float32)
        value_part = assembled[..., HD:].astype(jnp.float32)
        scores = jnp.einsum('thjd,hpd->hjtp', grouped, key_part) * score_scale
        visible = slot_ids[None, :] <= (req_length + token_ids)[:, None]
        row_max = lax.optimization_barrier(jnp.max(jnp.where(visible, scores, -jnp.inf), axis=-1, keepdims=True))
        weights = jnp.where(visible, jnp.exp(scores - row_max), 0.0)
        row_total = lax.optimization_barrier(jnp.sum(weights, axis=-1, keepdims=True))
        rounded = lax.optimization_barrier(weights.astype(jnp.bfloat16)).astype(jnp.float32)
        mixed_rows = jnp.einsum('hjtp,hpd->thjd', rounded, value_part) / jnp.transpose(row_total, (2, 0, 1, 3))
        context = mixed_rows.astype(jnp.bfloat16).reshape(NEW_TOK, QH * HD)
        live_mask = (slot_ids < req_length + NEW_TOK)[None, None, :, None]
        earlier_kept = jnp.where(live_mask, earlier, jnp.zeros_like(earlier))
        stacked = jnp.concatenate([earlier_kept, assembled[None]], axis=0)
        return (context, stacked)
    contexts, layers = lax.map(per_request, (lengths, jnp.transpose(queries, (1, 0, 2, 3)), jnp.transpose(key_value, (1, 0, 2, 3)), kv_cache, prior_kv))
    merged = jnp.transpose(contexts, (1, 0, 2)).reshape(NEW_TOK * REQS, QH * HD)
    attention_out = jnp.dot(merged, w_out, preferred_element_type=jnp.float32).astype(jnp.bfloat16).reshape(NEW_TOK, REQS, D)
    rows_group = GH * NB
    owner_rows = owners[..., 0].reshape(REQS, HL, N_DEC, rows_group)
    owner_hits = (owner_rows[..., None] == jnp.arange(OWNERS, dtype=jnp.int32)).astype(jnp.int32)
    owner_rank = lax.optimization_barrier(jnp.sum((jnp.cumsum(owner_hits, axis=3) - owner_hits) * owner_hits, axis=-1))
    block_rows = layers.reshape(REQS, HL, N_DEC, rows_group, BLK, 2 * HD)
    group_ids = jnp.arange(N_DEC, dtype=jnp.int32)[None, None, :, None]
    layer_ids = jnp.arange(HL, dtype=jnp.int32)[None, :, None, None]
    request_ids = jnp.arange(REQS, dtype=jnp.int32)[:, None, None, None]
    decode_pool = jnp.zeros((OWNERS, N_DEC, HL, REQS, CAP, BLK, 2 * HD), jnp.bfloat16)
    decode_pool = decode_pool.at[owner_rows, group_ids, layer_ids, request_ids, owner_rank].set(block_rows)
    return (attention_out, decode_pool)
```

```python
import jax
import jax.numpy as jnp
from jax import lax
from jax.sharding import PartitionSpec as P

HD = 64
NEW_TOK = 512


EPSILON = 1e-06
ROPE_BASE = 10000.0


def rotate(values, angles):
    half_dim = values.shape[-1] // 2
    first_half = values[..., :half_dim]
    second_half = values[..., half_dim:]
    cosine = jnp.cos(angles)
    sine_part = jnp.sin(angles)
    return jnp.concatenate(
        [
            first_half * cosine - second_half * sine_part,
            second_half * cosine + first_half * sine_part,
        ],
        axis=-1,
    )


def local(tokens, norm_gain, lengths, w_query, w_keyval, w_out, kv_cache, prior_kv, owners):
    query_cols = w_query.shape[1]
    heads_here = kv_cache.shape[1]
    layer_count = owners.shape[1]
    block_count = owners.shape[3]
    span_len = prior_kv.shape[3]
    block_len = span_len // block_count
    kv_width = 2 * HD
    rows_here = heads_here * block_count
    owner_count = lax.axis_size("seq")
    capacity = (rows_here + owner_count - 1) // owner_count
    req_length = lengths[lax.axis_index("seq")]
    slot_ids = jnp.arange(span_len, dtype=jnp.int32)
    zero_index = jnp.zeros((), jnp.int32)
    owner_rows = owners[0, :, :, :, 0].reshape(layer_count, rows_here)
    owner_hits = (owner_rows[:, :, None] == jnp.arange(owner_count, dtype=jnp.int32)).astype(
        jnp.int32
    )
    owner_rank = jnp.sum((jnp.cumsum(owner_hits, axis=1) - owner_hits) * owner_hits, axis=-1)
    row_ids = jnp.arange(rows_here, dtype=jnp.int32)
    match = (owner_rows[:, None, None, :] == jnp.arange(owner_count, dtype=jnp.int32)[None, :, None, None]) & (
        owner_rank[:, None, None, :] == jnp.arange(capacity, dtype=jnp.int32)[None, None, :, None]
    )
    pick_row = jnp.sum(jnp.where(match, row_ids, 0), axis=-1)
    pick_ok = jnp.any(match, axis=-1)
    me = lax.axis_index("seq")
    widened = tokens.astype(jnp.float32)
    normed = (
        widened
        * lax.rsqrt(jnp.mean(widened * widened, axis=-1, keepdims=True) + EPSILON)
        * norm_gain
    ).astype(jnp.bfloat16)
    portion = lax.all_gather(normed, "dec", axis=0, tiled=True)
    flattened = portion.reshape(-1, portion.shape[-1])
    combined = jnp.concatenate(
        [
            jnp.dot(flattened, w_query, preferred_element_type=jnp.float32),
            jnp.dot(flattened, w_keyval, preferred_element_type=jnp.float32),
        ],
        axis=-1,
    )
    positions = (jnp.arange(NEW_TOK, dtype=jnp.int32) + req_length).astype(jnp.float32)
    inverse_freq = ROPE_BASE ** (-(jnp.arange(0, HD, 2, dtype=jnp.float32) / HD))
    angles = positions[:, None, None] * inverse_freq
    queries = rotate(
        combined[:, :query_cols].reshape(NEW_TOK, query_cols // HD, HD), angles
    ).astype(jnp.bfloat16)
    key_value = combined[:, query_cols:].reshape(NEW_TOK, heads_here, kv_width)
    key_value = jnp.concatenate(
        [rotate(key_value[..., :HD], angles), key_value[..., HD:]], axis=-1
    ).astype(jnp.bfloat16)
    cached = kv_cache[0]
    padded = jnp.pad(cached, ((0, 0), (0, span_len - cached.shape[1]), (0, 0)))
    kept_cache = jnp.where((slot_ids < req_length)[None, :, None], padded, jnp.zeros_like(padded))
    fresh_rows = jnp.transpose(key_value, (1, 0, 2))
    assembled = lax.dynamic_update_slice(
        kept_cache, fresh_rows, (zero_index, req_length, zero_index)
    )
    grouped = queries.reshape(NEW_TOK, heads_here, query_cols // HD // heads_here, HD)
    visible = slot_ids[None, :] <= (req_length + jnp.arange(NEW_TOK, dtype=jnp.int32))[:, None]
    score_scale = HD ** (-0.5)
    contexts = []
    for head_index in range(heads_here):
        key_part = assembled[head_index, :, :HD]
        value_part = assembled[head_index, :, HD:]
        scores = (
            jnp.einsum(
                "tjd,pd->jtp", grouped[:, head_index], key_part, preferred_element_type=jnp.float32
            )
            * score_scale
        )
        row_max = jnp.max(jnp.where(visible, scores, -jnp.inf), axis=-1, keepdims=True)
        weights = jnp.where(visible, jnp.exp(scores - row_max), 0.0)
        row_total = jnp.sum(weights, axis=-1, keepdims=True)
        mixed_rows = jnp.einsum(
            "jtp,pd->tjd",
            weights.astype(jnp.bfloat16),
            value_part,
            preferred_element_type=jnp.float32,
        )
        contexts.append((mixed_rows / jnp.transpose(row_total, (1, 0, 2))).astype(jnp.bfloat16))
    context = jnp.concatenate(contexts, axis=1).reshape(NEW_TOK, query_cols)
    product = jnp.dot(context, w_out, preferred_element_type=jnp.float32)
    summed = lax.psum_scatter(
        product.reshape(
            NEW_TOK // lax.axis_size("dec") * lax.axis_size("dec"), 1, product.shape[-1]
        ).astype(jnp.bfloat16),
        "dec",
        scatter_dimension=0,
        tiled=True,
    )
    earlier_blocks = prior_kv[0].reshape(layer_count - 1, rows_here, block_len, kv_width)
    current_blocks = assembled.reshape(1, rows_here, block_len, kv_width)
    in_block = jnp.arange(block_len, dtype=jnp.int32)

    def pick(blocks, layers, target):
        rows = lax.dynamic_index_in_dim(pick_row[layers], target, axis=1, keepdims=False)
        ok = lax.dynamic_index_in_dim(pick_ok[layers], target, axis=1, keepdims=False)
        layer_ids = jnp.arange(blocks.shape[0], dtype=jnp.int32)[:, None]
        taken = blocks[layer_ids, rows]
        position = (rows % block_count)[:, :, None] * block_len + in_block
        keep = ok[:, :, None] & (position < req_length + NEW_TOK)
        return jnp.where(keep[..., None], taken, jnp.zeros_like(taken))

    pool = jnp.zeros((layer_count, owner_count, capacity, block_len, kv_width), jnp.bfloat16)
    for shift in range(owner_count):
        target = lax.rem(me + shift, owner_count)
        source = lax.rem(me - shift + owner_count, owner_count)
        parts = [
            pick(earlier_blocks, slice(0, layer_count - 1), target),
            pick(current_blocks, slice(layer_count - 1, layer_count), target),
        ]
        if shift:
            perm = [(i, (i + shift) % owner_count) for i in range(owner_count)]
            parts = [lax.ppermute(part, "seq", perm) for part in parts]
        piece = jnp.concatenate(parts, axis=0)
        pool = lax.dynamic_update_slice(
            pool, piece[:, None], (zero_index, source, zero_index, zero_index, zero_index)
        )
    decode_pool = pool.reshape(1, 1, layer_count, owner_count, capacity, block_len, kv_width)
    return (summed, decode_pool)


def solution(mesh):
    in_specs = (
        P("dec", "seq", None),
        P(),
        P(),
        P(None, "dec"),
        P(None, "dec"),
        P("dec", None),
        P("seq", "dec", None, None),
        P("seq", None, "dec", None, None),
        P("seq", None, "dec", None, None),
    )
    out_specs = (P("dec", "seq", None), P("seq", "dec", None, None, None, None, None))
    return jax.shard_map(local, mesh=mesh, in_specs=in_specs, out_specs=out_specs, check_vma=False)
```

```python
import jax
import jax.numpy as jnp
from jax import lax
from jax.sharding import PartitionSpec as P

HD = 64
NEW_TOK = 512


EPSILON = 1e-06
ROPE_BASE = 10000.0


def rotate(values, angles):
    half_dim = values.shape[-1] // 2
    first_half = values[..., :half_dim]
    second_half = values[..., half_dim:]
    cosine = jnp.cos(angles)
    sine_part = jnp.sin(angles)
    return jnp.concatenate(
        [
            first_half * cosine - second_half * sine_part,
            second_half * cosine + first_half * sine_part,
        ],
        axis=-1,
    )


def route_blocks(dispatch_table, block_data):
    layers = dispatch_table.shape[0]
    same_layer = jnp.eye(layers, dtype=dispatch_table.dtype)
    spread = dispatch_table[:, :, :, None, :] * same_layer[:, None, None, :, None]
    moved_blocks = jnp.einsum(
        "locms,msbw->olcbw", spread, block_data, preferred_element_type=jnp.float32
    ).astype(jnp.bfloat16)
    shape = moved_blocks.shape
    return moved_blocks.reshape(shape[0], shape[1] * shape[2] * shape[3], shape[4])


def local(tokens, norm_gain, lengths, w_query, w_keyval, w_out, kv_cache, prior_kv, owners):
    query_cols = w_query.shape[1]
    heads_here = kv_cache.shape[1]
    layer_count = owners.shape[1]
    block_count = owners.shape[3]
    span_len = prior_kv.shape[3]
    block_len = span_len // block_count
    kv_width = 2 * HD
    rows_here = heads_here * block_count
    owner_count = lax.axis_size("seq")
    capacity = (rows_here + owner_count - 1) // owner_count
    req_length = lengths[lax.axis_index("seq")]
    slot_ids = jnp.arange(span_len, dtype=jnp.int32)
    zero_index = jnp.zeros((), jnp.int32)
    owner_rows = owners[0, :, :, :, 0].reshape(layer_count, rows_here)
    owner_hits = (owner_rows[:, :, None] == jnp.arange(owner_count, dtype=jnp.int32)).astype(
        jnp.int32
    )
    owner_rank = jnp.sum((jnp.cumsum(owner_hits, axis=1) - owner_hits) * owner_hits, axis=-1)
    slot_index = owner_rows * capacity + owner_rank
    dispatch = (
        slot_index[:, None, :] == jnp.arange(owner_count * capacity, dtype=jnp.int32)[None, :, None]
    ).astype(jnp.bfloat16)
    dispatch = dispatch.reshape(layer_count, owner_count, capacity, rows_here)
    live_mask = (slot_ids < req_length + NEW_TOK)[None, None, :, None]
    earlier = jnp.where(live_mask, prior_kv[0], jnp.zeros_like(prior_kv[0]))
    earlier_rows = earlier.reshape(layer_count - 1, rows_here, block_len, kv_width)
    received_early = lax.all_to_all(
        route_blocks(dispatch[: layer_count - 1], earlier_rows), "seq", 0, 0, tiled=True
    )
    widened = tokens.astype(jnp.float32)
    normed = (
        widened
        * lax.rsqrt(jnp.mean(widened * widened, axis=-1, keepdims=True) + EPSILON)
        * norm_gain
    ).astype(jnp.bfloat16)
    portion = lax.all_gather(normed, "dec", axis=0, tiled=True)
    received_early, portion = lax.optimization_barrier((received_early, portion))
    flattened = portion.reshape(-1, portion.shape[-1])
    combined = jnp.concatenate(
        [
            jnp.dot(flattened, w_query, preferred_element_type=jnp.float32),
            jnp.dot(flattened, w_keyval, preferred_element_type=jnp.float32),
        ],
        axis=-1,
    )
    positions = (jnp.arange(NEW_TOK, dtype=jnp.int32) + req_length).astype(jnp.float32)
    inverse_freq = ROPE_BASE ** (-(jnp.arange(0, HD, 2, dtype=jnp.float32) / HD))
    angles = positions[:, None, None] * inverse_freq
    queries = rotate(
        combined[:, :query_cols].reshape(NEW_TOK, query_cols // HD, HD), angles
    ).astype(jnp.bfloat16)
    key_value = combined[:, query_cols:].reshape(NEW_TOK, heads_here, kv_width)
    key_value = jnp.concatenate(
        [rotate(key_value[..., :HD], angles), key_value[..., HD:]], axis=-1
    ).astype(jnp.bfloat16)
    cached = kv_cache[0]
    padded = jnp.pad(cached, ((0, 0), (0, span_len - cached.shape[1]), (0, 0)))
    kept_cache = jnp.where((slot_ids < req_length)[None, :, None], padded, jnp.zeros_like(padded))
    fresh_rows = jnp.transpose(key_value, (1, 0, 2))
    assembled = lax.dynamic_update_slice(
        kept_cache, fresh_rows, (zero_index, req_length, zero_index)
    )
    grouped = queries.reshape(NEW_TOK, heads_here, query_cols // HD // heads_here, HD)
    visible = slot_ids[None, :] <= (req_length + jnp.arange(NEW_TOK, dtype=jnp.int32))[:, None]
    score_scale = HD ** (-0.5)
    contexts = []
    for head_index in range(heads_here):
        key_part = assembled[head_index, :, :HD]
        value_part = assembled[head_index, :, HD:]
        scores = (
            jnp.einsum(
                "tjd,pd->jtp", grouped[:, head_index], key_part, preferred_element_type=jnp.float32
            )
            * score_scale
        )
        row_max = jnp.max(jnp.where(visible, scores, -jnp.inf), axis=-1, keepdims=True)
        weights = jnp.where(visible, jnp.exp(scores - row_max), 0.0)
        row_total = jnp.sum(weights, axis=-1, keepdims=True)
        mixed_rows = jnp.einsum(
            "jtp,pd->tjd",
            weights.astype(jnp.bfloat16),
            value_part,
            preferred_element_type=jnp.float32,
        )
        contexts.append((mixed_rows / jnp.transpose(row_total, (1, 0, 2))).astype(jnp.bfloat16))
    context = jnp.concatenate(contexts, axis=1).reshape(NEW_TOK, query_cols)
    product = jnp.dot(context, w_out, preferred_element_type=jnp.float32)
    summed = lax.psum_scatter(
        product.reshape(
            NEW_TOK // lax.axis_size("dec") * lax.axis_size("dec"), 1, product.shape[-1]
        ).astype(jnp.bfloat16),
        "dec",
        scatter_dimension=0,
        tiled=True,
    )
    current_rows = assembled.reshape(1, rows_here, block_len, kv_width)
    received_last = lax.all_to_all(
        route_blocks(dispatch[layer_count - 1 :], current_rows), "seq", 0, 0, tiled=True
    )
    received = jnp.concatenate(
        [
            received_early.reshape(owner_count, layer_count - 1, capacity, block_len, kv_width),
            received_last.reshape(owner_count, 1, capacity, block_len, kv_width),
        ],
        axis=1,
    )
    decode_pool = jnp.transpose(received, (1, 0, 2, 3, 4)).reshape(
        1, 1, layer_count, owner_count, capacity, block_len, kv_width
    )
    return (summed, decode_pool)


def solution(mesh):
    in_specs = (
        P("dec", "seq", None),
        P(),
        P(),
        P(None, "dec"),
        P(None, "dec"),
        P("dec", None),
        P("seq", "dec", None, None),
        P("seq", None, "dec", None, None),
        P("seq", None, "dec", None, None),
    )
    out_specs = (P("dec", "seq", None), P("seq", "dec", None, None, None, None, None))
    return jax.shard_map(local, mesh=mesh, in_specs=in_specs, out_specs=out_specs, check_vma=False)
```

```python
import jax
import jax.numpy as jnp
from jax import lax
from jax.sharding import PartitionSpec as P

HD = 64
NEW_TOK = 512


EPSILON = 1e-06
ROPE_BASE = 10000.0


def rotate(values, angles):
    half_dim = values.shape[-1] // 2
    first_half = values[..., :half_dim]
    second_half = values[..., half_dim:]
    cosine = jnp.cos(angles)
    sine_part = jnp.sin(angles)
    return jnp.concatenate(
        [
            first_half * cosine - second_half * sine_part,
            second_half * cosine + first_half * sine_part,
        ],
        axis=-1,
    )


def route_blocks(dispatch_table, block_data):
    layers = dispatch_table.shape[0]
    same_layer = jnp.eye(layers, dtype=dispatch_table.dtype)
    spread = dispatch_table[:, :, :, None, :] * same_layer[:, None, None, :, None]
    moved_blocks = jnp.einsum(
        "locms,msbw->olcbw", spread, block_data, preferred_element_type=jnp.float32
    ).astype(jnp.bfloat16)
    shape = moved_blocks.shape
    return moved_blocks.reshape(shape[0], shape[1] * shape[2] * shape[3], shape[4])


def local(tokens, norm_gain, lengths, w_query, w_keyval, w_out, kv_cache, prior_kv, owners):
    query_cols = w_query.shape[1]
    heads_here = kv_cache.shape[1]
    layer_count = owners.shape[1]
    block_count = owners.shape[3]
    span_len = prior_kv.shape[3]
    block_len = span_len // block_count
    kv_width = 2 * HD
    rows_here = heads_here * block_count
    owner_count = lax.axis_size("seq")
    capacity = (rows_here + owner_count - 1) // owner_count
    req_length = lengths[lax.axis_index("seq")]
    slot_ids = jnp.arange(span_len, dtype=jnp.int32)
    zero_index = jnp.zeros((), jnp.int32)
    owner_rows = owners[0, :, :, :, 0].reshape(layer_count, rows_here)
    owner_hits = (owner_rows[:, :, None] == jnp.arange(owner_count, dtype=jnp.int32)).astype(
        jnp.int32
    )
    owner_rank = jnp.sum((jnp.cumsum(owner_hits, axis=1) - owner_hits) * owner_hits, axis=-1)
    slot_index = owner_rows * capacity + owner_rank
    dispatch = (
        slot_index[:, None, :] == jnp.arange(owner_count * capacity, dtype=jnp.int32)[None, :, None]
    ).astype(jnp.bfloat16)
    dispatch = dispatch.reshape(layer_count, owner_count, capacity, rows_here)
    live_mask = (slot_ids < req_length + NEW_TOK)[None, None, :, None]
    earlier = jnp.where(live_mask, prior_kv[0], jnp.zeros_like(prior_kv[0]))
    earlier_rows = earlier.reshape(layer_count - 1, rows_here, block_len, kv_width)
    received_early = lax.all_to_all(
        route_blocks(dispatch[: layer_count - 1], earlier_rows), "seq", 0, 0, tiled=True
    )
    widened = tokens.astype(jnp.float32)
    normed = (
        widened
        * lax.rsqrt(jnp.mean(widened * widened, axis=-1, keepdims=True) + EPSILON)
        * norm_gain
    ).astype(jnp.bfloat16)
    portion = lax.all_gather(normed, "dec", axis=0, tiled=True)
    received_early, portion = lax.optimization_barrier((received_early, portion))
    flattened = portion.reshape(-1, portion.shape[-1])
    combined = jnp.concatenate(
        [
            jnp.dot(flattened, w_query, preferred_element_type=jnp.float32),
            jnp.dot(flattened, w_keyval, preferred_element_type=jnp.float32),
        ],
        axis=-1,
    )
    positions = (jnp.arange(NEW_TOK, dtype=jnp.int32) + req_length).astype(jnp.float32)
    inverse_freq = ROPE_BASE ** (-(jnp.arange(0, HD, 2, dtype=jnp.float32) / HD))
    angles = positions[:, None, None] * inverse_freq
    queries = rotate(
        combined[:, :query_cols].reshape(NEW_TOK, query_cols // HD, HD), angles
    ).astype(jnp.bfloat16)
    key_value = combined[:, query_cols:].reshape(NEW_TOK, heads_here, kv_width)
    key_value = jnp.concatenate(
        [rotate(key_value[..., :HD], angles), key_value[..., HD:]], axis=-1
    ).astype(jnp.bfloat16)
    cached = kv_cache[0]
    padded = jnp.pad(cached, ((0, 0), (0, span_len - cached.shape[1]), (0, 0)))
    kept_cache = jnp.where((slot_ids < req_length)[None, :, None], padded, jnp.zeros_like(padded))
    fresh_rows = jnp.transpose(key_value, (1, 0, 2))
    assembled = lax.dynamic_update_slice(
        kept_cache, fresh_rows, (zero_index, req_length, zero_index)
    )
    grouped = queries.reshape(NEW_TOK, heads_here, query_cols // HD // heads_here, HD)
    dec_count = lax.axis_size("dec")
    chunk_len = NEW_TOK // dec_count
    half_len = chunk_len // 2
    score_scale = HD ** (-0.5)

    def attend(half):
        row_ids = (
            jnp.arange(dec_count, dtype=jnp.int32)[:, None] * chunk_len
            + half * half_len
            + jnp.arange(half_len, dtype=jnp.int32)[None, :]
        ).reshape(-1)
        rows = grouped.reshape(dec_count, 2, half_len, *grouped.shape[1:])[:, half].reshape(
            dec_count * half_len, *grouped.shape[1:]
        )
        visible = slot_ids[None, :] <= (req_length + row_ids)[:, None]
        contexts = []
        for head_index in range(heads_here):
            key_part = assembled[head_index, :, :HD]
            value_part = assembled[head_index, :, HD:]
            scores = (
                jnp.einsum(
                    "tjd,pd->jtp", rows[:, head_index], key_part, preferred_element_type=jnp.float32
                )
                * score_scale
            )
            row_max = jnp.max(jnp.where(visible, scores, -jnp.inf), axis=-1, keepdims=True)
            weights = jnp.where(visible, jnp.exp(scores - row_max), 0.0)
            row_total = jnp.sum(weights, axis=-1, keepdims=True)
            mixed_rows = jnp.einsum(
                "jtp,pd->tjd",
                weights.astype(jnp.bfloat16),
                value_part,
                preferred_element_type=jnp.float32,
            )
            contexts.append((mixed_rows / jnp.transpose(row_total, (1, 0, 2))).astype(jnp.bfloat16))
        context = jnp.concatenate(contexts, axis=1).reshape(dec_count * half_len, query_cols)
        product = jnp.dot(context, w_out, preferred_element_type=jnp.float32)
        return lax.psum_scatter(
            product.reshape(dec_count * half_len, 1, product.shape[-1]).astype(jnp.bfloat16),
            "dec",
            scatter_dimension=0,
            tiled=True,
        )

    summed = jnp.concatenate([attend(0), attend(1)], axis=0)
    current_rows = assembled.reshape(1, rows_here, block_len, kv_width)
    received_last = lax.all_to_all(
        route_blocks(dispatch[layer_count - 1 :], current_rows), "seq", 0, 0, tiled=True
    )
    received = jnp.concatenate(
        [
            received_early.reshape(owner_count, layer_count - 1, capacity, block_len, kv_width),
            received_last.reshape(owner_count, 1, capacity, block_len, kv_width),
        ],
        axis=1,
    )
    decode_pool = jnp.transpose(received, (1, 0, 2, 3, 4)).reshape(
        1, 1, layer_count, owner_count, capacity, block_len, kv_width
    )
    return (summed, decode_pool)


def solution(mesh):
    in_specs = (
        P("dec", "seq", None),
        P(),
        P(),
        P(None, "dec"),
        P(None, "dec"),
        P("dec", None),
        P("seq", "dec", None, None),
        P("seq", None, "dec", None, None),
        P("seq", None, "dec", None, None),
    )
    out_specs = (P("dec", "seq", None), P("seq", "dec", None, None, None, None, None))
    return jax.shard_map(local, mesh=mesh, in_specs=in_specs, out_specs=out_specs, check_vma=False)
```

```python
import functools

import jax
import jax.numpy as jnp
from jax import lax
from jax.experimental import pallas as pl
from jax.experimental.pallas import tpu as pltpu
from jax.sharding import PartitionSpec as P

HD = 64
NEW_TOK = 512


EPSILON = 1e-06
ROPE_BASE = 10000.0


def rotate(values, angles):
    half_dim = values.shape[-1] // 2
    first_half = values[..., :half_dim]
    second_half = values[..., half_dim:]
    cosine = jnp.cos(angles)
    sine_part = jnp.sin(angles)
    return jnp.concatenate(
        [
            first_half * cosine - second_half * sine_part,
            second_half * cosine + first_half * sine_part,
        ],
        axis=-1,
    )


def route_blocks(dispatch_table, block_data):
    layers = dispatch_table.shape[0]
    same_layer = jnp.eye(layers, dtype=dispatch_table.dtype)
    spread = dispatch_table[:, :, :, None, :] * same_layer[:, None, None, :, None]
    moved_blocks = jnp.einsum(
        "locms,msbw->olcbw", spread, block_data, preferred_element_type=jnp.float32
    ).astype(jnp.bfloat16)
    shape = moved_blocks.shape
    return moved_blocks.reshape(shape[0], shape[1] * shape[2] * shape[3], shape[4])


def attention_kernel(length_ref, q_ref, k_ref, v_ref, out_ref, *, tile, scale):
    tile_index = pl.program_id(1)
    span = k_ref.shape[1]
    keys = k_ref[0]
    values = v_ref[0]
    token = lax.broadcasted_iota(jnp.int32, (tile, span), 0) + tile_index * tile
    slot = lax.broadcasted_iota(jnp.int32, (tile, span), 1)
    visible = slot <= length_ref[0] + token
    for group_index in range(q_ref.shape[1]):
        scores = (
            lax.dot_general(
                q_ref[0, group_index],
                keys,
                (((1,), (1,)), ((), ())),
                preferred_element_type=jnp.float32,
            )
            * scale
        )
        row_max = jnp.max(jnp.where(visible, scores, -jnp.inf), axis=-1, keepdims=True)
        weights = jnp.where(visible, jnp.exp(scores - row_max), 0.0)
        row_total = jnp.sum(weights, axis=-1, keepdims=True)
        mixed = jnp.dot(
            weights.astype(jnp.bfloat16), values, preferred_element_type=jnp.float32
        )
        out_ref[0, group_index] = (mixed / row_total).astype(out_ref.dtype)


def attend(length, queries, keys, values, tile=128):
    heads, group, tokens, width = queries.shape
    span = keys.shape[1]
    kernel = functools.partial(attention_kernel, tile=tile, scale=HD ** (-0.5))
    flops = 4 * heads * group * tokens * span * width
    return pl.pallas_call(
        kernel,
        out_shape=jax.ShapeDtypeStruct(queries.shape, jnp.bfloat16),
        grid_spec=pltpu.PrefetchScalarGridSpec(
            num_scalar_prefetch=1,
            grid=(heads, tokens // tile),
            in_specs=[
                pl.BlockSpec((1, group, tile, width), lambda h, i, n: (h, 0, i, 0)),
                pl.BlockSpec((1, span, width), lambda h, i, n: (h, 0, 0)),
                pl.BlockSpec((1, span, width), lambda h, i, n: (h, 0, 0)),
            ],
            out_specs=pl.BlockSpec((1, group, tile, width), lambda h, i, n: (h, 0, i, 0)),
        ),
        cost_estimate=pl.CostEstimate(
            flops=flops,
            transcendentals=heads * group * tokens * span,
            bytes_accessed=2 * (2 * queries.size + keys.size + values.size),
        ),
    )(length, queries, keys, values)


def local(tokens, norm_gain, lengths, w_query, w_keyval, w_out, kv_cache, prior_kv, owners):
    query_cols = w_query.shape[1]
    heads_here = kv_cache.shape[1]
    layer_count = owners.shape[1]
    block_count = owners.shape[3]
    span_len = prior_kv.shape[3]
    block_len = span_len // block_count
    kv_width = 2 * HD
    rows_here = heads_here * block_count
    owner_count = lax.axis_size("seq")
    capacity = (rows_here + owner_count - 1) // owner_count
    req_length = lengths[lax.axis_index("seq")]
    slot_ids = jnp.arange(span_len, dtype=jnp.int32)
    zero_index = jnp.zeros((), jnp.int32)
    owner_rows = owners[0, :, :, :, 0].reshape(layer_count, rows_here)
    owner_hits = (owner_rows[:, :, None] == jnp.arange(owner_count, dtype=jnp.int32)).astype(
        jnp.int32
    )
    owner_rank = jnp.sum((jnp.cumsum(owner_hits, axis=1) - owner_hits) * owner_hits, axis=-1)
    slot_index = owner_rows * capacity + owner_rank
    dispatch = (
        slot_index[:, None, :] == jnp.arange(owner_count * capacity, dtype=jnp.int32)[None, :, None]
    ).astype(jnp.bfloat16)
    dispatch = dispatch.reshape(layer_count, owner_count, capacity, rows_here)
    live_mask = (slot_ids < req_length + NEW_TOK)[None, None, :, None]
    earlier = jnp.where(live_mask, prior_kv[0], jnp.zeros_like(prior_kv[0]))
    earlier_rows = earlier.reshape(layer_count - 1, rows_here, block_len, kv_width)
    received_early = lax.all_to_all(
        route_blocks(dispatch[: layer_count - 1], earlier_rows), "seq", 0, 0, tiled=True
    )
    widened = tokens.astype(jnp.float32)
    normed = (
        widened
        * lax.rsqrt(jnp.mean(widened * widened, axis=-1, keepdims=True) + EPSILON)
        * norm_gain
    ).astype(jnp.bfloat16)
    portion = lax.all_gather(normed, "dec", axis=0, tiled=True)
    received_early, portion = lax.optimization_barrier((received_early, portion))
    flattened = portion.reshape(-1, portion.shape[-1])
    combined = jnp.concatenate(
        [
            jnp.dot(flattened, w_query, preferred_element_type=jnp.float32),
            jnp.dot(flattened, w_keyval, preferred_element_type=jnp.float32),
        ],
        axis=-1,
    )
    positions = (jnp.arange(NEW_TOK, dtype=jnp.int32) + req_length).astype(jnp.float32)
    inverse_freq = ROPE_BASE ** (-(jnp.arange(0, HD, 2, dtype=jnp.float32) / HD))
    angles = positions[:, None, None] * inverse_freq
    queries = rotate(
        combined[:, :query_cols].reshape(NEW_TOK, query_cols // HD, HD), angles
    ).astype(jnp.bfloat16)
    key_value = combined[:, query_cols:].reshape(NEW_TOK, heads_here, kv_width)
    key_value = jnp.concatenate(
        [rotate(key_value[..., :HD], angles), key_value[..., HD:]], axis=-1
    ).astype(jnp.bfloat16)
    cached = kv_cache[0]
    padded = jnp.pad(cached, ((0, 0), (0, span_len - cached.shape[1]), (0, 0)))
    kept_cache = jnp.where((slot_ids < req_length)[None, :, None], padded, jnp.zeros_like(padded))
    fresh_rows = jnp.transpose(key_value, (1, 0, 2))
    assembled = lax.dynamic_update_slice(
        kept_cache, fresh_rows, (zero_index, req_length, zero_index)
    )
    group_size = query_cols // HD // heads_here
    grouped = jnp.transpose(
        queries.reshape(NEW_TOK, heads_here, group_size, HD), (1, 2, 0, 3)
    )
    attended = attend(
        req_length.reshape(1), grouped, assembled[:, :, :HD], assembled[:, :, HD:]
    )
    context = jnp.transpose(attended, (2, 0, 1, 3)).reshape(NEW_TOK, query_cols)
    product = jnp.dot(context, w_out, preferred_element_type=jnp.float32)
    summed = lax.psum_scatter(
        product.reshape(
            NEW_TOK // lax.axis_size("dec") * lax.axis_size("dec"), 1, product.shape[-1]
        ).astype(jnp.bfloat16),
        "dec",
        scatter_dimension=0,
        tiled=True,
    )
    current_rows = assembled.reshape(1, rows_here, block_len, kv_width)
    received_last = lax.all_to_all(
        route_blocks(dispatch[layer_count - 1 :], current_rows), "seq", 0, 0, tiled=True
    )
    received = jnp.concatenate(
        [
            received_early.reshape(owner_count, layer_count - 1, capacity, block_len, kv_width),
            received_last.reshape(owner_count, 1, capacity, block_len, kv_width),
        ],
        axis=1,
    )
    decode_pool = jnp.transpose(received, (1, 0, 2, 3, 4)).reshape(
        1, 1, layer_count, owner_count, capacity, block_len, kv_width
    )
    return (summed, decode_pool)


def solution(mesh):
    in_specs = (
        P("dec", "seq", None),
        P(),
        P(),
        P(None, "dec"),
        P(None, "dec"),
        P("dec", None),
        P("seq", "dec", None, None),
        P("seq", None, "dec", None, None),
        P("seq", None, "dec", None, None),
    )
    out_specs = (P("dec", "seq", None), P("seq", "dec", None, None, None, None, None))
    return jax.shard_map(local, mesh=mesh, in_specs=in_specs, out_specs=out_specs, check_vma=False)
```

```python
import functools

import jax
import jax.numpy as jnp
from jax import lax
from jax.experimental import pallas as pl
from jax.experimental.pallas import tpu as pltpu
from jax.sharding import PartitionSpec as P

HD = 64
NEW_TOK = 512


EPSILON = 1e-06
ROPE_BASE = 10000.0


def rotate(values, angles):
    half_dim = values.shape[-1] // 2
    first_half = values[..., :half_dim]
    second_half = values[..., half_dim:]
    cosine = jnp.cos(angles)
    sine_part = jnp.sin(angles)
    return jnp.concatenate(
        [
            first_half * cosine - second_half * sine_part,
            second_half * cosine + first_half * sine_part,
        ],
        axis=-1,
    )


def route_blocks(dispatch_table, block_data):
    layers = dispatch_table.shape[0]
    same_layer = jnp.eye(layers, dtype=dispatch_table.dtype)
    spread = dispatch_table[:, :, :, None, :] * same_layer[:, None, None, :, None]
    moved_blocks = jnp.einsum(
        "locms,msbw->olcbw", spread, block_data, preferred_element_type=jnp.float32
    ).astype(jnp.bfloat16)
    shape = moved_blocks.shape
    return moved_blocks.reshape(shape[0], shape[1] * shape[2] * shape[3], shape[4])


def attention_kernel(length_ref, q_ref, k_ref, v_ref, out_ref, *, tile, scale):
    tile_index = pl.program_id(1)
    span = k_ref.shape[1]
    keys = k_ref[0]
    values = v_ref[0]
    token = lax.broadcasted_iota(jnp.int32, (tile, span), 0) + tile_index * tile
    slot = lax.broadcasted_iota(jnp.int32, (tile, span), 1)
    visible = slot <= length_ref[0] + token
    for group_index in range(q_ref.shape[1]):
        scores = (
            lax.dot_general(
                q_ref[0, group_index],
                keys,
                (((1,), (1,)), ((), ())),
                preferred_element_type=jnp.float32,
            )
            * scale
        )
        row_max = jnp.max(jnp.where(visible, scores, -jnp.inf), axis=-1, keepdims=True)
        weights = jnp.where(visible, jnp.exp(scores - row_max), 0.0)
        row_total = jnp.sum(weights, axis=-1, keepdims=True)
        mixed = jnp.dot(
            weights.astype(jnp.bfloat16), values, preferred_element_type=jnp.float32
        )
        out_ref[0, group_index] = (mixed / row_total).astype(out_ref.dtype)


def attend(length, queries, keys, values, tile=128):
    heads, group, tokens, width = queries.shape
    span = keys.shape[1]
    kernel = functools.partial(attention_kernel, tile=tile, scale=HD ** (-0.5))
    flops = 4 * heads * group * tokens * span * width
    return pl.pallas_call(
        kernel,
        out_shape=jax.ShapeDtypeStruct(queries.shape, jnp.bfloat16),
        grid_spec=pltpu.PrefetchScalarGridSpec(
            num_scalar_prefetch=1,
            grid=(heads, tokens // tile),
            in_specs=[
                pl.BlockSpec((1, group, tile, width), lambda h, i, n: (h, 0, i, 0)),
                pl.BlockSpec((1, span, width), lambda h, i, n: (h, 0, 0)),
                pl.BlockSpec((1, span, width), lambda h, i, n: (h, 0, 0)),
            ],
            out_specs=pl.BlockSpec((1, group, tile, width), lambda h, i, n: (h, 0, i, 0)),
        ),
        cost_estimate=pl.CostEstimate(
            flops=flops,
            transcendentals=heads * group * tokens * span,
            bytes_accessed=2 * (2 * queries.size + keys.size + values.size),
        ),
    )(length, queries, keys, values)


def line_all_gather(chunk, axis):
    count = lax.axis_size(axis)
    here = lax.axis_index(axis)
    upward = [(i, i + 1) for i in range(count - 1)]
    downward = [(i + 1, i) for i in range(count - 1)]
    from_below, from_above = [], []
    carry_up = chunk
    carry_down = chunk
    for step in range(1, count):
        carry_up = lax.ppermute(carry_up, axis, upward)
        carry_down = lax.ppermute(carry_down, axis, downward)
        from_below.append(carry_up)
        from_above.append(carry_down)
    below = jnp.stack(from_below)
    above = jnp.stack(from_above)
    pieces = []
    for index in range(count):
        gap = here - index
        near = jnp.where(
            gap > 0,
            lax.dynamic_index_in_dim(below, jnp.clip(gap - 1, 0, count - 2), keepdims=False),
            lax.dynamic_index_in_dim(above, jnp.clip(-gap - 1, 0, count - 2), keepdims=False),
        )
        pieces.append(jnp.where(gap == 0, chunk, near))
    return jnp.concatenate(pieces, axis=0)


def line_reduce_scatter(parts, axis):
    count = lax.axis_size(axis)
    here = lax.axis_index(axis)
    upward = [(i, i + 1) for i in range(count - 1)]
    downward = [(i + 1, i) for i in range(count - 1)]
    chunk = parts.shape[0] // count

    def part_of(index):
        index = jnp.clip(index, 0, count - 1)
        return lax.dynamic_slice_in_dim(parts, index * chunk, chunk, axis=0)

    got_up = jnp.zeros((chunk,) + parts.shape[1:], jnp.float32)
    got_down = jnp.zeros((chunk,) + parts.shape[1:], jnp.float32)
    for step in range(1, count):
        send_up = (part_of(here + count - step) + got_up).astype(jnp.bfloat16)
        send_down = (part_of(here - count + step) + got_down).astype(jnp.bfloat16)
        got_up = lax.ppermute(send_up, axis, upward).astype(jnp.float32)
        got_down = lax.ppermute(send_down, axis, downward).astype(jnp.float32)
    return (part_of(here) + got_up + got_down).astype(jnp.bfloat16)


def local(tokens, norm_gain, lengths, w_query, w_keyval, w_out, kv_cache, prior_kv, owners):
    query_cols = w_query.shape[1]
    heads_here = kv_cache.shape[1]
    layer_count = owners.shape[1]
    block_count = owners.shape[3]
    span_len = prior_kv.shape[3]
    block_len = span_len // block_count
    kv_width = 2 * HD
    rows_here = heads_here * block_count
    owner_count = lax.axis_size("seq")
    capacity = (rows_here + owner_count - 1) // owner_count
    req_length = lengths[lax.axis_index("seq")]
    slot_ids = jnp.arange(span_len, dtype=jnp.int32)
    zero_index = jnp.zeros((), jnp.int32)
    owner_rows = owners[0, :, :, :, 0].reshape(layer_count, rows_here)
    owner_hits = (owner_rows[:, :, None] == jnp.arange(owner_count, dtype=jnp.int32)).astype(
        jnp.int32
    )
    owner_rank = jnp.sum((jnp.cumsum(owner_hits, axis=1) - owner_hits) * owner_hits, axis=-1)
    slot_index = owner_rows * capacity + owner_rank
    dispatch = (
        slot_index[:, None, :] == jnp.arange(owner_count * capacity, dtype=jnp.int32)[None, :, None]
    ).astype(jnp.bfloat16)
    dispatch = dispatch.reshape(layer_count, owner_count, capacity, rows_here)
    live_mask = (slot_ids < req_length + NEW_TOK)[None, None, :, None]
    earlier = jnp.where(live_mask, prior_kv[0], jnp.zeros_like(prior_kv[0]))
    earlier_rows = earlier.reshape(layer_count - 1, rows_here, block_len, kv_width)
    received_early = lax.all_to_all(
        route_blocks(dispatch[: layer_count - 1], earlier_rows), "seq", 0, 0, tiled=True
    )
    widened = tokens.astype(jnp.float32)
    normed = (
        widened
        * lax.rsqrt(jnp.mean(widened * widened, axis=-1, keepdims=True) + EPSILON)
        * norm_gain
    ).astype(jnp.bfloat16)
    portion = line_all_gather(normed, "dec")
    received_early, portion = lax.optimization_barrier((received_early, portion))
    flattened = portion.reshape(-1, portion.shape[-1])
    combined = jnp.concatenate(
        [
            jnp.dot(flattened, w_query, preferred_element_type=jnp.float32),
            jnp.dot(flattened, w_keyval, preferred_element_type=jnp.float32),
        ],
        axis=-1,
    )
    positions = (jnp.arange(NEW_TOK, dtype=jnp.int32) + req_length).astype(jnp.float32)
    inverse_freq = ROPE_BASE ** (-(jnp.arange(0, HD, 2, dtype=jnp.float32) / HD))
    angles = positions[:, None, None] * inverse_freq
    queries = rotate(
        combined[:, :query_cols].reshape(NEW_TOK, query_cols // HD, HD), angles
    ).astype(jnp.bfloat16)
    key_value = combined[:, query_cols:].reshape(NEW_TOK, heads_here, kv_width)
    key_value = jnp.concatenate(
        [rotate(key_value[..., :HD], angles), key_value[..., HD:]], axis=-1
    ).astype(jnp.bfloat16)
    cached = kv_cache[0]
    padded = jnp.pad(cached, ((0, 0), (0, span_len - cached.shape[1]), (0, 0)))
    kept_cache = jnp.where((slot_ids < req_length)[None, :, None], padded, jnp.zeros_like(padded))
    fresh_rows = jnp.transpose(key_value, (1, 0, 2))
    assembled = lax.dynamic_update_slice(
        kept_cache, fresh_rows, (zero_index, req_length, zero_index)
    )
    group_size = query_cols // HD // heads_here
    grouped = jnp.transpose(
        queries.reshape(NEW_TOK, heads_here, group_size, HD), (1, 2, 0, 3)
    )
    attended = attend(
        req_length.reshape(1), grouped, assembled[:, :, :HD], assembled[:, :, HD:]
    )
    context = jnp.transpose(attended, (2, 0, 1, 3)).reshape(NEW_TOK, query_cols)
    product = jnp.dot(context, w_out, preferred_element_type=jnp.float32)
    summed = line_reduce_scatter(product.reshape(NEW_TOK, 1, product.shape[-1]), "dec")
    current_rows = assembled.reshape(1, rows_here, block_len, kv_width)
    received_last = lax.all_to_all(
        route_blocks(dispatch[layer_count - 1 :], current_rows), "seq", 0, 0, tiled=True
    )
    received = jnp.concatenate(
        [
            received_early.reshape(owner_count, layer_count - 1, capacity, block_len, kv_width),
            received_last.reshape(owner_count, 1, capacity, block_len, kv_width),
        ],
        axis=1,
    )
    decode_pool = jnp.transpose(received, (1, 0, 2, 3, 4)).reshape(
        1, 1, layer_count, owner_count, capacity, block_len, kv_width
    )
    return (summed, decode_pool)


def solution(mesh):
    in_specs = (
        P("dec", "seq", None),
        P(),
        P(),
        P(None, "dec"),
        P(None, "dec"),
        P("dec", None),
        P("seq", "dec", None, None),
        P("seq", None, "dec", None, None),
        P("seq", None, "dec", None, None),
    )
    out_specs = (P("dec", "seq", None), P("seq", "dec", None, None, None, None, None))
    return jax.shard_map(local, mesh=mesh, in_specs=in_specs, out_specs=out_specs, check_vma=False)
```

```python
import functools

import jax
import jax.numpy as jnp
from jax import lax
from jax.experimental import pallas as pl
from jax.experimental.pallas import tpu as pltpu
from jax.sharding import PartitionSpec as P

HD = 64
NEW_TOK = 512


EPSILON = 1e-06
ROPE_BASE = 10000.0


def rotate(values, angles):
    half_dim = values.shape[-1] // 2
    first_half = values[..., :half_dim]
    second_half = values[..., half_dim:]
    cosine = jnp.cos(angles)
    sine_part = jnp.sin(angles)
    return jnp.concatenate(
        [
            first_half * cosine - second_half * sine_part,
            second_half * cosine + first_half * sine_part,
        ],
        axis=-1,
    )


def route_blocks(dispatch_table, block_data):
    layers = dispatch_table.shape[0]
    same_layer = jnp.eye(layers, dtype=dispatch_table.dtype)
    spread = dispatch_table[:, :, :, None, :] * same_layer[:, None, None, :, None]
    moved_blocks = jnp.einsum(
        "locms,msbw->olcbw", spread, block_data, preferred_element_type=jnp.float32
    ).astype(jnp.bfloat16)
    shape = moved_blocks.shape
    return moved_blocks.reshape(shape[0], shape[1] * shape[2] * shape[3], shape[4])


def attention_kernel(length_ref, q_ref, k_ref, v_ref, out_ref, score_ref, weight_ref, total_ref, *, tile, scale, rows_per_pass):
    tile_index = pl.program_id(1)
    group, span = q_ref.shape[1], k_ref.shape[2]
    queries = q_ref[0].reshape(group * tile, q_ref.shape[3])
    score_ref[...] = jnp.dot(queries, k_ref[0], preferred_element_type=jnp.float32)
    slot = lax.broadcasted_iota(jnp.int32, (rows_per_pass, span), 1)
    row = lax.broadcasted_iota(jnp.int32, (rows_per_pass, span), 0)
    for first in range(0, group * tile, rows_per_pass):
        limit = length_ref[0] + tile_index * tile + (first % tile)
        visible = slot <= row + limit
        scores = score_ref[first : first + rows_per_pass, :] * scale
        row_max = jnp.max(jnp.where(visible, scores, -jnp.inf), axis=-1, keepdims=True)
        weights = jnp.where(visible, jnp.exp(scores - row_max), 0.0)
        total_ref[first : first + rows_per_pass, :] = jnp.sum(weights, axis=-1, keepdims=True)
        weight_ref[first : first + rows_per_pass, :] = weights.astype(jnp.bfloat16)
    mixed = jnp.dot(weight_ref[...], v_ref[0], preferred_element_type=jnp.float32)
    out_ref[0] = (mixed / total_ref[...]).astype(out_ref.dtype).reshape(out_ref.shape[1:])


def attend(length, queries, keys_t, values, tile=128, rows_per_pass=16):
    heads, group, tokens, width = queries.shape
    span = keys_t.shape[2]
    kernel = functools.partial(
        attention_kernel, tile=tile, scale=HD ** (-0.5), rows_per_pass=rows_per_pass
    )
    flops = 4 * heads * group * tokens * span * width
    return pl.pallas_call(
        kernel,
        out_shape=jax.ShapeDtypeStruct(queries.shape, jnp.bfloat16),
        grid_spec=pltpu.PrefetchScalarGridSpec(
            num_scalar_prefetch=1,
            grid=(heads, tokens // tile),
            in_specs=[
                pl.BlockSpec((1, group, tile, width), lambda h, i, n: (h, 0, i, 0)),
                pl.BlockSpec((1, width, span), lambda h, i, n: (h, 0, 0)),
                pl.BlockSpec((1, span, width), lambda h, i, n: (h, 0, 0)),
            ],
            out_specs=pl.BlockSpec((1, group, tile, width), lambda h, i, n: (h, 0, i, 0)),
            scratch_shapes=[
                pltpu.VMEM((group * tile, span), jnp.float32),
                pltpu.VMEM((group * tile, span), jnp.bfloat16),
                pltpu.VMEM((group * tile, 1), jnp.float32),
            ],
        ),
        cost_estimate=pl.CostEstimate(
            flops=flops,
            transcendentals=heads * group * tokens * span,
            bytes_accessed=2 * (2 * queries.size + keys_t.size + values.size),
        ),
    )(length, queries, keys_t, values)


def local(tokens, norm_gain, lengths, w_query, w_keyval, w_out, kv_cache, prior_kv, owners):
    query_cols = w_query.shape[1]
    heads_here = kv_cache.shape[1]
    layer_count = owners.shape[1]
    block_count = owners.shape[3]
    span_len = prior_kv.shape[3]
    block_len = span_len // block_count
    kv_width = 2 * HD
    rows_here = heads_here * block_count
    owner_count = lax.axis_size("seq")
    capacity = (rows_here + owner_count - 1) // owner_count
    req_length = lengths[lax.axis_index("seq")]
    slot_ids = jnp.arange(span_len, dtype=jnp.int32)
    zero_index = jnp.zeros((), jnp.int32)
    owner_rows = owners[0, :, :, :, 0].reshape(layer_count, rows_here)
    owner_hits = (owner_rows[:, :, None] == jnp.arange(owner_count, dtype=jnp.int32)).astype(
        jnp.int32
    )
    owner_rank = jnp.sum((jnp.cumsum(owner_hits, axis=1) - owner_hits) * owner_hits, axis=-1)
    slot_index = owner_rows * capacity + owner_rank
    dispatch = (
        slot_index[:, None, :] == jnp.arange(owner_count * capacity, dtype=jnp.int32)[None, :, None]
    ).astype(jnp.bfloat16)
    dispatch = dispatch.reshape(layer_count, owner_count, capacity, rows_here)
    live_mask = (slot_ids < req_length + NEW_TOK)[None, None, :, None]
    earlier = jnp.where(live_mask, prior_kv[0], jnp.zeros_like(prior_kv[0]))
    earlier_rows = earlier.reshape(layer_count - 1, rows_here, block_len, kv_width)
    received_early = lax.all_to_all(
        route_blocks(dispatch[: layer_count - 1], earlier_rows), "seq", 0, 0, tiled=True
    )
    widened = tokens.astype(jnp.float32)
    normed = (
        widened
        * lax.rsqrt(jnp.mean(widened * widened, axis=-1, keepdims=True) + EPSILON)
        * norm_gain
    ).astype(jnp.bfloat16)
    portion = lax.all_gather(normed, "dec", axis=0, tiled=True)
    received_early, portion = lax.optimization_barrier((received_early, portion))
    flattened = portion.reshape(-1, portion.shape[-1])
    combined = jnp.concatenate(
        [
            jnp.dot(flattened, w_query, preferred_element_type=jnp.float32),
            jnp.dot(flattened, w_keyval, preferred_element_type=jnp.float32),
        ],
        axis=-1,
    )
    positions = (jnp.arange(NEW_TOK, dtype=jnp.int32) + req_length).astype(jnp.float32)
    inverse_freq = ROPE_BASE ** (-(jnp.arange(0, HD, 2, dtype=jnp.float32) / HD))
    angles = positions[:, None, None] * inverse_freq
    queries = rotate(
        combined[:, :query_cols].reshape(NEW_TOK, query_cols // HD, HD), angles
    ).astype(jnp.bfloat16)
    key_value = combined[:, query_cols:].reshape(NEW_TOK, heads_here, kv_width)
    key_value = jnp.concatenate(
        [rotate(key_value[..., :HD], angles), key_value[..., HD:]], axis=-1
    ).astype(jnp.bfloat16)
    cached = kv_cache[0]
    padded = jnp.pad(cached, ((0, 0), (0, span_len - cached.shape[1]), (0, 0)))
    kept_cache = jnp.where((slot_ids < req_length)[None, :, None], padded, jnp.zeros_like(padded))
    fresh_rows = jnp.transpose(key_value, (1, 0, 2))
    assembled = lax.dynamic_update_slice(
        kept_cache, fresh_rows, (zero_index, req_length, zero_index)
    )
    group_size = query_cols // HD // heads_here
    grouped = jnp.transpose(
        queries.reshape(NEW_TOK, heads_here, group_size, HD), (1, 2, 0, 3)
    )
    attended = attend(
        req_length.reshape(1),
        grouped,
        jnp.transpose(assembled[:, :, :HD], (0, 2, 1)),
        assembled[:, :, HD:],
    )
    context = jnp.transpose(attended, (2, 0, 1, 3)).reshape(NEW_TOK, query_cols)
    product = jnp.dot(context, w_out, preferred_element_type=jnp.float32)
    summed = lax.psum_scatter(
        product.reshape(
            NEW_TOK // lax.axis_size("dec") * lax.axis_size("dec"), 1, product.shape[-1]
        ).astype(jnp.bfloat16),
        "dec",
        scatter_dimension=0,
        tiled=True,
    )
    current_rows = assembled.reshape(1, rows_here, block_len, kv_width)
    received_last = lax.all_to_all(
        route_blocks(dispatch[layer_count - 1 :], current_rows), "seq", 0, 0, tiled=True
    )
    received = jnp.concatenate(
        [
            received_early.reshape(owner_count, layer_count - 1, capacity, block_len, kv_width),
            received_last.reshape(owner_count, 1, capacity, block_len, kv_width),
        ],
        axis=1,
    )
    decode_pool = jnp.transpose(received, (1, 0, 2, 3, 4)).reshape(
        1, 1, layer_count, owner_count, capacity, block_len, kv_width
    )
    return (summed, decode_pool)


def solution(mesh):
    in_specs = (
        P("dec", "seq", None),
        P(),
        P(),
        P(None, "dec"),
        P(None, "dec"),
        P("dec", None),
        P("seq", "dec", None, None),
        P("seq", None, "dec", None, None),
        P("seq", None, "dec", None, None),
    )
    out_specs = (P("dec", "seq", None), P("seq", "dec", None, None, None, None, None))
    return jax.shard_map(local, mesh=mesh, in_specs=in_specs, out_specs=out_specs, check_vma=False)
```

```python
import functools

import jax
import jax.numpy as jnp
from jax import lax
from jax.experimental import pallas as pl
from jax.experimental.pallas import tpu as pltpu
from jax.sharding import PartitionSpec as P

HD = 64
NEW_TOK = 512


EPSILON = 1e-06
ROPE_BASE = 10000.0


def rotate(values, angles):
    half_dim = values.shape[-1] // 2
    first_half = values[..., :half_dim]
    second_half = values[..., half_dim:]
    cosine = jnp.cos(angles)
    sine_part = jnp.sin(angles)
    return jnp.concatenate(
        [
            first_half * cosine - second_half * sine_part,
            second_half * cosine + first_half * sine_part,
        ],
        axis=-1,
    )


def route_blocks(dispatch_table, block_data):
    layers = dispatch_table.shape[0]
    same_layer = jnp.eye(layers, dtype=dispatch_table.dtype)
    spread = dispatch_table[:, :, :, None, :] * same_layer[:, None, None, :, None]
    moved_blocks = jnp.einsum(
        "locms,msbw->olcbw", spread, block_data, preferred_element_type=jnp.float32
    ).astype(jnp.bfloat16)
    shape = moved_blocks.shape
    return moved_blocks.reshape(shape[0], shape[1] * shape[2] * shape[3], shape[4])


def attention_kernel(length_ref, q_ref, k_ref, v_ref, out_ref, *, tile, scale):
    tile_index = pl.program_id(1)
    span = k_ref.shape[2]
    keys = k_ref[0]
    values = v_ref[0]
    token = lax.broadcasted_iota(jnp.int32, (tile, span), 0) + tile_index * tile
    slot = lax.broadcasted_iota(jnp.int32, (tile, span), 1)
    visible = slot <= length_ref[0] + token
    for group_index in range(q_ref.shape[1]):
        scores = (
            jnp.dot(q_ref[0, group_index], keys, preferred_element_type=jnp.float32)
            * scale
        )
        row_max = jnp.max(jnp.where(visible, scores, -jnp.inf), axis=-1, keepdims=True)
        weights = jnp.where(visible, jnp.exp(scores - row_max), 0.0)
        row_total = jnp.sum(weights, axis=-1, keepdims=True)
        mixed = jnp.dot(
            weights.astype(jnp.bfloat16), values, preferred_element_type=jnp.float32
        )
        out_ref[0, group_index] = (mixed / row_total).astype(out_ref.dtype)


def attend(length, queries, keys_t, values, tile=256):
    heads, group, tokens, width = queries.shape
    span = keys_t.shape[2]
    kernel = functools.partial(attention_kernel, tile=tile, scale=HD ** (-0.5))
    flops = 4 * heads * group * tokens * span * width
    return pl.pallas_call(
        kernel,
        out_shape=jax.ShapeDtypeStruct(queries.shape, jnp.bfloat16),
        grid_spec=pltpu.PrefetchScalarGridSpec(
            num_scalar_prefetch=1,
            grid=(heads, tokens // tile),
            in_specs=[
                pl.BlockSpec((1, group, tile, width), lambda h, i, n: (h, 0, i, 0)),
                pl.BlockSpec((1, width, span), lambda h, i, n: (h, 0, 0)),
                pl.BlockSpec((1, span, width), lambda h, i, n: (h, 0, 0)),
            ],
            out_specs=pl.BlockSpec((1, group, tile, width), lambda h, i, n: (h, 0, i, 0)),
        ),
        cost_estimate=pl.CostEstimate(
            flops=flops,
            transcendentals=heads * group * tokens * span,
            bytes_accessed=2 * (2 * queries.size + keys_t.size + values.size),
        ),
    )(length, queries, keys_t, values)


def local(tokens, norm_gain, lengths, w_query, w_keyval, w_out, kv_cache, prior_kv, owners):
    query_cols = w_query.shape[1]
    heads_here = kv_cache.shape[1]
    layer_count = owners.shape[1]
    block_count = owners.shape[3]
    span_len = prior_kv.shape[3]
    block_len = span_len // block_count
    kv_width = 2 * HD
    rows_here = heads_here * block_count
    owner_count = lax.axis_size("seq")
    capacity = (rows_here + owner_count - 1) // owner_count
    req_length = lengths[lax.axis_index("seq")]
    slot_ids = jnp.arange(span_len, dtype=jnp.int32)
    zero_index = jnp.zeros((), jnp.int32)
    owner_rows = owners[0, :, :, :, 0].reshape(layer_count, rows_here)
    owner_hits = (owner_rows[:, :, None] == jnp.arange(owner_count, dtype=jnp.int32)).astype(
        jnp.int32
    )
    owner_rank = jnp.sum((jnp.cumsum(owner_hits, axis=1) - owner_hits) * owner_hits, axis=-1)
    slot_index = owner_rows * capacity + owner_rank
    dispatch = (
        slot_index[:, None, :] == jnp.arange(owner_count * capacity, dtype=jnp.int32)[None, :, None]
    ).astype(jnp.bfloat16)
    dispatch = dispatch.reshape(layer_count, owner_count, capacity, rows_here)
    live_mask = (slot_ids < req_length + NEW_TOK)[None, None, :, None]
    earlier = jnp.where(live_mask, prior_kv[0], jnp.zeros_like(prior_kv[0]))
    earlier_rows = earlier.reshape(layer_count - 1, rows_here, block_len, kv_width)
    received_early = lax.all_to_all(
        route_blocks(dispatch[: layer_count - 1], earlier_rows), "seq", 0, 0, tiled=True
    )
    widened = tokens.astype(jnp.float32)
    normed = (
        widened
        * lax.rsqrt(jnp.mean(widened * widened, axis=-1, keepdims=True) + EPSILON)
        * norm_gain
    ).astype(jnp.bfloat16)
    portion = lax.all_gather(normed, "dec", axis=0, tiled=True)
    received_early, portion = lax.optimization_barrier((received_early, portion))
    flattened = portion.reshape(-1, portion.shape[-1])
    combined = jnp.concatenate(
        [
            jnp.dot(flattened, w_query, preferred_element_type=jnp.float32),
            jnp.dot(flattened, w_keyval, preferred_element_type=jnp.float32),
        ],
        axis=-1,
    )
    positions = (jnp.arange(NEW_TOK, dtype=jnp.int32) + req_length).astype(jnp.float32)
    inverse_freq = ROPE_BASE ** (-(jnp.arange(0, HD, 2, dtype=jnp.float32) / HD))
    angles = positions[:, None, None] * inverse_freq
    queries = rotate(
        combined[:, :query_cols].reshape(NEW_TOK, query_cols // HD, HD), angles
    ).astype(jnp.bfloat16)
    key_value = combined[:, query_cols:].reshape(NEW_TOK, heads_here, kv_width)
    key_value = jnp.concatenate(
        [rotate(key_value[..., :HD], angles), key_value[..., HD:]], axis=-1
    ).astype(jnp.bfloat16)
    cached = kv_cache[0]
    padded = jnp.pad(cached, ((0, 0), (0, span_len - cached.shape[1]), (0, 0)))
    kept_cache = jnp.where((slot_ids < req_length)[None, :, None], padded, jnp.zeros_like(padded))
    fresh_rows = jnp.transpose(key_value, (1, 0, 2))
    assembled = lax.dynamic_update_slice(
        kept_cache, fresh_rows, (zero_index, req_length, zero_index)
    )
    group_size = query_cols // HD // heads_here
    grouped = jnp.transpose(
        queries.reshape(NEW_TOK, heads_here, group_size, HD), (1, 2, 0, 3)
    )
    attended = attend(
        req_length.reshape(1),
        grouped,
        jnp.transpose(assembled[:, :, :HD], (0, 2, 1)),
        assembled[:, :, HD:],
    )
    context = jnp.transpose(attended, (2, 0, 1, 3)).reshape(NEW_TOK, query_cols)
    product = jnp.dot(context, w_out, preferred_element_type=jnp.float32)
    summed = lax.psum_scatter(
        product.reshape(
            NEW_TOK // lax.axis_size("dec") * lax.axis_size("dec"), 1, product.shape[-1]
        ).astype(jnp.bfloat16),
        "dec",
        scatter_dimension=0,
        tiled=True,
    )
    current_rows = assembled.reshape(1, rows_here, block_len, kv_width)
    received_last = lax.all_to_all(
        route_blocks(dispatch[layer_count - 1 :], current_rows), "seq", 0, 0, tiled=True
    )
    received = jnp.concatenate(
        [
            received_early.reshape(owner_count, layer_count - 1, capacity, block_len, kv_width),
            received_last.reshape(owner_count, 1, capacity, block_len, kv_width),
        ],
        axis=1,
    )
    decode_pool = jnp.transpose(received, (1, 0, 2, 3, 4)).reshape(
        1, 1, layer_count, owner_count, capacity, block_len, kv_width
    )
    return (summed, decode_pool)


def solution(mesh):
    in_specs = (
        P("dec", "seq", None),
        P(),
        P(),
        P(None, "dec"),
        P(None, "dec"),
        P("dec", None),
        P("seq", "dec", None, None),
        P("seq", None, "dec", None, None),
        P("seq", None, "dec", None, None),
    )
    out_specs = (P("dec", "seq", None), P("seq", "dec", None, None, None, None, None))
    return jax.shard_map(local, mesh=mesh, in_specs=in_specs, out_specs=out_specs, check_vma=False)
```

```python
import functools

import jax
import jax.numpy as jnp
from jax import lax
from jax.experimental import pallas as pl
from jax.experimental.pallas import tpu as pltpu
from jax.sharding import PartitionSpec as P

HD = 64
NEW_TOK = 512


EPSILON = 1e-06
ROPE_BASE = 10000.0


def rotate(values, angles):
    half_dim = values.shape[-1] // 2
    first_half = values[..., :half_dim]
    second_half = values[..., half_dim:]
    cosine = jnp.cos(angles)
    sine_part = jnp.sin(angles)
    return jnp.concatenate(
        [
            first_half * cosine - second_half * sine_part,
            second_half * cosine + first_half * sine_part,
        ],
        axis=-1,
    )


def route_blocks(dispatch_table, block_data):
    layers = dispatch_table.shape[0]
    same_layer = jnp.eye(layers, dtype=dispatch_table.dtype)
    spread = dispatch_table[:, :, :, None, :] * same_layer[:, None, None, :, None]
    moved_blocks = jnp.einsum(
        "locms,msbw->olcbw", spread, block_data, preferred_element_type=jnp.float32
    ).astype(jnp.bfloat16)
    shape = moved_blocks.shape
    return moved_blocks.reshape(shape[0], shape[1] * shape[2] * shape[3], shape[4])


def swap_halves(values, half):
    lane = lax.broadcasted_iota(jnp.int32, values.shape, 1)
    width = values.shape[1]
    wanted = jnp.where((lane % (2 * half)) < half, lane + half, lane - half)
    ahead = pltpu.roll(values, half, 1)
    behind = pltpu.roll(values, width - half, 1)
    ahead_lane = pltpu.roll(lane, half, 1)
    return jnp.where(ahead_lane == wanted, ahead, behind)


def project_kernel(x_ref, wq_ref, wkv_ref, cq_ref, sq_ref, ckv_ref, skv_ref, q_out, kv_out):
    x = x_ref[...]
    query = jnp.dot(x, wq_ref[...], preferred_element_type=jnp.float32)
    q_out[...] = (query * cq_ref[...] + swap_halves(query, HD // 2) * sq_ref[...]).astype(
        q_out.dtype
    )
    key_value = jnp.dot(x, wkv_ref[...], preferred_element_type=jnp.float32)
    rotated = (
        key_value * ckv_ref[...] + swap_halves(key_value, HD // 2) * skv_ref[...]
    ).astype(kv_out.dtype)
    width = kv_out.shape[2]
    for head_index in range(kv_out.shape[0]):
        kv_out[head_index] = rotated[:, head_index * width : (head_index + 1) * width]


def project(x, w_query, w_keyval, cos_q, sin_q, cos_kv, sin_kv, tile=256):
    tokens, depth = x.shape
    q_cols, kv_cols = w_query.shape[1], w_keyval.shape[1]
    heads = kv_cols // (2 * HD)
    row_spec = lambda cols: pl.BlockSpec((tile, cols), lambda i: (i, 0))
    return pl.pallas_call(
        project_kernel,
        out_shape=(
            jax.ShapeDtypeStruct((tokens, q_cols), jnp.bfloat16),
            jax.ShapeDtypeStruct((heads, tokens, 2 * HD), jnp.bfloat16),
        ),
        grid=(tokens // tile,),
        in_specs=[
            row_spec(depth),
            pl.BlockSpec((depth, q_cols), lambda i: (0, 0)),
            pl.BlockSpec((depth, kv_cols), lambda i: (0, 0)),
            row_spec(q_cols),
            row_spec(q_cols),
            row_spec(kv_cols),
            row_spec(kv_cols),
        ],
        out_specs=(
            row_spec(q_cols),
            pl.BlockSpec((heads, tile, 2 * HD), lambda i: (0, i, 0)),
        ),
        cost_estimate=pl.CostEstimate(
            flops=2 * tokens * depth * (q_cols + kv_cols),
            transcendentals=0,
            bytes_accessed=2 * (x.size + w_query.size + w_keyval.size)
            + 8 * tokens * (q_cols + kv_cols),
        ),
    )(x, w_query, w_keyval, cos_q, sin_q, cos_kv, sin_kv)


def attention_kernel(length_ref, q_ref, kt_ref, kv_ref, out_ref, *, tile, scale, group):
    tile_index = pl.program_id(0)
    span = kt_ref.shape[2]
    pair = 2 * HD
    token = lax.broadcasted_iota(jnp.int32, (tile, span), 0) + tile_index * tile
    slot = lax.broadcasted_iota(jnp.int32, (tile, span), 1)
    visible = slot <= length_ref[0] + token
    lane = lax.broadcasted_iota(jnp.int32, (tile, pair), 1)
    for pair_index in range(q_ref.shape[1] // pair):
        both = q_ref[:, pair_index * pair : (pair_index + 1) * pair]
        halves = []
        for parity in range(2):
            head = (2 * pair_index + parity) // group
            lined = both if parity == 0 else pltpu.roll(both, HD, 1)
            scores = (
                jnp.dot(lined[:, :HD], kt_ref[head], preferred_element_type=jnp.float32) * scale
            )
            row_max = jnp.max(jnp.where(visible, scores, -jnp.inf), axis=-1, keepdims=True)
            weights = jnp.where(visible, jnp.exp(scores - row_max), 0.0)
            row_total = jnp.sum(weights, axis=-1, keepdims=True)
            mixed = jnp.dot(
                weights.astype(jnp.bfloat16), kv_ref[head], preferred_element_type=jnp.float32
            )
            halves.append((mixed, row_total))
        (even, even_total), (odd, odd_total) = halves
        joined = jnp.where(lane < HD, pltpu.roll(even, HD, 1) / even_total, odd / odd_total)
        out_ref[:, pair_index * pair : (pair_index + 1) * pair] = joined.astype(out_ref.dtype)


def attend(length, queries, keys_t, assembled, group, tile=256):
    tokens, q_cols = queries.shape
    heads, span = assembled.shape[0], assembled.shape[1]
    kernel = functools.partial(attention_kernel, tile=tile, scale=HD ** (-0.5), group=group)
    flops = 4 * tokens * q_cols * span
    return pl.pallas_call(
        kernel,
        out_shape=jax.ShapeDtypeStruct(queries.shape, jnp.bfloat16),
        grid_spec=pltpu.PrefetchScalarGridSpec(
            num_scalar_prefetch=1,
            grid=(tokens // tile,),
            in_specs=[
                pl.BlockSpec((tile, q_cols), lambda i, n: (i, 0)),
                pl.BlockSpec(keys_t.shape, lambda i, n: (0, 0, 0)),
                pl.BlockSpec(assembled.shape, lambda i, n: (0, 0, 0)),
            ],
            out_specs=pl.BlockSpec((tile, q_cols), lambda i, n: (i, 0)),
        ),
        cost_estimate=pl.CostEstimate(
            flops=flops,
            transcendentals=tokens * (q_cols // HD) * span,
            bytes_accessed=2 * (2 * queries.size + keys_t.size + assembled.size),
        ),
    )(length, queries, keys_t, assembled)


def local(tokens, norm_gain, lengths, w_query, w_keyval, w_out, kv_cache, prior_kv, owners):
    query_cols = w_query.shape[1]
    heads_here = kv_cache.shape[1]
    layer_count = owners.shape[1]
    block_count = owners.shape[3]
    span_len = prior_kv.shape[3]
    block_len = span_len // block_count
    kv_width = 2 * HD
    rows_here = heads_here * block_count
    owner_count = lax.axis_size("seq")
    capacity = (rows_here + owner_count - 1) // owner_count
    req_length = lengths[lax.axis_index("seq")]
    slot_ids = jnp.arange(span_len, dtype=jnp.int32)
    zero_index = jnp.zeros((), jnp.int32)
    owner_rows = owners[0, :, :, :, 0].reshape(layer_count, rows_here)
    owner_hits = (owner_rows[:, :, None] == jnp.arange(owner_count, dtype=jnp.int32)).astype(
        jnp.int32
    )
    owner_rank = jnp.sum((jnp.cumsum(owner_hits, axis=1) - owner_hits) * owner_hits, axis=-1)
    slot_index = owner_rows * capacity + owner_rank
    dispatch = (
        slot_index[:, None, :] == jnp.arange(owner_count * capacity, dtype=jnp.int32)[None, :, None]
    ).astype(jnp.bfloat16)
    dispatch = dispatch.reshape(layer_count, owner_count, capacity, rows_here)
    live_mask = (slot_ids < req_length + NEW_TOK)[None, None, :, None]
    earlier = jnp.where(live_mask, prior_kv[0], jnp.zeros_like(prior_kv[0]))
    earlier_rows = earlier.reshape(layer_count - 1, rows_here, block_len, kv_width)
    received_early = lax.all_to_all(
        route_blocks(dispatch[: layer_count - 1], earlier_rows), "seq", 0, 0, tiled=True
    )
    widened = tokens.astype(jnp.float32)
    normed = (
        widened
        * lax.rsqrt(jnp.mean(widened * widened, axis=-1, keepdims=True) + EPSILON)
        * norm_gain
    ).astype(jnp.bfloat16)
    portion = lax.all_gather(normed, "dec", axis=0, tiled=True)
    received_early, portion = lax.optimization_barrier((received_early, portion))
    flattened = portion.reshape(-1, portion.shape[-1])
    positions = (jnp.arange(NEW_TOK, dtype=jnp.int32) + req_length).astype(jnp.float32)
    inverse_freq = ROPE_BASE ** (-(jnp.arange(0, HD, 2, dtype=jnp.float32) / HD))
    angles = positions[:, None] * inverse_freq
    cosine, sine = jnp.cos(angles), jnp.sin(angles)
    signed_sine = jnp.concatenate([-sine, sine], axis=-1)
    head_cos = jnp.concatenate([cosine, cosine], axis=-1)
    cos_q = jnp.tile(head_cos, (1, query_cols // HD))
    sin_q = jnp.tile(signed_sine, (1, query_cols // HD))
    cos_kv = jnp.tile(jnp.concatenate([head_cos, jnp.ones_like(head_cos)], axis=-1), (1, heads_here))
    sin_kv = jnp.tile(
        jnp.concatenate([signed_sine, jnp.zeros_like(signed_sine)], axis=-1), (1, heads_here)
    )
    queries, fresh_rows = project(flattened, w_query, w_keyval, cos_q, sin_q, cos_kv, sin_kv)
    cached = kv_cache[0]
    padded = jnp.pad(cached, ((0, 0), (0, span_len - cached.shape[1]), (0, 0)))
    kept_cache = jnp.where((slot_ids < req_length)[None, :, None], padded, jnp.zeros_like(padded))
    assembled = lax.dynamic_update_slice(
        kept_cache, fresh_rows, (zero_index, req_length, zero_index)
    )
    group_size = query_cols // HD // heads_here
    context = attend(
        req_length.reshape(1),
        queries,
        jnp.transpose(assembled[:, :, :HD], (0, 2, 1)),
        assembled,
        group_size,
    )
    product = jnp.dot(context, w_out, preferred_element_type=jnp.float32)
    summed = lax.psum_scatter(
        product.reshape(
            NEW_TOK // lax.axis_size("dec") * lax.axis_size("dec"), 1, product.shape[-1]
        ).astype(jnp.bfloat16),
        "dec",
        scatter_dimension=0,
        tiled=True,
    )
    current_rows = assembled.reshape(1, rows_here, block_len, kv_width)
    received_last = lax.all_to_all(
        route_blocks(dispatch[layer_count - 1 :], current_rows), "seq", 0, 0, tiled=True
    )
    received = jnp.concatenate(
        [
            received_early.reshape(owner_count, layer_count - 1, capacity, block_len, kv_width),
            received_last.reshape(owner_count, 1, capacity, block_len, kv_width),
        ],
        axis=1,
    )
    decode_pool = jnp.transpose(received, (1, 0, 2, 3, 4)).reshape(
        1, 1, layer_count, owner_count, capacity, block_len, kv_width
    )
    return (summed, decode_pool)


def solution(mesh):
    in_specs = (
        P("dec", "seq", None),
        P(),
        P(),
        P(None, "dec"),
        P(None, "dec"),
        P("dec", None),
        P("seq", "dec", None, None),
        P("seq", None, "dec", None, None),
        P("seq", None, "dec", None, None),
    )
    out_specs = (P("dec", "seq", None), P("seq", "dec", None, None, None, None, None))
    return jax.shard_map(local, mesh=mesh, in_specs=in_specs, out_specs=out_specs, check_vma=False)
```

```python
import functools

import jax
import jax.numpy as jnp
from jax import lax
from jax.experimental import pallas as pl
from jax.experimental.pallas import tpu as pltpu
from jax.sharding import PartitionSpec as P

HD = 64
NEW_TOK = 512


EPSILON = 1e-06
ROPE_BASE = 10000.0


def rotate(values, angles):
    half_dim = values.shape[-1] // 2
    first_half = values[..., :half_dim]
    second_half = values[..., half_dim:]
    cosine = jnp.cos(angles)
    sine_part = jnp.sin(angles)
    return jnp.concatenate(
        [
            first_half * cosine - second_half * sine_part,
            second_half * cosine + first_half * sine_part,
        ],
        axis=-1,
    )


def route_blocks(dispatch_table, block_data):
    layers = dispatch_table.shape[0]
    same_layer = jnp.eye(layers, dtype=dispatch_table.dtype)
    spread = dispatch_table[:, :, :, None, :] * same_layer[:, None, None, :, None]
    moved_blocks = jnp.einsum(
        "locms,msbw->olcbw", spread, block_data, preferred_element_type=jnp.float32
    ).astype(jnp.bfloat16)
    shape = moved_blocks.shape
    return moved_blocks.reshape(shape[0], shape[1] * shape[2] * shape[3], shape[4])


def swap_halves(values, half):
    lane = lax.broadcasted_iota(jnp.int32, values.shape, 1)
    width = values.shape[1]
    wanted = jnp.where((lane % (2 * half)) < half, lane + half, lane - half)
    ahead = pltpu.roll(values, half, 1)
    behind = pltpu.roll(values, width - half, 1)
    ahead_lane = pltpu.roll(lane, half, 1)
    return jnp.where(ahead_lane == wanted, ahead, behind)


def project_kernel(x_ref, wq_ref, wkv_ref, cq_ref, sq_ref, ckv_ref, skv_ref, q_out, kv_out):
    x = x_ref[...]
    query = jnp.dot(x, wq_ref[...], preferred_element_type=jnp.float32)
    q_out[...] = (query * cq_ref[...] + swap_halves(query, HD // 2) * sq_ref[...]).astype(
        q_out.dtype
    )
    key_value = jnp.dot(x, wkv_ref[...], preferred_element_type=jnp.float32)
    rotated = (
        key_value * ckv_ref[...] + swap_halves(key_value, HD // 2) * skv_ref[...]
    ).astype(kv_out.dtype)
    width = kv_out.shape[2]
    for head_index in range(kv_out.shape[0]):
        kv_out[head_index] = rotated[:, head_index * width : (head_index + 1) * width]


def project(x, w_query, w_keyval, cos_q, sin_q, cos_kv, sin_kv, tile=256):
    tokens, depth = x.shape
    q_cols, kv_cols = w_query.shape[1], w_keyval.shape[1]
    heads = kv_cols // (2 * HD)
    row_spec = lambda cols: pl.BlockSpec((tile, cols), lambda i: (i, 0))
    return pl.pallas_call(
        project_kernel,
        out_shape=(
            jax.ShapeDtypeStruct((tokens, q_cols), jnp.bfloat16),
            jax.ShapeDtypeStruct((heads, tokens, 2 * HD), jnp.bfloat16),
        ),
        grid=(tokens // tile,),
        in_specs=[
            row_spec(depth),
            pl.BlockSpec((depth, q_cols), lambda i: (0, 0)),
            pl.BlockSpec((depth, kv_cols), lambda i: (0, 0)),
            row_spec(q_cols),
            row_spec(q_cols),
            row_spec(kv_cols),
            row_spec(kv_cols),
        ],
        out_specs=(
            row_spec(q_cols),
            pl.BlockSpec((heads, tile, 2 * HD), lambda i: (0, i, 0)),
        ),
        cost_estimate=pl.CostEstimate(
            flops=2 * tokens * depth * (q_cols + kv_cols),
            transcendentals=0,
            bytes_accessed=2 * (x.size + w_query.size + w_keyval.size)
            + 8 * tokens * (q_cols + kv_cols),
        ),
    )(x, w_query, w_keyval, cos_q, sin_q, cos_kv, sin_kv)


def attention_kernel(length_ref, q_ref, kt_ref, kv_ref, wo_ref, out_ref, ctx_ref, *, tile, scale, group):
    tile_index = pl.program_id(0)
    span = kt_ref.shape[2]
    pair = 2 * HD
    token = lax.broadcasted_iota(jnp.int32, (tile, span), 0) + tile_index * tile
    slot = lax.broadcasted_iota(jnp.int32, (tile, span), 1)
    visible = slot <= length_ref[0] + token
    lane = lax.broadcasted_iota(jnp.int32, (tile, pair), 1)
    for pair_index in range(q_ref.shape[1] // pair):
        both = q_ref[:, pair_index * pair : (pair_index + 1) * pair]
        halves = []
        for parity in range(2):
            head = (2 * pair_index + parity) // group
            lined = both if parity == 0 else pltpu.roll(both, HD, 1)
            scores = (
                jnp.dot(lined[:, :HD], kt_ref[head], preferred_element_type=jnp.float32) * scale
            )
            row_max = jnp.max(jnp.where(visible, scores, -jnp.inf), axis=-1, keepdims=True)
            weights = jnp.where(visible, jnp.exp(scores - row_max), 0.0)
            row_total = jnp.sum(weights, axis=-1, keepdims=True)
            mixed = jnp.dot(
                weights.astype(jnp.bfloat16), kv_ref[head], preferred_element_type=jnp.float32
            )
            halves.append((mixed, row_total))
        (even, even_total), (odd, odd_total) = halves
        joined = jnp.where(lane < HD, pltpu.roll(even, HD, 1) / even_total, odd / odd_total)
        ctx_ref[:, pair_index * pair : (pair_index + 1) * pair] = joined.astype(ctx_ref.dtype)
    out_ref[...] = jnp.dot(ctx_ref[...], wo_ref[...], preferred_element_type=jnp.float32).astype(
        out_ref.dtype
    )


def attend(length, queries, keys_t, assembled, w_out, group, tile=256):
    tokens, q_cols = queries.shape
    heads, span = assembled.shape[0], assembled.shape[1]
    model = w_out.shape[1]
    kernel = functools.partial(attention_kernel, tile=tile, scale=HD ** (-0.5), group=group)
    flops = 4 * tokens * q_cols * span + 2 * tokens * q_cols * model
    return pl.pallas_call(
        kernel,
        out_shape=jax.ShapeDtypeStruct((tokens, model), jnp.bfloat16),
        grid_spec=pltpu.PrefetchScalarGridSpec(
            num_scalar_prefetch=1,
            grid=(tokens // tile,),
            in_specs=[
                pl.BlockSpec((tile, q_cols), lambda i, n: (i, 0)),
                pl.BlockSpec(keys_t.shape, lambda i, n: (0, 0, 0)),
                pl.BlockSpec(assembled.shape, lambda i, n: (0, 0, 0)),
                pl.BlockSpec(w_out.shape, lambda i, n: (0, 0)),
            ],
            out_specs=pl.BlockSpec((tile, model), lambda i, n: (i, 0)),
            scratch_shapes=[pltpu.VMEM((tile, q_cols), jnp.bfloat16)],
        ),
        cost_estimate=pl.CostEstimate(
            flops=flops,
            transcendentals=tokens * (q_cols // HD) * span,
            bytes_accessed=2 * (queries.size + keys_t.size + assembled.size + w_out.size)
            + 2 * tokens * model,
        ),
    )(length, queries, keys_t, assembled, w_out)


def norm_kernel(x_ref, gain_ref, out_ref):
    widened = x_ref[...].astype(jnp.float32)
    scale = lax.rsqrt(jnp.mean(widened * widened, axis=-1, keepdims=True) + EPSILON)
    out_ref[...] = (widened * scale * gain_ref[...]).astype(out_ref.dtype)


def rms_norm(x, gain):
    return pl.pallas_call(
        norm_kernel,
        out_shape=jax.ShapeDtypeStruct(x.shape, jnp.bfloat16),
        cost_estimate=pl.CostEstimate(
            flops=4 * x.size, transcendentals=x.shape[0], bytes_accessed=4 * x.size
        ),
    )(x, gain.reshape(1, -1))


def local(tokens, norm_gain, lengths, w_query, w_keyval, w_out, kv_cache, prior_kv, owners):
    query_cols = w_query.shape[1]
    heads_here = kv_cache.shape[1]
    layer_count = owners.shape[1]
    block_count = owners.shape[3]
    span_len = prior_kv.shape[3]
    block_len = span_len // block_count
    kv_width = 2 * HD
    rows_here = heads_here * block_count
    owner_count = lax.axis_size("seq")
    capacity = (rows_here + owner_count - 1) // owner_count
    req_length = lengths[lax.axis_index("seq")]
    slot_ids = jnp.arange(span_len, dtype=jnp.int32)
    zero_index = jnp.zeros((), jnp.int32)
    owner_rows = owners[0, :, :, :, 0].reshape(layer_count, rows_here)
    owner_hits = (owner_rows[:, :, None] == jnp.arange(owner_count, dtype=jnp.int32)).astype(
        jnp.int32
    )
    owner_rank = jnp.sum((jnp.cumsum(owner_hits, axis=1) - owner_hits) * owner_hits, axis=-1)
    slot_index = owner_rows * capacity + owner_rank
    dispatch = (
        slot_index[:, None, :] == jnp.arange(owner_count * capacity, dtype=jnp.int32)[None, :, None]
    ).astype(jnp.bfloat16)
    dispatch = dispatch.reshape(layer_count, owner_count, capacity, rows_here)
    live_mask = (slot_ids < req_length + NEW_TOK)[None, None, :, None]
    earlier = jnp.where(live_mask, prior_kv[0], jnp.zeros_like(prior_kv[0]))
    earlier_rows = earlier.reshape(layer_count - 1, rows_here, block_len, kv_width)
    received_early = lax.all_to_all(
        route_blocks(dispatch[: layer_count - 1], earlier_rows), "seq", 0, 0, tiled=True
    )
    normed = rms_norm(tokens.reshape(-1, tokens.shape[-1]), norm_gain).reshape(tokens.shape)
    portion = lax.all_gather(normed, "dec", axis=0, tiled=True)
    received_early, portion = lax.optimization_barrier((received_early, portion))
    flattened = portion.reshape(-1, portion.shape[-1])
    positions = (jnp.arange(NEW_TOK, dtype=jnp.int32) + req_length).astype(jnp.float32)
    inverse_freq = ROPE_BASE ** (-(jnp.arange(0, HD, 2, dtype=jnp.float32) / HD))
    angles = positions[:, None] * inverse_freq
    cosine, sine = jnp.cos(angles), jnp.sin(angles)
    signed_sine = jnp.concatenate([-sine, sine], axis=-1)
    head_cos = jnp.concatenate([cosine, cosine], axis=-1)
    cos_q = jnp.tile(head_cos, (1, query_cols // HD))
    sin_q = jnp.tile(signed_sine, (1, query_cols // HD))
    cos_kv = jnp.tile(jnp.concatenate([head_cos, jnp.ones_like(head_cos)], axis=-1), (1, heads_here))
    sin_kv = jnp.tile(
        jnp.concatenate([signed_sine, jnp.zeros_like(signed_sine)], axis=-1), (1, heads_here)
    )
    queries, fresh_rows = project(flattened, w_query, w_keyval, cos_q, sin_q, cos_kv, sin_kv)
    cached = kv_cache[0]
    padded = jnp.pad(cached, ((0, 0), (0, span_len - cached.shape[1]), (0, 0)))
    kept_cache = jnp.where((slot_ids < req_length)[None, :, None], padded, jnp.zeros_like(padded))
    assembled = lax.dynamic_update_slice(
        kept_cache, fresh_rows, (zero_index, req_length, zero_index)
    )
    group_size = query_cols // HD // heads_here
    product = attend(
        req_length.reshape(1),
        queries,
        jnp.transpose(assembled[:, :, :HD], (0, 2, 1)),
        assembled,
        w_out,
        group_size,
    )
    summed = lax.psum_scatter(
        product.reshape(NEW_TOK, 1, product.shape[-1]),
        "dec",
        scatter_dimension=0,
        tiled=True,
    )
    current_rows = assembled.reshape(1, rows_here, block_len, kv_width)
    received_last = lax.all_to_all(
        route_blocks(dispatch[layer_count - 1 :], current_rows), "seq", 0, 0, tiled=True
    )
    received = jnp.concatenate(
        [
            received_early.reshape(owner_count, layer_count - 1, capacity, block_len, kv_width),
            received_last.reshape(owner_count, 1, capacity, block_len, kv_width),
        ],
        axis=1,
    )
    decode_pool = jnp.transpose(received, (1, 0, 2, 3, 4)).reshape(
        1, 1, layer_count, owner_count, capacity, block_len, kv_width
    )
    return (summed, decode_pool)


def solution(mesh):
    in_specs = (
        P("dec", "seq", None),
        P(),
        P(),
        P(None, "dec"),
        P(None, "dec"),
        P("dec", None),
        P("seq", "dec", None, None),
        P("seq", None, "dec", None, None),
        P("seq", None, "dec", None, None),
    )
    out_specs = (P("dec", "seq", None), P("seq", "dec", None, None, None, None, None))
    return jax.shard_map(local, mesh=mesh, in_specs=in_specs, out_specs=out_specs, check_vma=False)
```

```python
import functools

import jax
import jax.numpy as jnp
from jax import lax
from jax.experimental import pallas as pl
from jax.experimental.pallas import tpu as pltpu
from jax.sharding import PartitionSpec as P

HD = 64
NEW_TOK = 512


EPSILON = 1e-06
ROPE_BASE = 10000.0


def rotate(values, angles):
    half_dim = values.shape[-1] // 2
    first_half = values[..., :half_dim]
    second_half = values[..., half_dim:]
    cosine = jnp.cos(angles)
    sine_part = jnp.sin(angles)
    return jnp.concatenate(
        [
            first_half * cosine - second_half * sine_part,
            second_half * cosine + first_half * sine_part,
        ],
        axis=-1,
    )


def route_blocks(dispatch_table, block_data):
    layers = dispatch_table.shape[0]
    same_layer = jnp.eye(layers, dtype=dispatch_table.dtype)
    spread = dispatch_table[:, :, :, None, :] * same_layer[:, None, None, :, None]
    moved_blocks = jnp.einsum(
        "locms,msbw->olcbw", spread, block_data, preferred_element_type=jnp.float32
    ).astype(jnp.bfloat16)
    shape = moved_blocks.shape
    return moved_blocks.reshape(shape[0], shape[1] * shape[2] * shape[3], shape[4])


def swap_halves(values, half):
    lane = lax.broadcasted_iota(jnp.int32, values.shape, 1)
    width = values.shape[1]
    wanted = jnp.where((lane % (2 * half)) < half, lane + half, lane - half)
    ahead = pltpu.roll(values, half, 1)
    behind = pltpu.roll(values, width - half, 1)
    ahead_lane = pltpu.roll(lane, half, 1)
    return jnp.where(ahead_lane == wanted, ahead, behind)


def project_kernel(x_ref, wq_ref, wkv_ref, cq_ref, sq_ref, ckv_ref, skv_ref, q_out, kv_out, kt_out):
    x = x_ref[...]
    query = jnp.dot(x, wq_ref[...], preferred_element_type=jnp.float32)
    q_out[...] = (query * cq_ref[...] + swap_halves(query, HD // 2) * sq_ref[...]).astype(
        q_out.dtype
    )
    key_value = jnp.dot(x, wkv_ref[...], preferred_element_type=jnp.float32)
    rotated = key_value * ckv_ref[...] + swap_halves(key_value, HD // 2) * skv_ref[...]
    width = kv_out.shape[2]
    for head_index in range(kv_out.shape[0]):
        block = rotated[:, head_index * width : (head_index + 1) * width].astype(kv_out.dtype)
        kv_out[head_index] = block
        kt_out[head_index] = block[:, :HD].astype(jnp.float32).T.astype(kt_out.dtype)


def project(x, w_query, w_keyval, cos_q, sin_q, cos_kv, sin_kv, tile=256):
    tokens, depth = x.shape
    q_cols, kv_cols = w_query.shape[1], w_keyval.shape[1]
    heads = kv_cols // (2 * HD)
    row_spec = lambda cols: pl.BlockSpec((tile, cols), lambda i: (i, 0))
    return pl.pallas_call(
        project_kernel,
        out_shape=(
            jax.ShapeDtypeStruct((tokens, q_cols), jnp.bfloat16),
            jax.ShapeDtypeStruct((heads, tokens, 2 * HD), jnp.bfloat16),
            jax.ShapeDtypeStruct((heads, HD, tokens), jnp.bfloat16),
        ),
        grid=(tokens // tile,),
        in_specs=[
            row_spec(depth),
            pl.BlockSpec((depth, q_cols), lambda i: (0, 0)),
            pl.BlockSpec((depth, kv_cols), lambda i: (0, 0)),
            row_spec(q_cols),
            row_spec(q_cols),
            row_spec(kv_cols),
            row_spec(kv_cols),
        ],
        out_specs=(
            row_spec(q_cols),
            pl.BlockSpec((heads, tile, 2 * HD), lambda i: (0, i, 0)),
            pl.BlockSpec((heads, HD, tile), lambda i: (0, 0, i)),
        ),
        cost_estimate=pl.CostEstimate(
            flops=2 * tokens * depth * (q_cols + kv_cols),
            transcendentals=0,
            bytes_accessed=2 * (x.size + w_query.size + w_keyval.size)
            + 8 * tokens * (q_cols + kv_cols),
        ),
    )(x, w_query, w_keyval, cos_q, sin_q, cos_kv, sin_kv)


def attention_kernel(
    length_ref, q_ref, kt_ref, kv_ref, ktf_ref, kvf_ref, wo_ref, out_ref, ctx_ref, *, tile, scale, group
):
    tile_index = pl.program_id(0)
    span, fresh = kt_ref.shape[2], ktf_ref.shape[2]
    pair = 2 * HD
    slot = lax.broadcasted_iota(jnp.int32, (tile, span), 1)
    cached_visible = slot < length_ref[0]
    token = lax.broadcasted_iota(jnp.int32, (tile, fresh), 0) + tile_index * tile
    new_slot = lax.broadcasted_iota(jnp.int32, (tile, fresh), 1)
    fresh_visible = new_slot <= token
    lane = lax.broadcasted_iota(jnp.int32, (tile, pair), 1)
    for pair_index in range(q_ref.shape[1] // pair):
        both = q_ref[:, pair_index * pair : (pair_index + 1) * pair]
        halves = []
        for parity in range(2):
            head = (2 * pair_index + parity) // group
            lined = (both if parity == 0 else pltpu.roll(both, HD, 1))[:, :HD]
            old = jnp.dot(lined, kt_ref[head], preferred_element_type=jnp.float32) * scale
            new = jnp.dot(lined, ktf_ref[head], preferred_element_type=jnp.float32) * scale
            row_max = jnp.maximum(
                jnp.max(jnp.where(cached_visible, old, -jnp.inf), axis=-1, keepdims=True),
                jnp.max(jnp.where(fresh_visible, new, -jnp.inf), axis=-1, keepdims=True),
            )
            old_w = jnp.where(cached_visible, jnp.exp(old - row_max), 0.0)
            new_w = jnp.where(fresh_visible, jnp.exp(new - row_max), 0.0)
            row_total = jnp.sum(old_w, axis=-1, keepdims=True) + jnp.sum(
                new_w, axis=-1, keepdims=True
            )
            mixed = jnp.dot(
                old_w.astype(jnp.bfloat16), kv_ref[head], preferred_element_type=jnp.float32
            ) + jnp.dot(new_w.astype(jnp.bfloat16), kvf_ref[head], preferred_element_type=jnp.float32)
            halves.append((mixed, row_total))
        (even, even_total), (odd, odd_total) = halves
        joined = jnp.where(lane < HD, pltpu.roll(even, HD, 1) / even_total, odd / odd_total)
        ctx_ref[:, pair_index * pair : (pair_index + 1) * pair] = joined.astype(ctx_ref.dtype)
    out_ref[...] = jnp.dot(ctx_ref[...], wo_ref[...], preferred_element_type=jnp.float32).astype(
        out_ref.dtype
    )


def attend(length, queries, keys_t, cache, fresh_keys_t, fresh, w_out, group, tile=256):
    tokens, q_cols = queries.shape
    span = cache.shape[1] + fresh.shape[1]
    model = w_out.shape[1]
    kernel = functools.partial(attention_kernel, tile=tile, scale=HD ** (-0.5), group=group)
    flops = 4 * tokens * q_cols * span + 2 * tokens * q_cols * model
    whole = lambda shape: pl.BlockSpec(shape, lambda i, n: (0,) * len(shape))
    return pl.pallas_call(
        kernel,
        out_shape=jax.ShapeDtypeStruct((tokens, model), jnp.bfloat16),
        grid_spec=pltpu.PrefetchScalarGridSpec(
            num_scalar_prefetch=1,
            grid=(tokens // tile,),
            in_specs=[
                pl.BlockSpec((tile, q_cols), lambda i, n: (i, 0)),
                whole(keys_t.shape),
                whole(cache.shape),
                whole(fresh_keys_t.shape),
                whole(fresh.shape),
                whole(w_out.shape),
            ],
            out_specs=pl.BlockSpec((tile, model), lambda i, n: (i, 0)),
            scratch_shapes=[pltpu.VMEM((tile, q_cols), jnp.bfloat16)],
        ),
        cost_estimate=pl.CostEstimate(
            flops=flops,
            transcendentals=tokens * (q_cols // HD) * span,
            bytes_accessed=2
            * (queries.size + keys_t.size + cache.size + fresh_keys_t.size + fresh.size + w_out.size)
            + 2 * tokens * model,
        ),
    )(length, queries, keys_t, cache, fresh_keys_t, fresh, w_out)


def norm_kernel(x_ref, gain_ref, out_ref):
    widened = x_ref[...].astype(jnp.float32)
    scale = lax.rsqrt(jnp.mean(widened * widened, axis=-1, keepdims=True) + EPSILON)
    out_ref[...] = (widened * scale * gain_ref[...]).astype(out_ref.dtype)


def rms_norm(x, gain):
    return pl.pallas_call(
        norm_kernel,
        out_shape=jax.ShapeDtypeStruct(x.shape, jnp.bfloat16),
        cost_estimate=pl.CostEstimate(
            flops=4 * x.size, transcendentals=x.shape[0], bytes_accessed=4 * x.size
        ),
    )(x, gain.reshape(1, -1))


def local(tokens, norm_gain, lengths, w_query, w_keyval, w_out, kv_cache, prior_kv, owners):
    query_cols = w_query.shape[1]
    heads_here = kv_cache.shape[1]
    layer_count = owners.shape[1]
    block_count = owners.shape[3]
    span_len = prior_kv.shape[3]
    block_len = span_len // block_count
    kv_width = 2 * HD
    rows_here = heads_here * block_count
    owner_count = lax.axis_size("seq")
    capacity = (rows_here + owner_count - 1) // owner_count
    req_length = lengths[lax.axis_index("seq")]
    slot_ids = jnp.arange(span_len, dtype=jnp.int32)
    zero_index = jnp.zeros((), jnp.int32)
    owner_rows = owners[0, :, :, :, 0].reshape(layer_count, rows_here)
    owner_hits = (owner_rows[:, :, None] == jnp.arange(owner_count, dtype=jnp.int32)).astype(
        jnp.int32
    )
    owner_rank = jnp.sum((jnp.cumsum(owner_hits, axis=1) - owner_hits) * owner_hits, axis=-1)
    slot_index = owner_rows * capacity + owner_rank
    dispatch = (
        slot_index[:, None, :] == jnp.arange(owner_count * capacity, dtype=jnp.int32)[None, :, None]
    ).astype(jnp.bfloat16)
    dispatch = dispatch.reshape(layer_count, owner_count, capacity, rows_here)
    live_mask = (slot_ids < req_length + NEW_TOK)[None, None, :, None]
    earlier = jnp.where(live_mask, prior_kv[0], jnp.zeros_like(prior_kv[0]))
    earlier_rows = earlier.reshape(layer_count - 1, rows_here, block_len, kv_width)
    received_early = lax.all_to_all(
        route_blocks(dispatch[: layer_count - 1], earlier_rows), "seq", 0, 0, tiled=True
    )
    normed = rms_norm(tokens.reshape(-1, tokens.shape[-1]), norm_gain).reshape(tokens.shape)
    portion = lax.all_gather(normed, "dec", axis=0, tiled=True)
    received_early, portion = lax.optimization_barrier((received_early, portion))
    flattened = portion.reshape(-1, portion.shape[-1])
    positions = (jnp.arange(NEW_TOK, dtype=jnp.int32) + req_length).astype(jnp.float32)
    inverse_freq = ROPE_BASE ** (-(jnp.arange(0, HD, 2, dtype=jnp.float32) / HD))
    angles = positions[:, None] * inverse_freq
    cosine, sine = jnp.cos(angles), jnp.sin(angles)
    signed_sine = jnp.concatenate([-sine, sine], axis=-1)
    head_cos = jnp.concatenate([cosine, cosine], axis=-1)
    cos_q = jnp.tile(head_cos, (1, query_cols // HD))
    sin_q = jnp.tile(signed_sine, (1, query_cols // HD))
    cos_kv = jnp.tile(jnp.concatenate([head_cos, jnp.ones_like(head_cos)], axis=-1), (1, heads_here))
    sin_kv = jnp.tile(
        jnp.concatenate([signed_sine, jnp.zeros_like(signed_sine)], axis=-1), (1, heads_here)
    )
    queries, fresh_rows, fresh_keys_t = project(
        flattened, w_query, w_keyval, cos_q, sin_q, cos_kv, sin_kv
    )
    cached = kv_cache[0]
    padded = jnp.pad(cached, ((0, 0), (0, span_len - cached.shape[1]), (0, 0)))
    kept_cache = jnp.where((slot_ids < req_length)[None, :, None], padded, jnp.zeros_like(padded))
    assembled = lax.dynamic_update_slice(
        kept_cache, fresh_rows, (zero_index, req_length, zero_index)
    )
    group_size = query_cols // HD // heads_here
    product = attend(
        req_length.reshape(1),
        queries,
        jnp.transpose(cached[:, :, :HD], (0, 2, 1)),
        cached,
        fresh_keys_t,
        fresh_rows,
        w_out,
        group_size,
    )
    summed = lax.psum_scatter(
        product.reshape(NEW_TOK, 1, product.shape[-1]),
        "dec",
        scatter_dimension=0,
        tiled=True,
    )
    current_rows = assembled.reshape(1, rows_here, block_len, kv_width)
    received_last = lax.all_to_all(
        route_blocks(dispatch[layer_count - 1 :], current_rows), "seq", 0, 0, tiled=True
    )
    received = jnp.concatenate(
        [
            received_early.reshape(owner_count, layer_count - 1, capacity, block_len, kv_width),
            received_last.reshape(owner_count, 1, capacity, block_len, kv_width),
        ],
        axis=1,
    )
    decode_pool = jnp.transpose(received, (1, 0, 2, 3, 4)).reshape(
        1, 1, layer_count, owner_count, capacity, block_len, kv_width
    )
    return (summed, decode_pool)


def solution(mesh):
    in_specs = (
        P("dec", "seq", None),
        P(),
        P(),
        P(None, "dec"),
        P(None, "dec"),
        P("dec", None),
        P("seq", "dec", None, None),
        P("seq", None, "dec", None, None),
        P("seq", None, "dec", None, None),
    )
    out_specs = (P("dec", "seq", None), P("seq", "dec", None, None, None, None, None))
    return jax.shard_map(local, mesh=mesh, in_specs=in_specs, out_specs=out_specs, check_vma=False)
```

```python
import functools

import jax
import jax.numpy as jnp
from jax import lax
from jax.experimental import pallas as pl
from jax.experimental.pallas import tpu as pltpu
from jax.sharding import PartitionSpec as P

HD = 64
NEW_TOK = 512


EPSILON = 1e-06
ROPE_BASE = 10000.0


def rotate(values, angles):
    half_dim = values.shape[-1] // 2
    first_half = values[..., :half_dim]
    second_half = values[..., half_dim:]
    cosine = jnp.cos(angles)
    sine_part = jnp.sin(angles)
    return jnp.concatenate(
        [
            first_half * cosine - second_half * sine_part,
            second_half * cosine + first_half * sine_part,
        ],
        axis=-1,
    )


def route_blocks(dispatch_table, block_data):
    layers = dispatch_table.shape[0]
    same_layer = jnp.eye(layers, dtype=dispatch_table.dtype)
    spread = dispatch_table[:, :, :, None, :] * same_layer[:, None, None, :, None]
    moved_blocks = jnp.einsum(
        "locms,msbw->olcbw", spread, block_data, preferred_element_type=jnp.float32
    ).astype(jnp.bfloat16)
    shape = moved_blocks.shape
    return moved_blocks.reshape(shape[0], shape[1] * shape[2] * shape[3], shape[4])


def swap_halves(values, half):
    lane = lax.broadcasted_iota(jnp.int32, values.shape, 1)
    width = values.shape[1]
    wanted = jnp.where((lane % (2 * half)) < half, lane + half, lane - half)
    ahead = pltpu.roll(values, half, 1)
    behind = pltpu.roll(values, width - half, 1)
    ahead_lane = pltpu.roll(lane, half, 1)
    return jnp.where(ahead_lane == wanted, ahead, behind)


def project_kernel(x_ref, wq_ref, wkv_ref, cq_ref, sq_ref, ckv_ref, skv_ref, q_out, kv_out, kt_out):
    x = x_ref[...]
    query = jnp.dot(x, wq_ref[...], preferred_element_type=jnp.float32)
    q_out[...] = (query * cq_ref[...] + swap_halves(query, HD // 2) * sq_ref[...]).astype(
        q_out.dtype
    )
    key_value = jnp.dot(x, wkv_ref[...], preferred_element_type=jnp.float32)
    rotated = key_value * ckv_ref[...] + swap_halves(key_value, HD // 2) * skv_ref[...]
    width = kv_out.shape[2]
    for head_index in range(kv_out.shape[0]):
        block = rotated[:, head_index * width : (head_index + 1) * width].astype(kv_out.dtype)
        kv_out[head_index] = block
        kt_out[head_index] = block[:, :HD].astype(jnp.float32).T.astype(kt_out.dtype)


def project(x, w_query, w_keyval, cos_q, sin_q, cos_kv, sin_kv, tile=256):
    tokens, depth = x.shape
    q_cols, kv_cols = w_query.shape[1], w_keyval.shape[1]
    heads = kv_cols // (2 * HD)
    row_spec = lambda cols: pl.BlockSpec((tile, cols), lambda i: (i, 0))
    return pl.pallas_call(
        project_kernel,
        out_shape=(
            jax.ShapeDtypeStruct((tokens, q_cols), jnp.bfloat16),
            jax.ShapeDtypeStruct((heads, tokens, 2 * HD), jnp.bfloat16),
            jax.ShapeDtypeStruct((heads, HD, tokens), jnp.bfloat16),
        ),
        grid=(tokens // tile,),
        in_specs=[
            row_spec(depth),
            pl.BlockSpec((depth, q_cols), lambda i: (0, 0)),
            pl.BlockSpec((depth, kv_cols), lambda i: (0, 0)),
            row_spec(q_cols),
            row_spec(q_cols),
            row_spec(kv_cols),
            row_spec(kv_cols),
        ],
        out_specs=(
            row_spec(q_cols),
            pl.BlockSpec((heads, tile, 2 * HD), lambda i: (0, i, 0)),
            pl.BlockSpec((heads, HD, tile), lambda i: (0, 0, i)),
        ),
        cost_estimate=pl.CostEstimate(
            flops=2 * tokens * depth * (q_cols + kv_cols),
            transcendentals=0,
            bytes_accessed=2 * (x.size + w_query.size + w_keyval.size)
            + 8 * tokens * (q_cols + kv_cols),
        ),
    )(x, w_query, w_keyval, cos_q, sin_q, cos_kv, sin_kv)


def attention_kernel(
    length_ref, q_ref, kt_ref, kv_ref, ktf_ref, kvf_ref, wo_ref, out_ref, ctx_ref, *, tile, scale, group
):
    tile_index = pl.program_id(0)
    span, fresh = kt_ref.shape[2], ktf_ref.shape[2]
    pair = 2 * HD
    slot = lax.broadcasted_iota(jnp.int32, (tile, span), 1)
    cached_visible = slot < length_ref[0]
    token = lax.broadcasted_iota(jnp.int32, (tile, fresh), 0) + tile_index * tile
    new_slot = lax.broadcasted_iota(jnp.int32, (tile, fresh), 1)
    fresh_visible = new_slot <= token
    lane = lax.broadcasted_iota(jnp.int32, (tile, pair), 1)
    for pair_index in range(q_ref.shape[1] // pair):
        both = q_ref[:, pair_index * pair : (pair_index + 1) * pair]
        halves = []
        for parity in range(2):
            head = (2 * pair_index + parity) // group
            lined = (both if parity == 0 else pltpu.roll(both, HD, 1))[:, :HD]
            old = jnp.dot(lined, kt_ref[head], preferred_element_type=jnp.float32) * scale
            new = jnp.dot(lined, ktf_ref[head], preferred_element_type=jnp.float32) * scale
            row_max = jnp.maximum(
                jnp.max(jnp.where(cached_visible, old, -jnp.inf), axis=-1, keepdims=True),
                jnp.max(jnp.where(fresh_visible, new, -jnp.inf), axis=-1, keepdims=True),
            )
            old_w = jnp.where(cached_visible, jnp.exp(old - row_max), 0.0)
            new_w = jnp.where(fresh_visible, jnp.exp(new - row_max), 0.0)
            row_total = jnp.sum(old_w, axis=-1, keepdims=True) + jnp.sum(
                new_w, axis=-1, keepdims=True
            )
            mixed = jnp.dot(
                old_w.astype(jnp.bfloat16), kv_ref[head], preferred_element_type=jnp.float32
            ) + jnp.dot(new_w.astype(jnp.bfloat16), kvf_ref[head], preferred_element_type=jnp.float32)
            halves.append((mixed, row_total))
        (even, even_total), (odd, odd_total) = halves
        joined = jnp.where(lane < HD, pltpu.roll(even, HD, 1) / even_total, odd / odd_total)
        ctx_ref[:, pair_index * pair : (pair_index + 1) * pair] = joined.astype(ctx_ref.dtype)
    out_ref[...] = jnp.dot(ctx_ref[...], wo_ref[...], preferred_element_type=jnp.float32).astype(
        out_ref.dtype
    )


def attend(length, queries, keys_t, cache, fresh_keys_t, fresh, w_out, group, tile=256):
    tokens, q_cols = queries.shape
    span = cache.shape[1] + fresh.shape[1]
    model = w_out.shape[1]
    kernel = functools.partial(attention_kernel, tile=tile, scale=HD ** (-0.5), group=group)
    flops = 4 * tokens * q_cols * span + 2 * tokens * q_cols * model
    whole = lambda shape: pl.BlockSpec(shape, lambda i, n: (0,) * len(shape))
    return pl.pallas_call(
        kernel,
        out_shape=jax.ShapeDtypeStruct((tokens, model), jnp.bfloat16),
        grid_spec=pltpu.PrefetchScalarGridSpec(
            num_scalar_prefetch=1,
            grid=(tokens // tile,),
            in_specs=[
                pl.BlockSpec((tile, q_cols), lambda i, n: (i, 0)),
                whole(keys_t.shape),
                whole(cache.shape),
                whole(fresh_keys_t.shape),
                whole(fresh.shape),
                whole(w_out.shape),
            ],
            out_specs=pl.BlockSpec((tile, model), lambda i, n: (i, 0)),
            scratch_shapes=[pltpu.VMEM((tile, q_cols), jnp.bfloat16)],
        ),
        cost_estimate=pl.CostEstimate(
            flops=flops,
            transcendentals=tokens * (q_cols // HD) * span,
            bytes_accessed=2
            * (queries.size + keys_t.size + cache.size + fresh_keys_t.size + fresh.size + w_out.size)
            + 2 * tokens * model,
        ),
    )(length, queries, keys_t, cache, fresh_keys_t, fresh, w_out)


def norm_kernel(x_ref, gain_ref, out_ref):
    widened = x_ref[...].astype(jnp.float32)
    scale = lax.rsqrt(jnp.mean(widened * widened, axis=-1, keepdims=True) + EPSILON)
    out_ref[...] = (widened * scale * gain_ref[...]).astype(out_ref.dtype)


def rms_norm(x, gain):
    return pl.pallas_call(
        norm_kernel,
        out_shape=jax.ShapeDtypeStruct(x.shape, jnp.bfloat16),
        cost_estimate=pl.CostEstimate(
            flops=4 * x.size, transcendentals=x.shape[0], bytes_accessed=4 * x.size
        ),
    )(x, gain)


def local(tokens, norm_gain, lengths, w_query, w_keyval, w_out, kv_cache, prior_kv, owners):
    query_cols = w_query.shape[1]
    heads_here = kv_cache.shape[1]
    layer_count = owners.shape[1]
    block_count = owners.shape[3]
    span_len = prior_kv.shape[3]
    block_len = span_len // block_count
    kv_width = 2 * HD
    rows_here = heads_here * block_count
    owner_count = lax.axis_size("seq")
    capacity = (rows_here + owner_count - 1) // owner_count
    req_length = lengths[lax.axis_index("seq")]
    slot_ids = jnp.arange(span_len, dtype=jnp.int32)
    zero_index = jnp.zeros((), jnp.int32)
    owner_rows = owners[0, :, :, :, 0].reshape(layer_count, rows_here)
    owner_hits = (owner_rows[:, :, None] == jnp.arange(owner_count, dtype=jnp.int32)).astype(
        jnp.int32
    )
    owner_rank = jnp.sum((jnp.cumsum(owner_hits, axis=1) - owner_hits) * owner_hits, axis=-1)
    slot_index = owner_rows * capacity + owner_rank
    dispatch = (
        slot_index[:, None, :] == jnp.arange(owner_count * capacity, dtype=jnp.int32)[None, :, None]
    ).astype(jnp.bfloat16)
    dispatch = dispatch.reshape(layer_count, owner_count, capacity, rows_here)
    live_mask = (slot_ids < req_length + NEW_TOK)[None, None, :, None]
    earlier = jnp.where(live_mask, prior_kv[0], jnp.zeros_like(prior_kv[0]))
    earlier_rows = earlier.reshape(layer_count - 1, rows_here, block_len, kv_width)
    received_early = lax.all_to_all(
        route_blocks(dispatch[: layer_count - 1], earlier_rows), "seq", 0, 0, tiled=True
    )
    normed = rms_norm(tokens.reshape(-1, tokens.shape[-1]), norm_gain).reshape(tokens.shape)
    portion = lax.all_gather(normed, "dec", axis=0, tiled=True)
    flattened = portion.reshape(-1, portion.shape[-1])
    positions = (jnp.arange(NEW_TOK, dtype=jnp.int32) + req_length).astype(jnp.float32)
    inverse_freq = ROPE_BASE ** (-(jnp.arange(0, HD, 2, dtype=jnp.float32) / HD))
    angles = positions[:, None] * inverse_freq
    cosine, sine = jnp.cos(angles), jnp.sin(angles)
    signed_sine = jnp.concatenate([-sine, sine], axis=-1)
    head_cos = jnp.concatenate([cosine, cosine], axis=-1)
    cos_q = jnp.tile(head_cos, (1, query_cols // HD))
    sin_q = jnp.tile(signed_sine, (1, query_cols // HD))
    cos_kv = jnp.tile(jnp.concatenate([head_cos, jnp.ones_like(head_cos)], axis=-1), (1, heads_here))
    sin_kv = jnp.tile(
        jnp.concatenate([signed_sine, jnp.zeros_like(signed_sine)], axis=-1), (1, heads_here)
    )
    queries, fresh_rows, fresh_keys_t = project(
        flattened, w_query, w_keyval, cos_q, sin_q, cos_kv, sin_kv
    )
    received_early, queries = lax.optimization_barrier((received_early, queries))
    cached = kv_cache[0]
    padded = jnp.pad(cached, ((0, 0), (0, span_len - cached.shape[1]), (0, 0)))
    kept_cache = jnp.where((slot_ids < req_length)[None, :, None], padded, jnp.zeros_like(padded))
    assembled = lax.dynamic_update_slice(
        kept_cache, fresh_rows, (zero_index, req_length, zero_index)
    )
    group_size = query_cols // HD // heads_here
    product = attend(
        req_length.reshape(1),
        queries,
        jnp.transpose(cached[:, :, :HD], (0, 2, 1)),
        cached,
        fresh_keys_t,
        fresh_rows,
        w_out,
        group_size,
    )
    summed = lax.psum_scatter(
        product.reshape(NEW_TOK, 1, product.shape[-1]),
        "dec",
        scatter_dimension=0,
        tiled=True,
    )
    current_rows = assembled.reshape(1, rows_here, block_len, kv_width)
    received_last = lax.all_to_all(
        route_blocks(dispatch[layer_count - 1 :], current_rows), "seq", 0, 0, tiled=True
    )
    received = jnp.concatenate(
        [
            received_early.reshape(owner_count, layer_count - 1, capacity, block_len, kv_width),
            received_last.reshape(owner_count, 1, capacity, block_len, kv_width),
        ],
        axis=1,
    )
    decode_pool = jnp.transpose(received, (1, 0, 2, 3, 4)).reshape(
        1, 1, layer_count, owner_count, capacity, block_len, kv_width
    )
    return (summed, decode_pool)


def solution(mesh):
    in_specs = (
        P("dec", "seq", None),
        P(),
        P(),
        P(None, "dec"),
        P(None, "dec"),
        P("dec", None),
        P("seq", "dec", None, None),
        P("seq", None, "dec", None, None),
        P("seq", None, "dec", None, None),
    )
    out_specs = (P("dec", "seq", None), P("seq", "dec", None, None, None, None, None))
    return jax.shard_map(local, mesh=mesh, in_specs=in_specs, out_specs=out_specs, check_vma=False)
```

```python
import functools

import jax
import jax.numpy as jnp
from jax import lax
from jax.experimental import pallas as pl
from jax.experimental.pallas import tpu as pltpu
from jax.sharding import PartitionSpec as P

HD = 64
NEW_TOK = 512


EPSILON = 1e-06
ROPE_BASE = 10000.0


def rotate(values, angles):
    half_dim = values.shape[-1] // 2
    first_half = values[..., :half_dim]
    second_half = values[..., half_dim:]
    cosine = jnp.cos(angles)
    sine_part = jnp.sin(angles)
    return jnp.concatenate(
        [
            first_half * cosine - second_half * sine_part,
            second_half * cosine + first_half * sine_part,
        ],
        axis=-1,
    )


def route_blocks(dispatch_table, block_data):
    layers = dispatch_table.shape[0]
    same_layer = jnp.eye(layers, dtype=dispatch_table.dtype)
    spread = dispatch_table[:, :, :, None, :] * same_layer[:, None, None, :, None]
    moved_blocks = jnp.einsum(
        "locms,msbw->olcbw", spread, block_data, preferred_element_type=jnp.float32
    ).astype(jnp.bfloat16)
    shape = moved_blocks.shape
    return moved_blocks.reshape(shape[0], shape[1] * shape[2] * shape[3], shape[4])


def swap_halves(values, half):
    lane = lax.broadcasted_iota(jnp.int32, values.shape, 1)
    width = values.shape[1]
    wanted = jnp.where((lane % (2 * half)) < half, lane + half, lane - half)
    ahead = pltpu.roll(values, half, 1)
    behind = pltpu.roll(values, width - half, 1)
    ahead_lane = pltpu.roll(lane, half, 1)
    return jnp.where(ahead_lane == wanted, ahead, behind)


def project_kernel(x_ref, wq_ref, wkv_ref, cq_ref, sq_ref, ckv_ref, skv_ref, q_out, kv_out, kt_out):
    x = x_ref[...]
    query = jnp.dot(x, wq_ref[...], preferred_element_type=jnp.float32)
    q_out[...] = (query * cq_ref[...] + swap_halves(query, HD // 2) * sq_ref[...]).astype(
        q_out.dtype
    )
    key_value = jnp.dot(x, wkv_ref[...], preferred_element_type=jnp.float32)
    rotated = key_value * ckv_ref[...] + swap_halves(key_value, HD // 2) * skv_ref[...]
    width = kv_out.shape[2]
    for head_index in range(kv_out.shape[0]):
        block = rotated[:, head_index * width : (head_index + 1) * width].astype(kv_out.dtype)
        kv_out[head_index] = block
        kt_out[head_index] = block[:, :HD].astype(jnp.float32).T.astype(kt_out.dtype)


def project(x, w_query, w_keyval, cos_q, sin_q, cos_kv, sin_kv, tile=256):
    tokens, depth = x.shape
    q_cols, kv_cols = w_query.shape[1], w_keyval.shape[1]
    heads = kv_cols // (2 * HD)
    row_spec = lambda cols: pl.BlockSpec((tile, cols), lambda i: (i, 0))
    return pl.pallas_call(
        project_kernel,
        out_shape=(
            jax.ShapeDtypeStruct((tokens, q_cols), jnp.bfloat16),
            jax.ShapeDtypeStruct((heads, tokens, 2 * HD), jnp.bfloat16),
            jax.ShapeDtypeStruct((heads, HD, tokens), jnp.bfloat16),
        ),
        grid=(tokens // tile,),
        in_specs=[
            row_spec(depth),
            pl.BlockSpec((depth, q_cols), lambda i: (0, 0)),
            pl.BlockSpec((depth, kv_cols), lambda i: (0, 0)),
            row_spec(q_cols),
            row_spec(q_cols),
            row_spec(kv_cols),
            row_spec(kv_cols),
        ],
        out_specs=(
            row_spec(q_cols),
            pl.BlockSpec((heads, tile, 2 * HD), lambda i: (0, i, 0)),
            pl.BlockSpec((heads, HD, tile), lambda i: (0, 0, i)),
        ),
        cost_estimate=pl.CostEstimate(
            flops=2 * tokens * depth * (q_cols + kv_cols),
            transcendentals=0,
            bytes_accessed=2 * (x.size + w_query.size + w_keyval.size)
            + 8 * tokens * (q_cols + kv_cols),
        ),
    )(x, w_query, w_keyval, cos_q, sin_q, cos_kv, sin_kv)


def attention_kernel(
    length_ref, q_ref, kt_ref, kv_ref, ktf_ref, kvf_ref, wo_ref, out_ref, ctx_ref, *, tile, scale, group
):
    tile_index = pl.program_id(0)
    span, fresh = kt_ref.shape[2], ktf_ref.shape[2]
    pair = 2 * HD
    slot = lax.broadcasted_iota(jnp.int32, (1, span), 1)
    cached_bias = jnp.where(slot < length_ref[0], 0.0, -jnp.inf).astype(jnp.float32)
    token = lax.broadcasted_iota(jnp.int32, (tile, fresh), 0) + tile_index * tile
    new_slot = lax.broadcasted_iota(jnp.int32, (tile, fresh), 1)
    fresh_bias = jnp.where(new_slot <= token, 0.0, -jnp.inf).astype(jnp.float32)
    lane = lax.broadcasted_iota(jnp.int32, (tile, pair), 1)
    for pair_index in range(q_ref.shape[1] // pair):
        both = q_ref[:, pair_index * pair : (pair_index + 1) * pair]
        halves = []
        for parity in range(2):
            head = (2 * pair_index + parity) // group
            lined = (both if parity == 0 else pltpu.roll(both, HD, 1))[:, :HD]
            lined = lined * jnp.asarray(scale, lined.dtype)
            old = jnp.dot(lined, kt_ref[head], preferred_element_type=jnp.float32) + cached_bias
            new = jnp.dot(lined, ktf_ref[head], preferred_element_type=jnp.float32) + fresh_bias
            row_max = jnp.maximum(
                jnp.max(old, axis=-1, keepdims=True), jnp.max(new, axis=-1, keepdims=True)
            )
            old_w = jnp.exp(old - row_max)
            new_w = jnp.exp(new - row_max)
            row_total = jnp.sum(old_w, axis=-1, keepdims=True) + jnp.sum(
                new_w, axis=-1, keepdims=True
            )
            mixed = jnp.dot(
                old_w.astype(jnp.bfloat16), kv_ref[head], preferred_element_type=jnp.float32
            ) + jnp.dot(new_w.astype(jnp.bfloat16), kvf_ref[head], preferred_element_type=jnp.float32)
            halves.append((mixed, row_total))
        (even, even_total), (odd, odd_total) = halves
        joined = jnp.where(lane < HD, pltpu.roll(even, HD, 1) / even_total, odd / odd_total)
        ctx_ref[:, pair_index * pair : (pair_index + 1) * pair] = joined.astype(ctx_ref.dtype)
    out_ref[...] = jnp.dot(ctx_ref[...], wo_ref[...], preferred_element_type=jnp.float32).astype(
        out_ref.dtype
    )


def attend(length, queries, keys_t, cache, fresh_keys_t, fresh, w_out, group, tile=256):
    tokens, q_cols = queries.shape
    span = cache.shape[1] + fresh.shape[1]
    model = w_out.shape[1]
    kernel = functools.partial(attention_kernel, tile=tile, scale=HD ** (-0.5), group=group)
    flops = 4 * tokens * q_cols * span + 2 * tokens * q_cols * model
    whole = lambda shape: pl.BlockSpec(shape, lambda i, n: (0,) * len(shape))
    return pl.pallas_call(
        kernel,
        out_shape=jax.ShapeDtypeStruct((tokens, model), jnp.bfloat16),
        grid_spec=pltpu.PrefetchScalarGridSpec(
            num_scalar_prefetch=1,
            grid=(tokens // tile,),
            in_specs=[
                pl.BlockSpec((tile, q_cols), lambda i, n: (i, 0)),
                whole(keys_t.shape),
                whole(cache.shape),
                whole(fresh_keys_t.shape),
                whole(fresh.shape),
                whole(w_out.shape),
            ],
            out_specs=pl.BlockSpec((tile, model), lambda i, n: (i, 0)),
            scratch_shapes=[pltpu.VMEM((tile, q_cols), jnp.bfloat16)],
        ),
        cost_estimate=pl.CostEstimate(
            flops=flops,
            transcendentals=tokens * (q_cols // HD) * span,
            bytes_accessed=2
            * (queries.size + keys_t.size + cache.size + fresh_keys_t.size + fresh.size + w_out.size)
            + 2 * tokens * model,
        ),
    )(length, queries, keys_t, cache, fresh_keys_t, fresh, w_out)


def norm_kernel(x_ref, gain_ref, out_ref):
    widened = x_ref[...].astype(jnp.float32)
    scale = lax.rsqrt(jnp.mean(widened * widened, axis=-1, keepdims=True) + EPSILON)
    out_ref[...] = (widened * scale * gain_ref[...]).astype(out_ref.dtype)


def rms_norm(x, gain):
    return pl.pallas_call(
        norm_kernel,
        out_shape=jax.ShapeDtypeStruct(x.shape, jnp.bfloat16),
        cost_estimate=pl.CostEstimate(
            flops=4 * x.size, transcendentals=x.shape[0], bytes_accessed=4 * x.size
        ),
    )(x, gain)


def local(tokens, norm_gain, lengths, w_query, w_keyval, w_out, kv_cache, prior_kv, owners):
    query_cols = w_query.shape[1]
    heads_here = kv_cache.shape[1]
    layer_count = owners.shape[1]
    block_count = owners.shape[3]
    span_len = prior_kv.shape[3]
    block_len = span_len // block_count
    kv_width = 2 * HD
    rows_here = heads_here * block_count
    owner_count = lax.axis_size("seq")
    capacity = (rows_here + owner_count - 1) // owner_count
    req_length = lengths[lax.axis_index("seq")]
    slot_ids = jnp.arange(span_len, dtype=jnp.int32)
    zero_index = jnp.zeros((), jnp.int32)
    owner_rows = owners[0, :, :, :, 0].reshape(layer_count, rows_here)
    owner_hits = (owner_rows[:, :, None] == jnp.arange(owner_count, dtype=jnp.int32)).astype(
        jnp.int32
    )
    owner_rank = jnp.sum((jnp.cumsum(owner_hits, axis=1) - owner_hits) * owner_hits, axis=-1)
    slot_index = owner_rows * capacity + owner_rank
    dispatch = (
        slot_index[:, None, :] == jnp.arange(owner_count * capacity, dtype=jnp.int32)[None, :, None]
    ).astype(jnp.bfloat16)
    dispatch = dispatch.reshape(layer_count, owner_count, capacity, rows_here)
    live_mask = (slot_ids < req_length + NEW_TOK)[None, None, :, None]
    earlier = jnp.where(live_mask, prior_kv[0], jnp.zeros_like(prior_kv[0]))
    earlier_rows = earlier.reshape(layer_count - 1, rows_here, block_len, kv_width)
    received_early = lax.all_to_all(
        route_blocks(dispatch[: layer_count - 1], earlier_rows), "seq", 0, 0, tiled=True
    )
    normed = rms_norm(tokens.reshape(-1, tokens.shape[-1]), norm_gain).reshape(tokens.shape)
    portion = lax.all_gather(normed, "dec", axis=0, tiled=True)
    flattened = portion.reshape(-1, portion.shape[-1])
    positions = (jnp.arange(NEW_TOK, dtype=jnp.int32) + req_length).astype(jnp.float32)
    inverse_freq = ROPE_BASE ** (-(jnp.arange(0, HD, 2, dtype=jnp.float32) / HD))
    angles = positions[:, None] * inverse_freq
    cosine, sine = jnp.cos(angles), jnp.sin(angles)
    signed_sine = jnp.concatenate([-sine, sine], axis=-1)
    head_cos = jnp.concatenate([cosine, cosine], axis=-1)
    cos_q = jnp.tile(head_cos, (1, query_cols // HD))
    sin_q = jnp.tile(signed_sine, (1, query_cols // HD))
    cos_kv = jnp.tile(jnp.concatenate([head_cos, jnp.ones_like(head_cos)], axis=-1), (1, heads_here))
    sin_kv = jnp.tile(
        jnp.concatenate([signed_sine, jnp.zeros_like(signed_sine)], axis=-1), (1, heads_here)
    )
    queries, fresh_rows, fresh_keys_t = project(
        flattened, w_query, w_keyval, cos_q, sin_q, cos_kv, sin_kv
    )
    received_early, queries = lax.optimization_barrier((received_early, queries))
    cached = kv_cache[0]
    padded = jnp.pad(cached, ((0, 0), (0, span_len - cached.shape[1]), (0, 0)))
    kept_cache = jnp.where((slot_ids < req_length)[None, :, None], padded, jnp.zeros_like(padded))
    assembled = lax.dynamic_update_slice(
        kept_cache, fresh_rows, (zero_index, req_length, zero_index)
    )
    group_size = query_cols // HD // heads_here
    product = attend(
        req_length.reshape(1),
        queries,
        jnp.transpose(cached[:, :, :HD], (0, 2, 1)),
        cached,
        fresh_keys_t,
        fresh_rows,
        w_out,
        group_size,
    )
    summed = lax.psum_scatter(
        product.reshape(NEW_TOK, 1, product.shape[-1]),
        "dec",
        scatter_dimension=0,
        tiled=True,
    )
    current_rows = assembled.reshape(1, rows_here, block_len, kv_width)
    received_last = lax.all_to_all(
        route_blocks(dispatch[layer_count - 1 :], current_rows), "seq", 0, 0, tiled=True
    )
    received = jnp.concatenate(
        [
            received_early.reshape(owner_count, layer_count - 1, capacity, block_len, kv_width),
            received_last.reshape(owner_count, 1, capacity, block_len, kv_width),
        ],
        axis=1,
    )
    decode_pool = jnp.transpose(received, (1, 0, 2, 3, 4)).reshape(
        1, 1, layer_count, owner_count, capacity, block_len, kv_width
    )
    return (summed, decode_pool)


def solution(mesh):
    in_specs = (
        P("dec", "seq", None),
        P(),
        P(),
        P(None, "dec"),
        P(None, "dec"),
        P("dec", None),
        P("seq", "dec", None, None),
        P("seq", None, "dec", None, None),
        P("seq", None, "dec", None, None),
    )
    out_specs = (P("dec", "seq", None), P("seq", "dec", None, None, None, None, None))
    return jax.shard_map(local, mesh=mesh, in_specs=in_specs, out_specs=out_specs, check_vma=False)
```

```python
import functools

import jax
import jax.numpy as jnp
from jax import lax
from jax.experimental import pallas as pl
from jax.experimental.pallas import tpu as pltpu
from jax.sharding import PartitionSpec as P

HD = 64
NEW_TOK = 512


EPSILON = 1e-06
ROPE_BASE = 10000.0


def rotate(values, angles):
    half_dim = values.shape[-1] // 2
    first_half = values[..., :half_dim]
    second_half = values[..., half_dim:]
    cosine = jnp.cos(angles)
    sine_part = jnp.sin(angles)
    return jnp.concatenate(
        [
            first_half * cosine - second_half * sine_part,
            second_half * cosine + first_half * sine_part,
        ],
        axis=-1,
    )


def route_blocks(dispatch_table, block_data):
    layers = dispatch_table.shape[0]
    same_layer = jnp.eye(layers, dtype=dispatch_table.dtype)
    spread = dispatch_table[:, :, :, None, :] * same_layer[:, None, None, :, None]
    moved_blocks = jnp.einsum(
        "locms,msbw->olcbw", spread, block_data, preferred_element_type=jnp.float32
    ).astype(jnp.bfloat16)
    shape = moved_blocks.shape
    return moved_blocks.reshape(shape[0], shape[1] * shape[2] * shape[3], shape[4])


def swap_halves(values, half):
    lane = lax.broadcasted_iota(jnp.int32, values.shape, 1)
    width = values.shape[1]
    wanted = jnp.where((lane % (2 * half)) < half, lane + half, lane - half)
    ahead = pltpu.roll(values, half, 1)
    behind = pltpu.roll(values, width - half, 1)
    ahead_lane = pltpu.roll(lane, half, 1)
    return jnp.where(ahead_lane == wanted, ahead, behind)


def project_kernel(
    x_ref, gain_ref, wq_ref, wkv_ref, cq_ref, sq_ref, ckv_ref, skv_ref, q_out, kv_out, kt_out
):
    widened = x_ref[...].astype(jnp.float32)
    scale = lax.rsqrt(jnp.mean(widened * widened, axis=-1, keepdims=True) + EPSILON)
    x = (widened * scale * gain_ref[...]).astype(jnp.bfloat16)
    query = jnp.dot(x, wq_ref[...], preferred_element_type=jnp.float32)
    q_out[...] = (query * cq_ref[...] + swap_halves(query, HD // 2) * sq_ref[...]).astype(
        q_out.dtype
    )
    key_value = jnp.dot(x, wkv_ref[...], preferred_element_type=jnp.float32)
    rotated = key_value * ckv_ref[...] + swap_halves(key_value, HD // 2) * skv_ref[...]
    width = kv_out.shape[2]
    for head_index in range(kv_out.shape[0]):
        block = rotated[:, head_index * width : (head_index + 1) * width].astype(kv_out.dtype)
        kv_out[head_index] = block
        kt_out[head_index] = block[:, :HD].astype(jnp.float32).T.astype(kt_out.dtype)


def project(x, gain, w_query, w_keyval, cos_q, sin_q, cos_kv, sin_kv, tile=256):
    tokens, depth = x.shape
    q_cols, kv_cols = w_query.shape[1], w_keyval.shape[1]
    heads = kv_cols // (2 * HD)
    row_spec = lambda cols: pl.BlockSpec((tile, cols), lambda i: (i, 0))
    return pl.pallas_call(
        project_kernel,
        out_shape=(
            jax.ShapeDtypeStruct((tokens, q_cols), jnp.bfloat16),
            jax.ShapeDtypeStruct((heads, tokens, 2 * HD), jnp.bfloat16),
            jax.ShapeDtypeStruct((heads, HD, tokens), jnp.bfloat16),
        ),
        grid=(tokens // tile,),
        in_specs=[
            row_spec(depth),
            pl.BlockSpec((depth,), lambda i: (0,)),
            pl.BlockSpec((depth, q_cols), lambda i: (0, 0)),
            pl.BlockSpec((depth, kv_cols), lambda i: (0, 0)),
            row_spec(q_cols),
            row_spec(q_cols),
            row_spec(kv_cols),
            row_spec(kv_cols),
        ],
        out_specs=(
            row_spec(q_cols),
            pl.BlockSpec((heads, tile, 2 * HD), lambda i: (0, i, 0)),
            pl.BlockSpec((heads, HD, tile), lambda i: (0, 0, i)),
        ),
        cost_estimate=pl.CostEstimate(
            flops=2 * tokens * depth * (q_cols + kv_cols),
            transcendentals=0,
            bytes_accessed=2 * (x.size + w_query.size + w_keyval.size)
            + 8 * tokens * (q_cols + kv_cols),
        ),
    )(x, gain, w_query, w_keyval, cos_q, sin_q, cos_kv, sin_kv)


def attention_kernel(
    length_ref, q_ref, kt_ref, kv_ref, ktf_ref, kvf_ref, wo_ref, out_ref, ctx_ref, *, tile, scale, group
):
    tile_index = pl.program_id(0)
    span, fresh = kt_ref.shape[2], ktf_ref.shape[2]
    pair = 2 * HD
    slot = lax.broadcasted_iota(jnp.int32, (1, span), 1)
    cached_bias = jnp.where(slot < length_ref[0], 0.0, -jnp.inf).astype(jnp.float32)
    token = lax.broadcasted_iota(jnp.int32, (tile, fresh), 0) + tile_index * tile
    new_slot = lax.broadcasted_iota(jnp.int32, (tile, fresh), 1)
    fresh_bias = jnp.where(new_slot <= token, 0.0, -jnp.inf).astype(jnp.float32)
    lane = lax.broadcasted_iota(jnp.int32, (tile, pair), 1)
    for pair_index in range(q_ref.shape[1] // pair):
        both = q_ref[:, pair_index * pair : (pair_index + 1) * pair]
        halves = []
        for parity in range(2):
            head = (2 * pair_index + parity) // group
            lined = (both if parity == 0 else pltpu.roll(both, HD, 1))[:, :HD]
            lined = lined * jnp.asarray(scale, lined.dtype)
            old = jnp.dot(lined, kt_ref[head], preferred_element_type=jnp.float32) + cached_bias
            new = jnp.dot(lined, ktf_ref[head], preferred_element_type=jnp.float32) + fresh_bias
            row_max = jnp.maximum(
                jnp.max(old, axis=-1, keepdims=True), jnp.max(new, axis=-1, keepdims=True)
            )
            old_w = jnp.exp(old - row_max)
            new_w = jnp.exp(new - row_max)
            row_total = jnp.sum(old_w, axis=-1, keepdims=True) + jnp.sum(
                new_w, axis=-1, keepdims=True
            )
            mixed = jnp.dot(
                old_w.astype(jnp.bfloat16), kv_ref[head], preferred_element_type=jnp.float32
            ) + jnp.dot(new_w.astype(jnp.bfloat16), kvf_ref[head], preferred_element_type=jnp.float32)
            halves.append((mixed, row_total))
        (even, even_total), (odd, odd_total) = halves
        joined = jnp.where(lane < HD, pltpu.roll(even, HD, 1) / even_total, odd / odd_total)
        ctx_ref[:, pair_index * pair : (pair_index + 1) * pair] = joined.astype(ctx_ref.dtype)
    out_ref[...] = jnp.dot(ctx_ref[...], wo_ref[...], preferred_element_type=jnp.float32).astype(
        out_ref.dtype
    )


def attend(length, queries, keys_t, cache, fresh_keys_t, fresh, w_out, group, tile=256):
    tokens, q_cols = queries.shape
    span = cache.shape[1] + fresh.shape[1]
    model = w_out.shape[1]
    kernel = functools.partial(attention_kernel, tile=tile, scale=HD ** (-0.5), group=group)
    flops = 4 * tokens * q_cols * span + 2 * tokens * q_cols * model
    whole = lambda shape: pl.BlockSpec(shape, lambda i, n: (0,) * len(shape))
    return pl.pallas_call(
        kernel,
        out_shape=jax.ShapeDtypeStruct((tokens, model), jnp.bfloat16),
        grid_spec=pltpu.PrefetchScalarGridSpec(
            num_scalar_prefetch=1,
            grid=(tokens // tile,),
            in_specs=[
                pl.BlockSpec((tile, q_cols), lambda i, n: (i, 0)),
                whole(keys_t.shape),
                whole(cache.shape),
                whole(fresh_keys_t.shape),
                whole(fresh.shape),
                whole(w_out.shape),
            ],
            out_specs=pl.BlockSpec((tile, model), lambda i, n: (i, 0)),
            scratch_shapes=[pltpu.VMEM((tile, q_cols), jnp.bfloat16)],
        ),
        cost_estimate=pl.CostEstimate(
            flops=flops,
            transcendentals=tokens * (q_cols // HD) * span,
            bytes_accessed=2
            * (queries.size + keys_t.size + cache.size + fresh_keys_t.size + fresh.size + w_out.size)
            + 2 * tokens * model,
        ),
    )(length, queries, keys_t, cache, fresh_keys_t, fresh, w_out)


def norm_kernel(x_ref, gain_ref, out_ref):
    widened = x_ref[...].astype(jnp.float32)
    scale = lax.rsqrt(jnp.mean(widened * widened, axis=-1, keepdims=True) + EPSILON)
    out_ref[...] = (widened * scale * gain_ref[...]).astype(out_ref.dtype)


def rms_norm(x, gain):
    return pl.pallas_call(
        norm_kernel,
        out_shape=jax.ShapeDtypeStruct(x.shape, jnp.bfloat16),
        cost_estimate=pl.CostEstimate(
            flops=4 * x.size, transcendentals=x.shape[0], bytes_accessed=4 * x.size
        ),
    )(x, gain)


def local(tokens, norm_gain, lengths, w_query, w_keyval, w_out, kv_cache, prior_kv, owners):
    query_cols = w_query.shape[1]
    heads_here = kv_cache.shape[1]
    layer_count = owners.shape[1]
    block_count = owners.shape[3]
    span_len = prior_kv.shape[3]
    block_len = span_len // block_count
    kv_width = 2 * HD
    rows_here = heads_here * block_count
    owner_count = lax.axis_size("seq")
    capacity = (rows_here + owner_count - 1) // owner_count
    req_length = lengths[lax.axis_index("seq")]
    slot_ids = jnp.arange(span_len, dtype=jnp.int32)
    zero_index = jnp.zeros((), jnp.int32)
    owner_rows = owners[0, :, :, :, 0].reshape(layer_count, rows_here)
    owner_hits = (owner_rows[:, :, None] == jnp.arange(owner_count, dtype=jnp.int32)).astype(
        jnp.int32
    )
    owner_rank = jnp.sum((jnp.cumsum(owner_hits, axis=1) - owner_hits) * owner_hits, axis=-1)
    slot_index = owner_rows * capacity + owner_rank
    dispatch = (
        slot_index[:, None, :] == jnp.arange(owner_count * capacity, dtype=jnp.int32)[None, :, None]
    ).astype(jnp.bfloat16)
    dispatch = dispatch.reshape(layer_count, owner_count, capacity, rows_here)
    live_mask = (slot_ids < req_length + NEW_TOK)[None, None, :, None]
    earlier = jnp.where(live_mask, prior_kv[0], jnp.zeros_like(prior_kv[0]))
    earlier_rows = earlier.reshape(layer_count - 1, rows_here, block_len, kv_width)
    received_early = lax.all_to_all(
        route_blocks(dispatch[: layer_count - 1], earlier_rows), "seq", 0, 0, tiled=True
    )
    portion = lax.all_gather(tokens, "dec", axis=0, tiled=True)
    flattened = portion.reshape(-1, portion.shape[-1])
    positions = (jnp.arange(NEW_TOK, dtype=jnp.int32) + req_length).astype(jnp.float32)
    inverse_freq = ROPE_BASE ** (-(jnp.arange(0, HD, 2, dtype=jnp.float32) / HD))
    angles = positions[:, None] * inverse_freq
    cosine, sine = jnp.cos(angles), jnp.sin(angles)
    signed_sine = jnp.concatenate([-sine, sine], axis=-1)
    head_cos = jnp.concatenate([cosine, cosine], axis=-1)
    cos_q = jnp.tile(head_cos, (1, query_cols // HD))
    sin_q = jnp.tile(signed_sine, (1, query_cols // HD))
    cos_kv = jnp.tile(jnp.concatenate([head_cos, jnp.ones_like(head_cos)], axis=-1), (1, heads_here))
    sin_kv = jnp.tile(
        jnp.concatenate([signed_sine, jnp.zeros_like(signed_sine)], axis=-1), (1, heads_here)
    )
    queries, fresh_rows, fresh_keys_t = project(
        flattened, norm_gain, w_query, w_keyval, cos_q, sin_q, cos_kv, sin_kv
    )
    received_early, queries = lax.optimization_barrier((received_early, queries))
    cached = kv_cache[0]
    padded = jnp.pad(cached, ((0, 0), (0, span_len - cached.shape[1]), (0, 0)))
    kept_cache = jnp.where((slot_ids < req_length)[None, :, None], padded, jnp.zeros_like(padded))
    assembled = lax.dynamic_update_slice(
        kept_cache, fresh_rows, (zero_index, req_length, zero_index)
    )
    group_size = query_cols // HD // heads_here
    product = attend(
        req_length.reshape(1),
        queries,
        jnp.transpose(cached[:, :, :HD], (0, 2, 1)),
        cached,
        fresh_keys_t,
        fresh_rows,
        w_out,
        group_size,
    )
    summed = lax.psum_scatter(
        product.reshape(NEW_TOK, 1, product.shape[-1]),
        "dec",
        scatter_dimension=0,
        tiled=True,
    )
    current_rows = assembled.reshape(1, rows_here, block_len, kv_width)
    received_last = lax.all_to_all(
        route_blocks(dispatch[layer_count - 1 :], current_rows), "seq", 0, 0, tiled=True
    )
    received = jnp.concatenate(
        [
            received_early.reshape(owner_count, layer_count - 1, capacity, block_len, kv_width),
            received_last.reshape(owner_count, 1, capacity, block_len, kv_width),
        ],
        axis=1,
    )
    decode_pool = jnp.transpose(received, (1, 0, 2, 3, 4)).reshape(
        1, 1, layer_count, owner_count, capacity, block_len, kv_width
    )
    return (summed, decode_pool)


def solution(mesh):
    in_specs = (
        P("dec", "seq", None),
        P(),
        P(),
        P(None, "dec"),
        P(None, "dec"),
        P("dec", None),
        P("seq", "dec", None, None),
        P("seq", None, "dec", None, None),
        P("seq", None, "dec", None, None),
    )
    out_specs = (P("dec", "seq", None), P("seq", "dec", None, None, None, None, None))
    return jax.shard_map(local, mesh=mesh, in_specs=in_specs, out_specs=out_specs, check_vma=False)
```

```python
import functools

import jax
import jax.numpy as jnp
from jax import lax
from jax.experimental import pallas as pl
from jax.experimental.pallas import tpu as pltpu
from jax.sharding import PartitionSpec as P

HD = 64
NEW_TOK = 512


EPSILON = 1e-06
ROPE_BASE = 10000.0


def rotate(values, angles):
    half_dim = values.shape[-1] // 2
    first_half = values[..., :half_dim]
    second_half = values[..., half_dim:]
    cosine = jnp.cos(angles)
    sine_part = jnp.sin(angles)
    return jnp.concatenate(
        [
            first_half * cosine - second_half * sine_part,
            second_half * cosine + first_half * sine_part,
        ],
        axis=-1,
    )


def route_blocks(dispatch_table, block_data):
    layers = dispatch_table.shape[0]
    same_layer = jnp.eye(layers, dtype=dispatch_table.dtype)
    spread = dispatch_table[:, :, :, None, :] * same_layer[:, None, None, :, None]
    moved_blocks = jnp.einsum(
        "locms,msbw->olcbw", spread, block_data, preferred_element_type=jnp.float32
    ).astype(jnp.bfloat16)
    shape = moved_blocks.shape
    return moved_blocks.reshape(shape[0], shape[1] * shape[2] * shape[3], shape[4])


def swap_halves(values, half):
    lane = lax.broadcasted_iota(jnp.int32, values.shape, 1)
    width = values.shape[1]
    wanted = jnp.where((lane % (2 * half)) < half, lane + half, lane - half)
    ahead = pltpu.roll(values, half, 1)
    behind = pltpu.roll(values, width - half, 1)
    ahead_lane = pltpu.roll(lane, half, 1)
    return jnp.where(ahead_lane == wanted, ahead, behind)


def project_kernel(
    x_ref, gain_ref, wq_ref, wkv_ref, cq_ref, sq_ref, ckv_ref, skv_ref, q_out, kv_out, kt_out
):
    widened = x_ref[...].astype(jnp.float32)
    scale = lax.rsqrt(jnp.mean(widened * widened, axis=-1, keepdims=True) + EPSILON)
    x = (widened * scale * gain_ref[...]).astype(jnp.bfloat16)
    query = jnp.dot(x, wq_ref[...], preferred_element_type=jnp.float32)
    q_out[...] = (query * cq_ref[...] + swap_halves(query, HD // 2) * sq_ref[...]).astype(
        q_out.dtype
    )
    key_value = jnp.dot(x, wkv_ref[...], preferred_element_type=jnp.float32)
    rotated = key_value * ckv_ref[...] + swap_halves(key_value, HD // 2) * skv_ref[...]
    width = kv_out.shape[2]
    for head_index in range(kv_out.shape[0]):
        block = rotated[:, head_index * width : (head_index + 1) * width].astype(kv_out.dtype)
        kv_out[head_index] = block
        kt_out[head_index] = block[:, :HD].astype(jnp.float32).T.astype(kt_out.dtype)


def project(x, gain, w_query, w_keyval, cos_q, sin_q, cos_kv, sin_kv, tile=128):
    tokens, depth = x.shape
    q_cols, kv_cols = w_query.shape[1], w_keyval.shape[1]
    heads = kv_cols // (2 * HD)
    row_spec = lambda cols: pl.BlockSpec((tile, cols), lambda i: (i, 0))
    return pl.pallas_call(
        project_kernel,
        out_shape=(
            jax.ShapeDtypeStruct((tokens, q_cols), jnp.bfloat16),
            jax.ShapeDtypeStruct((heads, tokens, 2 * HD), jnp.bfloat16),
            jax.ShapeDtypeStruct((heads, HD, tokens), jnp.bfloat16),
        ),
        grid=(tokens // tile,),
        in_specs=[
            row_spec(depth),
            pl.BlockSpec((depth,), lambda i: (0,)),
            pl.BlockSpec((depth, q_cols), lambda i: (0, 0)),
            pl.BlockSpec((depth, kv_cols), lambda i: (0, 0)),
            row_spec(q_cols),
            row_spec(q_cols),
            row_spec(kv_cols),
            row_spec(kv_cols),
        ],
        out_specs=(
            row_spec(q_cols),
            pl.BlockSpec((heads, tile, 2 * HD), lambda i: (0, i, 0)),
            pl.BlockSpec((heads, HD, tile), lambda i: (0, 0, i)),
        ),
        cost_estimate=pl.CostEstimate(
            flops=2 * tokens * depth * (q_cols + kv_cols),
            transcendentals=0,
            bytes_accessed=2 * (x.size + w_query.size + w_keyval.size)
            + 8 * tokens * (q_cols + kv_cols),
        ),
    )(x, gain, w_query, w_keyval, cos_q, sin_q, cos_kv, sin_kv)


def attention_kernel(
    length_ref, q_ref, kt_ref, kv_ref, ktf_ref, kvf_ref, wo_ref, out_ref, ctx_ref, *, tile, scale, group
):
    tile_index = pl.program_id(0)
    span, fresh = kt_ref.shape[2], ktf_ref.shape[2]
    pair = 2 * HD
    slot = lax.broadcasted_iota(jnp.int32, (1, span), 1)
    cached_bias = jnp.where(slot < length_ref[0], 0.0, -jnp.inf).astype(jnp.float32)
    token = lax.broadcasted_iota(jnp.int32, (tile, fresh), 0) + tile_index * tile
    new_slot = lax.broadcasted_iota(jnp.int32, (tile, fresh), 1)
    fresh_bias = jnp.where(new_slot <= token, 0.0, -jnp.inf).astype(jnp.float32)
    lane = lax.broadcasted_iota(jnp.int32, (tile, pair), 1)
    for pair_index in range(q_ref.shape[1] // pair):
        both = q_ref[:, pair_index * pair : (pair_index + 1) * pair]
        halves = []
        for parity in range(2):
            head = (2 * pair_index + parity) // group
            lined = (both if parity == 0 else pltpu.roll(both, HD, 1))[:, :HD]
            lined = lined * jnp.asarray(scale, lined.dtype)
            old = jnp.dot(lined, kt_ref[head], preferred_element_type=jnp.float32) + cached_bias
            new = jnp.dot(lined, ktf_ref[head], preferred_element_type=jnp.float32) + fresh_bias
            row_max = jnp.maximum(
                jnp.max(old, axis=-1, keepdims=True), jnp.max(new, axis=-1, keepdims=True)
            )
            old_w = jnp.exp(old - row_max)
            new_w = jnp.exp(new - row_max)
            row_total = jnp.sum(old_w, axis=-1, keepdims=True) + jnp.sum(
                new_w, axis=-1, keepdims=True
            )
            mixed = jnp.dot(
                old_w.astype(jnp.bfloat16), kv_ref[head], preferred_element_type=jnp.float32
            ) + jnp.dot(new_w.astype(jnp.bfloat16), kvf_ref[head], preferred_element_type=jnp.float32)
            halves.append((mixed, row_total))
        (even, even_total), (odd, odd_total) = halves
        joined = jnp.where(lane < HD, pltpu.roll(even, HD, 1) / even_total, odd / odd_total)
        ctx_ref[:, pair_index * pair : (pair_index + 1) * pair] = joined.astype(ctx_ref.dtype)
    out_ref[...] = jnp.dot(ctx_ref[...], wo_ref[...], preferred_element_type=jnp.float32).astype(
        out_ref.dtype
    )


def attend(length, queries, keys_t, cache, fresh_keys_t, fresh, w_out, group, tile=256):
    tokens, q_cols = queries.shape
    span = cache.shape[1] + fresh.shape[1]
    model = w_out.shape[1]
    kernel = functools.partial(attention_kernel, tile=tile, scale=HD ** (-0.5), group=group)
    flops = 4 * tokens * q_cols * span + 2 * tokens * q_cols * model
    whole = lambda shape: pl.BlockSpec(shape, lambda i, n: (0,) * len(shape))
    return pl.pallas_call(
        kernel,
        out_shape=jax.ShapeDtypeStruct((tokens, model), jnp.bfloat16),
        grid_spec=pltpu.PrefetchScalarGridSpec(
            num_scalar_prefetch=1,
            grid=(tokens // tile,),
            in_specs=[
                pl.BlockSpec((tile, q_cols), lambda i, n: (i, 0)),
                whole(keys_t.shape),
                whole(cache.shape),
                whole(fresh_keys_t.shape),
                whole(fresh.shape),
                whole(w_out.shape),
            ],
            out_specs=pl.BlockSpec((tile, model), lambda i, n: (i, 0)),
            scratch_shapes=[pltpu.VMEM((tile, q_cols), jnp.bfloat16)],
        ),
        cost_estimate=pl.CostEstimate(
            flops=flops,
            transcendentals=tokens * (q_cols // HD) * span,
            bytes_accessed=2
            * (queries.size + keys_t.size + cache.size + fresh_keys_t.size + fresh.size + w_out.size)
            + 2 * tokens * model,
        ),
    )(length, queries, keys_t, cache, fresh_keys_t, fresh, w_out)


def norm_kernel(x_ref, gain_ref, out_ref):
    widened = x_ref[...].astype(jnp.float32)
    scale = lax.rsqrt(jnp.mean(widened * widened, axis=-1, keepdims=True) + EPSILON)
    out_ref[...] = (widened * scale * gain_ref[...]).astype(out_ref.dtype)


def rms_norm(x, gain):
    return pl.pallas_call(
        norm_kernel,
        out_shape=jax.ShapeDtypeStruct(x.shape, jnp.bfloat16),
        cost_estimate=pl.CostEstimate(
            flops=4 * x.size, transcendentals=x.shape[0], bytes_accessed=4 * x.size
        ),
    )(x, gain)


def local(tokens, norm_gain, lengths, w_query, w_keyval, w_out, kv_cache, prior_kv, owners):
    query_cols = w_query.shape[1]
    heads_here = kv_cache.shape[1]
    layer_count = owners.shape[1]
    block_count = owners.shape[3]
    span_len = prior_kv.shape[3]
    block_len = span_len // block_count
    kv_width = 2 * HD
    rows_here = heads_here * block_count
    owner_count = lax.axis_size("seq")
    capacity = (rows_here + owner_count - 1) // owner_count
    req_length = lengths[lax.axis_index("seq")]
    slot_ids = jnp.arange(span_len, dtype=jnp.int32)
    zero_index = jnp.zeros((), jnp.int32)
    owner_rows = owners[0, :, :, :, 0].reshape(layer_count, rows_here)
    owner_hits = (owner_rows[:, :, None] == jnp.arange(owner_count, dtype=jnp.int32)).astype(
        jnp.int32
    )
    owner_rank = jnp.sum((jnp.cumsum(owner_hits, axis=1) - owner_hits) * owner_hits, axis=-1)
    slot_index = owner_rows * capacity + owner_rank
    dispatch = (
        slot_index[:, None, :] == jnp.arange(owner_count * capacity, dtype=jnp.int32)[None, :, None]
    ).astype(jnp.bfloat16)
    dispatch = dispatch.reshape(layer_count, owner_count, capacity, rows_here)
    live_mask = (slot_ids < req_length + NEW_TOK)[None, None, :, None]
    earlier = jnp.where(live_mask, prior_kv[0], jnp.zeros_like(prior_kv[0]))
    earlier_rows = earlier.reshape(layer_count - 1, rows_here, block_len, kv_width)
    received_early = lax.all_to_all(
        route_blocks(dispatch[: layer_count - 1], earlier_rows), "seq", 0, 0, tiled=True
    )
    portion = lax.all_gather(tokens, "dec", axis=0, tiled=True)
    flattened = portion.reshape(-1, portion.shape[-1])
    positions = (jnp.arange(NEW_TOK, dtype=jnp.int32) + req_length).astype(jnp.float32)
    inverse_freq = ROPE_BASE ** (-(jnp.arange(0, HD, 2, dtype=jnp.float32) / HD))
    angles = positions[:, None] * inverse_freq
    cosine, sine = jnp.cos(angles), jnp.sin(angles)
    signed_sine = jnp.concatenate([-sine, sine], axis=-1)
    head_cos = jnp.concatenate([cosine, cosine], axis=-1)
    cos_q = jnp.tile(head_cos, (1, query_cols // HD))
    sin_q = jnp.tile(signed_sine, (1, query_cols // HD))
    cos_kv = jnp.tile(jnp.concatenate([head_cos, jnp.ones_like(head_cos)], axis=-1), (1, heads_here))
    sin_kv = jnp.tile(
        jnp.concatenate([signed_sine, jnp.zeros_like(signed_sine)], axis=-1), (1, heads_here)
    )
    queries, fresh_rows, fresh_keys_t = project(
        flattened, norm_gain, w_query, w_keyval, cos_q, sin_q, cos_kv, sin_kv
    )
    received_early, queries = lax.optimization_barrier((received_early, queries))
    cached = kv_cache[0]
    padded = jnp.pad(cached, ((0, 0), (0, span_len - cached.shape[1]), (0, 0)))
    kept_cache = jnp.where((slot_ids < req_length)[None, :, None], padded, jnp.zeros_like(padded))
    assembled = lax.dynamic_update_slice(
        kept_cache, fresh_rows, (zero_index, req_length, zero_index)
    )
    group_size = query_cols // HD // heads_here
    product = attend(
        req_length.reshape(1),
        queries,
        jnp.transpose(cached[:, :, :HD], (0, 2, 1)),
        cached,
        fresh_keys_t,
        fresh_rows,
        w_out,
        group_size,
    )
    summed = lax.psum_scatter(
        product.reshape(NEW_TOK, 1, product.shape[-1]),
        "dec",
        scatter_dimension=0,
        tiled=True,
    )
    current_rows = assembled.reshape(1, rows_here, block_len, kv_width)
    received_last = lax.all_to_all(
        route_blocks(dispatch[layer_count - 1 :], current_rows), "seq", 0, 0, tiled=True
    )
    received = jnp.concatenate(
        [
            received_early.reshape(owner_count, layer_count - 1, capacity, block_len, kv_width),
            received_last.reshape(owner_count, 1, capacity, block_len, kv_width),
        ],
        axis=1,
    )
    decode_pool = jnp.transpose(received, (1, 0, 2, 3, 4)).reshape(
        1, 1, layer_count, owner_count, capacity, block_len, kv_width
    )
    return (summed, decode_pool)


def solution(mesh):
    in_specs = (
        P("dec", "seq", None),
        P(),
        P(),
        P(None, "dec"),
        P(None, "dec"),
        P("dec", None),
        P("seq", "dec", None, None),
        P("seq", None, "dec", None, None),
        P("seq", None, "dec", None, None),
    )
    out_specs = (P("dec", "seq", None), P("seq", "dec", None, None, None, None, None))
    return jax.shard_map(local, mesh=mesh, in_specs=in_specs, out_specs=out_specs, check_vma=False)
```

```python
import functools

import jax
import jax.numpy as jnp
from jax import lax
from jax.experimental import pallas as pl
from jax.experimental.pallas import tpu as pltpu
from jax.sharding import PartitionSpec as P

HD = 64
NEW_TOK = 512


EPSILON = 1e-06
ROPE_BASE = 10000.0


def rotate(values, angles):
    half_dim = values.shape[-1] // 2
    first_half = values[..., :half_dim]
    second_half = values[..., half_dim:]
    cosine = jnp.cos(angles)
    sine_part = jnp.sin(angles)
    return jnp.concatenate(
        [
            first_half * cosine - second_half * sine_part,
            second_half * cosine + first_half * sine_part,
        ],
        axis=-1,
    )


def route_blocks(dispatch_table, block_data):
    layers = dispatch_table.shape[0]
    same_layer = jnp.eye(layers, dtype=dispatch_table.dtype)
    spread = dispatch_table[:, :, :, None, :] * same_layer[:, None, None, :, None]
    moved_blocks = jnp.einsum(
        "locms,msbw->olcbw", spread, block_data, preferred_element_type=jnp.float32
    ).astype(jnp.bfloat16)
    shape = moved_blocks.shape
    return moved_blocks.reshape(shape[0], shape[1] * shape[2] * shape[3], shape[4])


def swap_halves(values, half):
    lane = lax.broadcasted_iota(jnp.int32, values.shape, 1)
    width = values.shape[1]
    wanted = jnp.where((lane % (2 * half)) < half, lane + half, lane - half)
    ahead = pltpu.roll(values, half, 1)
    behind = pltpu.roll(values, width - half, 1)
    ahead_lane = pltpu.roll(lane, half, 1)
    return jnp.where(ahead_lane == wanted, ahead, behind)


def project_kernel(
    x_ref, gain_ref, wq_ref, wkv_ref, cq_ref, sq_ref, ckv_ref, skv_ref, q_out, kv_out, kt_out
):
    widened = x_ref[...].astype(jnp.float32)
    scale = lax.rsqrt(jnp.mean(widened * widened, axis=-1, keepdims=True) + EPSILON)
    x = (widened * scale * gain_ref[...]).astype(jnp.bfloat16)
    query = jnp.dot(x, wq_ref[...], preferred_element_type=jnp.float32)
    q_out[...] = (query * cq_ref[...] + swap_halves(query, HD // 2) * sq_ref[...]).astype(
        q_out.dtype
    )
    key_value = jnp.dot(x, wkv_ref[...], preferred_element_type=jnp.float32)
    rotated = key_value * ckv_ref[...] + swap_halves(key_value, HD // 2) * skv_ref[...]
    width = kv_out.shape[2]
    for head_index in range(kv_out.shape[0]):
        block = rotated[:, head_index * width : (head_index + 1) * width].astype(kv_out.dtype)
        kv_out[head_index] = block
        kt_out[head_index] = block[:, :HD].astype(jnp.float32).T.astype(kt_out.dtype)


def project(x, gain, w_query, w_keyval, cos_q, sin_q, cos_kv, sin_kv, tile=256):
    tokens, depth = x.shape
    q_cols, kv_cols = w_query.shape[1], w_keyval.shape[1]
    heads = kv_cols // (2 * HD)
    row_spec = lambda cols: pl.BlockSpec((tile, cols), lambda i: (i, 0))
    return pl.pallas_call(
        project_kernel,
        out_shape=(
            jax.ShapeDtypeStruct((tokens, q_cols), jnp.bfloat16),
            jax.ShapeDtypeStruct((heads, tokens, 2 * HD), jnp.bfloat16),
            jax.ShapeDtypeStruct((heads, HD, tokens), jnp.bfloat16),
        ),
        grid=(tokens // tile,),
        in_specs=[
            row_spec(depth),
            pl.BlockSpec((depth,), lambda i: (0,)),
            pl.BlockSpec((depth, q_cols), lambda i: (0, 0)),
            pl.BlockSpec((depth, kv_cols), lambda i: (0, 0)),
            row_spec(q_cols),
            row_spec(q_cols),
            row_spec(kv_cols),
            row_spec(kv_cols),
        ],
        out_specs=(
            row_spec(q_cols),
            pl.BlockSpec((heads, tile, 2 * HD), lambda i: (0, i, 0)),
            pl.BlockSpec((heads, HD, tile), lambda i: (0, 0, i)),
        ),
        cost_estimate=pl.CostEstimate(
            flops=2 * tokens * depth * (q_cols + kv_cols),
            transcendentals=0,
            bytes_accessed=2 * (x.size + w_query.size + w_keyval.size)
            + 8 * tokens * (q_cols + kv_cols),
        ),
    )(x, gain, w_query, w_keyval, cos_q, sin_q, cos_kv, sin_kv)


def attend_tile(length_ref, q_ref, kt_ref, kv_ref, ktf_ref, kvf_ref, ctx_ref, *, tile, scale, group, tile_index):
    span = kt_ref.shape[2]
    fresh = min(ktf_ref.shape[2], (tile_index + 1) * tile)
    pair = 2 * HD
    slot = lax.broadcasted_iota(jnp.int32, (1, span), 1)
    cached_bias = jnp.where(slot < length_ref[0], 0.0, -jnp.inf).astype(jnp.float32)
    token = lax.broadcasted_iota(jnp.int32, (tile, fresh), 0) + tile_index * tile
    new_slot = lax.broadcasted_iota(jnp.int32, (tile, fresh), 1)
    fresh_bias = jnp.where(new_slot <= token, 0.0, -jnp.inf).astype(jnp.float32)
    lane = lax.broadcasted_iota(jnp.int32, (tile, pair), 1)
    for pair_index in range(q_ref.shape[1] // pair):
        both = q_ref[:, pair_index * pair : (pair_index + 1) * pair]
        halves = []
        for parity in range(2):
            head = (2 * pair_index + parity) // group
            lined = (both if parity == 0 else pltpu.roll(both, HD, 1))[:, :HD]
            lined = lined * jnp.asarray(scale, lined.dtype)
            old = jnp.dot(lined, kt_ref[head], preferred_element_type=jnp.float32) + cached_bias
            new = jnp.dot(lined, ktf_ref[head][:, :fresh], preferred_element_type=jnp.float32) + fresh_bias
            row_max = jnp.maximum(
                jnp.max(old, axis=-1, keepdims=True), jnp.max(new, axis=-1, keepdims=True)
            )
            old_w = jnp.exp(old - row_max)
            new_w = jnp.exp(new - row_max)
            row_total = jnp.sum(old_w, axis=-1, keepdims=True) + jnp.sum(
                new_w, axis=-1, keepdims=True
            )
            mixed = jnp.dot(
                old_w.astype(jnp.bfloat16), kv_ref[head], preferred_element_type=jnp.float32
            ) + jnp.dot(new_w.astype(jnp.bfloat16), kvf_ref[head][:fresh], preferred_element_type=jnp.float32)
            halves.append((mixed, row_total))
        (even, even_total), (odd, odd_total) = halves
        joined = jnp.where(lane < HD, pltpu.roll(even, HD, 1) / even_total, odd / odd_total)
        ctx_ref[:, pair_index * pair : (pair_index + 1) * pair] = joined.astype(ctx_ref.dtype)


def attention_kernel(
    length_ref, q_ref, kt_ref, kv_ref, ktf_ref, kvf_ref, wo_ref, out_ref, ctx_ref, *, tile, scale, group, q_tiles
):
    tile_index = pl.program_id(0)
    for static_tile in range(q_tiles):

        @pl.when(tile_index == static_tile)
        def _():
            attend_tile(
                length_ref, q_ref, kt_ref, kv_ref, ktf_ref, kvf_ref, ctx_ref,
                tile=tile, scale=scale, group=group, tile_index=static_tile,
            )

    out_ref[...] = jnp.dot(ctx_ref[...], wo_ref[...], preferred_element_type=jnp.float32).astype(
        out_ref.dtype
    )


def attend(length, queries, keys_t, cache, fresh_keys_t, fresh, w_out, group, tile=256):
    tokens, q_cols = queries.shape
    span = cache.shape[1] + fresh.shape[1]
    model = w_out.shape[1]
    kernel = functools.partial(
        attention_kernel, tile=tile, scale=HD ** (-0.5), group=group, q_tiles=tokens // tile
    )
    flops = 4 * tokens * q_cols * span + 2 * tokens * q_cols * model
    whole = lambda shape: pl.BlockSpec(shape, lambda i, n: (0,) * len(shape))
    return pl.pallas_call(
        kernel,
        out_shape=jax.ShapeDtypeStruct((tokens, model), jnp.bfloat16),
        grid_spec=pltpu.PrefetchScalarGridSpec(
            num_scalar_prefetch=1,
            grid=(tokens // tile,),
            in_specs=[
                pl.BlockSpec((tile, q_cols), lambda i, n: (i, 0)),
                whole(keys_t.shape),
                whole(cache.shape),
                whole(fresh_keys_t.shape),
                whole(fresh.shape),
                whole(w_out.shape),
            ],
            out_specs=pl.BlockSpec((tile, model), lambda i, n: (i, 0)),
            scratch_shapes=[pltpu.VMEM((tile, q_cols), jnp.bfloat16)],
        ),
        cost_estimate=pl.CostEstimate(
            flops=flops,
            transcendentals=tokens * (q_cols // HD) * span,
            bytes_accessed=2
            * (queries.size + keys_t.size + cache.size + fresh_keys_t.size + fresh.size + w_out.size)
            + 2 * tokens * model,
        ),
    )(length, queries, keys_t, cache, fresh_keys_t, fresh, w_out)


def norm_kernel(x_ref, gain_ref, out_ref):
    widened = x_ref[...].astype(jnp.float32)
    scale = lax.rsqrt(jnp.mean(widened * widened, axis=-1, keepdims=True) + EPSILON)
    out_ref[...] = (widened * scale * gain_ref[...]).astype(out_ref.dtype)


def rms_norm(x, gain):
    return pl.pallas_call(
        norm_kernel,
        out_shape=jax.ShapeDtypeStruct(x.shape, jnp.bfloat16),
        cost_estimate=pl.CostEstimate(
            flops=4 * x.size, transcendentals=x.shape[0], bytes_accessed=4 * x.size
        ),
    )(x, gain)


def local(tokens, norm_gain, lengths, w_query, w_keyval, w_out, kv_cache, prior_kv, owners):
    query_cols = w_query.shape[1]
    heads_here = kv_cache.shape[1]
    layer_count = owners.shape[1]
    block_count = owners.shape[3]
    span_len = prior_kv.shape[3]
    block_len = span_len // block_count
    kv_width = 2 * HD
    rows_here = heads_here * block_count
    owner_count = lax.axis_size("seq")
    capacity = (rows_here + owner_count - 1) // owner_count
    req_length = lengths[lax.axis_index("seq")]
    slot_ids = jnp.arange(span_len, dtype=jnp.int32)
    zero_index = jnp.zeros((), jnp.int32)
    owner_rows = owners[0, :, :, :, 0].reshape(layer_count, rows_here)
    owner_hits = (owner_rows[:, :, None] == jnp.arange(owner_count, dtype=jnp.int32)).astype(
        jnp.int32
    )
    owner_rank = jnp.sum((jnp.cumsum(owner_hits, axis=1) - owner_hits) * owner_hits, axis=-1)
    slot_index = owner_rows * capacity + owner_rank
    dispatch = (
        slot_index[:, None, :] == jnp.arange(owner_count * capacity, dtype=jnp.int32)[None, :, None]
    ).astype(jnp.bfloat16)
    dispatch = dispatch.reshape(layer_count, owner_count, capacity, rows_here)
    live_mask = (slot_ids < req_length + NEW_TOK)[None, None, :, None]
    earlier = jnp.where(live_mask, prior_kv[0], jnp.zeros_like(prior_kv[0]))
    earlier_rows = earlier.reshape(layer_count - 1, rows_here, block_len, kv_width)
    received_early = lax.all_to_all(
        route_blocks(dispatch[: layer_count - 1], earlier_rows), "seq", 0, 0, tiled=True
    )
    portion = lax.all_gather(tokens, "dec", axis=0, tiled=True)
    flattened = portion.reshape(-1, portion.shape[-1])
    positions = (jnp.arange(NEW_TOK, dtype=jnp.int32) + req_length).astype(jnp.float32)
    inverse_freq = ROPE_BASE ** (-(jnp.arange(0, HD, 2, dtype=jnp.float32) / HD))
    angles = positions[:, None] * inverse_freq
    cosine, sine = jnp.cos(angles), jnp.sin(angles)
    signed_sine = jnp.concatenate([-sine, sine], axis=-1)
    head_cos = jnp.concatenate([cosine, cosine], axis=-1)
    cos_q = jnp.tile(head_cos, (1, query_cols // HD))
    sin_q = jnp.tile(signed_sine, (1, query_cols // HD))
    cos_kv = jnp.tile(jnp.concatenate([head_cos, jnp.ones_like(head_cos)], axis=-1), (1, heads_here))
    sin_kv = jnp.tile(
        jnp.concatenate([signed_sine, jnp.zeros_like(signed_sine)], axis=-1), (1, heads_here)
    )
    queries, fresh_rows, fresh_keys_t = project(
        flattened, norm_gain, w_query, w_keyval, cos_q, sin_q, cos_kv, sin_kv
    )
    received_early, queries = lax.optimization_barrier((received_early, queries))
    cached = kv_cache[0]
    padded = jnp.pad(cached, ((0, 0), (0, span_len - cached.shape[1]), (0, 0)))
    kept_cache = jnp.where((slot_ids < req_length)[None, :, None], padded, jnp.zeros_like(padded))
    assembled = lax.dynamic_update_slice(
        kept_cache, fresh_rows, (zero_index, req_length, zero_index)
    )
    group_size = query_cols // HD // heads_here
    product = attend(
        req_length.reshape(1),
        queries,
        jnp.transpose(cached[:, :, :HD], (0, 2, 1)),
        cached,
        fresh_keys_t,
        fresh_rows,
        w_out,
        group_size,
    )
    summed = lax.psum_scatter(
        product.reshape(NEW_TOK, 1, product.shape[-1]),
        "dec",
        scatter_dimension=0,
        tiled=True,
    )
    current_rows = assembled.reshape(1, rows_here, block_len, kv_width)
    received_last = lax.all_to_all(
        route_blocks(dispatch[layer_count - 1 :], current_rows), "seq", 0, 0, tiled=True
    )
    received = jnp.concatenate(
        [
            received_early.reshape(owner_count, layer_count - 1, capacity, block_len, kv_width),
            received_last.reshape(owner_count, 1, capacity, block_len, kv_width),
        ],
        axis=1,
    )
    decode_pool = jnp.transpose(received, (1, 0, 2, 3, 4)).reshape(
        1, 1, layer_count, owner_count, capacity, block_len, kv_width
    )
    return (summed, decode_pool)


def solution(mesh):
    in_specs = (
        P("dec", "seq", None),
        P(),
        P(),
        P(None, "dec"),
        P(None, "dec"),
        P("dec", None),
        P("seq", "dec", None, None),
        P("seq", None, "dec", None, None),
        P("seq", None, "dec", None, None),
    )
    out_specs = (P("dec", "seq", None), P("seq", "dec", None, None, None, None, None))
    return jax.shard_map(local, mesh=mesh, in_specs=in_specs, out_specs=out_specs, check_vma=False)
```

```python
import functools

import jax
import jax.numpy as jnp
from jax import lax
from jax.experimental import pallas as pl
from jax.experimental.pallas import tpu as pltpu
from jax.sharding import PartitionSpec as P

HD = 64
NEW_TOK = 512


EPSILON = 1e-06
ROPE_BASE = 10000.0


def rotate(values, angles):
    half_dim = values.shape[-1] // 2
    first_half = values[..., :half_dim]
    second_half = values[..., half_dim:]
    cosine = jnp.cos(angles)
    sine_part = jnp.sin(angles)
    return jnp.concatenate(
        [
            first_half * cosine - second_half * sine_part,
            second_half * cosine + first_half * sine_part,
        ],
        axis=-1,
    )


def route_blocks(dispatch_table, block_data):
    layers = dispatch_table.shape[0]
    same_layer = jnp.eye(layers, dtype=dispatch_table.dtype)
    spread = dispatch_table[:, :, :, None, :] * same_layer[:, None, None, :, None]
    moved_blocks = jnp.einsum(
        "locms,msbw->olcbw", spread, block_data, preferred_element_type=jnp.float32
    ).astype(jnp.bfloat16)
    shape = moved_blocks.shape
    return moved_blocks.reshape(shape[0], shape[1] * shape[2] * shape[3], shape[4])


def swap_halves(values, half):
    lane = lax.broadcasted_iota(jnp.int32, values.shape, 1)
    width = values.shape[1]
    wanted = jnp.where((lane % (2 * half)) < half, lane + half, lane - half)
    ahead = pltpu.roll(values, half, 1)
    behind = pltpu.roll(values, width - half, 1)
    ahead_lane = pltpu.roll(lane, half, 1)
    return jnp.where(ahead_lane == wanted, ahead, behind)


def project_kernel(
    x_ref, gain_ref, wq_ref, wkv_ref, cq_ref, sq_ref, ckv_ref, skv_ref, q_out, kv_out, kt_out
):
    widened = x_ref[...].astype(jnp.float32)
    scale = lax.rsqrt(jnp.mean(widened * widened, axis=-1, keepdims=True) + EPSILON)
    x = (widened * scale * gain_ref[...]).astype(jnp.bfloat16)
    query = jnp.dot(x, wq_ref[...], preferred_element_type=jnp.float32)
    q_out[...] = (query * cq_ref[...] + swap_halves(query, HD // 2) * sq_ref[...]).astype(
        q_out.dtype
    )
    key_value = jnp.dot(x, wkv_ref[...], preferred_element_type=jnp.float32)
    rotated = key_value * ckv_ref[...] + swap_halves(key_value, HD // 2) * skv_ref[...]
    width = kv_out.shape[2]
    for head_index in range(kv_out.shape[0]):
        block = rotated[:, head_index * width : (head_index + 1) * width].astype(kv_out.dtype)
        kv_out[head_index] = block
        kt_out[head_index] = block[:, :HD].astype(jnp.float32).T.astype(kt_out.dtype)


def project(x, gain, w_query, w_keyval, cos_q, sin_q, cos_kv, sin_kv, tile=512):
    tokens, depth = x.shape
    q_cols, kv_cols = w_query.shape[1], w_keyval.shape[1]
    heads = kv_cols // (2 * HD)
    row_spec = lambda cols: pl.BlockSpec((tile, cols), lambda i: (i, 0))
    return pl.pallas_call(
        project_kernel,
        out_shape=(
            jax.ShapeDtypeStruct((tokens, q_cols), jnp.bfloat16),
            jax.ShapeDtypeStruct((heads, tokens, 2 * HD), jnp.bfloat16),
            jax.ShapeDtypeStruct((heads, HD, tokens), jnp.bfloat16),
        ),
        grid=(tokens // tile,),
        in_specs=[
            row_spec(depth),
            pl.BlockSpec((depth,), lambda i: (0,)),
            pl.BlockSpec((depth, q_cols), lambda i: (0, 0)),
            pl.BlockSpec((depth, kv_cols), lambda i: (0, 0)),
            row_spec(q_cols),
            row_spec(q_cols),
            row_spec(kv_cols),
            row_spec(kv_cols),
        ],
        out_specs=(
            row_spec(q_cols),
            pl.BlockSpec((heads, tile, 2 * HD), lambda i: (0, i, 0)),
            pl.BlockSpec((heads, HD, tile), lambda i: (0, 0, i)),
        ),
        cost_estimate=pl.CostEstimate(
            flops=2 * tokens * depth * (q_cols + kv_cols),
            transcendentals=0,
            bytes_accessed=2 * (x.size + w_query.size + w_keyval.size)
            + 8 * tokens * (q_cols + kv_cols),
        ),
    )(x, gain, w_query, w_keyval, cos_q, sin_q, cos_kv, sin_kv)


def attend_tile(length_ref, q_ref, kt_ref, kv_ref, ktf_ref, kvf_ref, ctx_ref, *, tile, scale, group, tile_index):
    span = kt_ref.shape[2]
    fresh = min(ktf_ref.shape[2], (tile_index + 1) * tile)
    pair = 2 * HD
    slot = lax.broadcasted_iota(jnp.int32, (1, span), 1)
    cached_bias = jnp.where(slot < length_ref[0], 0.0, -jnp.inf).astype(jnp.float32)
    token = lax.broadcasted_iota(jnp.int32, (tile, fresh), 0) + tile_index * tile
    new_slot = lax.broadcasted_iota(jnp.int32, (tile, fresh), 1)
    fresh_bias = jnp.where(new_slot <= token, 0.0, -jnp.inf).astype(jnp.float32)
    lane = lax.broadcasted_iota(jnp.int32, (tile, pair), 1)
    for pair_index in range(q_ref.shape[1] // pair):
        both = q_ref[:, pair_index * pair : (pair_index + 1) * pair]
        halves = []
        for parity in range(2):
            head = (2 * pair_index + parity) // group
            lined = (both if parity == 0 else pltpu.roll(both, HD, 1))[:, :HD]
            lined = lined * jnp.asarray(scale, lined.dtype)
            old = jnp.dot(lined, kt_ref[head], preferred_element_type=jnp.float32) + cached_bias
            new = jnp.dot(lined, ktf_ref[head][:, :fresh], preferred_element_type=jnp.float32) + fresh_bias
            row_max = jnp.maximum(
                jnp.max(old, axis=-1, keepdims=True), jnp.max(new, axis=-1, keepdims=True)
            )
            old_w = jnp.exp(old - row_max)
            new_w = jnp.exp(new - row_max)
            row_total = jnp.sum(old_w, axis=-1, keepdims=True) + jnp.sum(
                new_w, axis=-1, keepdims=True
            )
            mixed = jnp.dot(
                old_w.astype(jnp.bfloat16), kv_ref[head], preferred_element_type=jnp.float32
            ) + jnp.dot(new_w.astype(jnp.bfloat16), kvf_ref[head][:fresh], preferred_element_type=jnp.float32)
            halves.append((mixed, row_total))
        (even, even_total), (odd, odd_total) = halves
        joined = jnp.where(lane < HD, pltpu.roll(even, HD, 1) / even_total, odd / odd_total)
        ctx_ref[:, pair_index * pair : (pair_index + 1) * pair] = joined.astype(ctx_ref.dtype)


def attention_kernel(
    length_ref, q_ref, kt_ref, kv_ref, ktf_ref, kvf_ref, wo_ref, out_ref, ctx_ref, *, tile, scale, group, q_tiles
):
    tile_index = pl.program_id(0)
    for static_tile in range(q_tiles):

        @pl.when(tile_index == static_tile)
        def _():
            attend_tile(
                length_ref, q_ref, kt_ref, kv_ref, ktf_ref, kvf_ref, ctx_ref,
                tile=tile, scale=scale, group=group, tile_index=static_tile,
            )

    out_ref[...] = jnp.dot(ctx_ref[...], wo_ref[...], preferred_element_type=jnp.float32).astype(
        out_ref.dtype
    )


def attend(length, queries, keys_t, cache, fresh_keys_t, fresh, w_out, group, tile=256):
    tokens, q_cols = queries.shape
    span = cache.shape[1] + fresh.shape[1]
    model = w_out.shape[1]
    kernel = functools.partial(
        attention_kernel, tile=tile, scale=HD ** (-0.5), group=group, q_tiles=tokens // tile
    )
    flops = 4 * tokens * q_cols * span + 2 * tokens * q_cols * model
    whole = lambda shape: pl.BlockSpec(shape, lambda i, n: (0,) * len(shape))
    return pl.pallas_call(
        kernel,
        out_shape=jax.ShapeDtypeStruct((tokens, model), jnp.bfloat16),
        grid_spec=pltpu.PrefetchScalarGridSpec(
            num_scalar_prefetch=1,
            grid=(tokens // tile,),
            in_specs=[
                pl.BlockSpec((tile, q_cols), lambda i, n: (i, 0)),
                whole(keys_t.shape),
                whole(cache.shape),
                whole(fresh_keys_t.shape),
                whole(fresh.shape),
                whole(w_out.shape),
            ],
            out_specs=pl.BlockSpec((tile, model), lambda i, n: (i, 0)),
            scratch_shapes=[pltpu.VMEM((tile, q_cols), jnp.bfloat16)],
        ),
        cost_estimate=pl.CostEstimate(
            flops=flops,
            transcendentals=tokens * (q_cols // HD) * span,
            bytes_accessed=2
            * (queries.size + keys_t.size + cache.size + fresh_keys_t.size + fresh.size + w_out.size)
            + 2 * tokens * model,
        ),
    )(length, queries, keys_t, cache, fresh_keys_t, fresh, w_out)


def norm_kernel(x_ref, gain_ref, out_ref):
    widened = x_ref[...].astype(jnp.float32)
    scale = lax.rsqrt(jnp.mean(widened * widened, axis=-1, keepdims=True) + EPSILON)
    out_ref[...] = (widened * scale * gain_ref[...]).astype(out_ref.dtype)


def rms_norm(x, gain):
    return pl.pallas_call(
        norm_kernel,
        out_shape=jax.ShapeDtypeStruct(x.shape, jnp.bfloat16),
        cost_estimate=pl.CostEstimate(
            flops=4 * x.size, transcendentals=x.shape[0], bytes_accessed=4 * x.size
        ),
    )(x, gain)


def local(tokens, norm_gain, lengths, w_query, w_keyval, w_out, kv_cache, prior_kv, owners):
    query_cols = w_query.shape[1]
    heads_here = kv_cache.shape[1]
    layer_count = owners.shape[1]
    block_count = owners.shape[3]
    span_len = prior_kv.shape[3]
    block_len = span_len // block_count
    kv_width = 2 * HD
    rows_here = heads_here * block_count
    owner_count = lax.axis_size("seq")
    capacity = (rows_here + owner_count - 1) // owner_count
    req_length = lengths[lax.axis_index("seq")]
    slot_ids = jnp.arange(span_len, dtype=jnp.int32)
    zero_index = jnp.zeros((), jnp.int32)
    owner_rows = owners[0, :, :, :, 0].reshape(layer_count, rows_here)
    owner_hits = (owner_rows[:, :, None] == jnp.arange(owner_count, dtype=jnp.int32)).astype(
        jnp.int32
    )
    owner_rank = jnp.sum((jnp.cumsum(owner_hits, axis=1) - owner_hits) * owner_hits, axis=-1)
    slot_index = owner_rows * capacity + owner_rank
    dispatch = (
        slot_index[:, None, :] == jnp.arange(owner_count * capacity, dtype=jnp.int32)[None, :, None]
    ).astype(jnp.bfloat16)
    dispatch = dispatch.reshape(layer_count, owner_count, capacity, rows_here)
    live_mask = (slot_ids < req_length + NEW_TOK)[None, None, :, None]
    earlier = jnp.where(live_mask, prior_kv[0], jnp.zeros_like(prior_kv[0]))
    earlier_rows = earlier.reshape(layer_count - 1, rows_here, block_len, kv_width)
    received_early = lax.all_to_all(
        route_blocks(dispatch[: layer_count - 1], earlier_rows), "seq", 0, 0, tiled=True
    )
    portion = lax.all_gather(tokens, "dec", axis=0, tiled=True)
    flattened = portion.reshape(-1, portion.shape[-1])
    positions = (jnp.arange(NEW_TOK, dtype=jnp.int32) + req_length).astype(jnp.float32)
    inverse_freq = ROPE_BASE ** (-(jnp.arange(0, HD, 2, dtype=jnp.float32) / HD))
    angles = positions[:, None] * inverse_freq
    cosine, sine = jnp.cos(angles), jnp.sin(angles)
    signed_sine = jnp.concatenate([-sine, sine], axis=-1)
    head_cos = jnp.concatenate([cosine, cosine], axis=-1)
    cos_q = jnp.tile(head_cos, (1, query_cols // HD))
    sin_q = jnp.tile(signed_sine, (1, query_cols // HD))
    cos_kv = jnp.tile(jnp.concatenate([head_cos, jnp.ones_like(head_cos)], axis=-1), (1, heads_here))
    sin_kv = jnp.tile(
        jnp.concatenate([signed_sine, jnp.zeros_like(signed_sine)], axis=-1), (1, heads_here)
    )
    queries, fresh_rows, fresh_keys_t = project(
        flattened, norm_gain, w_query, w_keyval, cos_q, sin_q, cos_kv, sin_kv
    )
    received_early, queries = lax.optimization_barrier((received_early, queries))
    cached = kv_cache[0]
    padded = jnp.pad(cached, ((0, 0), (0, span_len - cached.shape[1]), (0, 0)))
    kept_cache = jnp.where((slot_ids < req_length)[None, :, None], padded, jnp.zeros_like(padded))
    assembled = lax.dynamic_update_slice(
        kept_cache, fresh_rows, (zero_index, req_length, zero_index)
    )
    group_size = query_cols // HD // heads_here
    product = attend(
        req_length.reshape(1),
        queries,
        jnp.transpose(cached[:, :, :HD], (0, 2, 1)),
        cached,
        fresh_keys_t,
        fresh_rows,
        w_out,
        group_size,
    )
    summed = lax.psum_scatter(
        product.reshape(NEW_TOK, 1, product.shape[-1]),
        "dec",
        scatter_dimension=0,
        tiled=True,
    )
    current_rows = assembled.reshape(1, rows_here, block_len, kv_width)
    received_last = lax.all_to_all(
        route_blocks(dispatch[layer_count - 1 :], current_rows), "seq", 0, 0, tiled=True
    )
    received = jnp.concatenate(
        [
            received_early.reshape(owner_count, layer_count - 1, capacity, block_len, kv_width),
            received_last.reshape(owner_count, 1, capacity, block_len, kv_width),
        ],
        axis=1,
    )
    decode_pool = jnp.transpose(received, (1, 0, 2, 3, 4)).reshape(
        1, 1, layer_count, owner_count, capacity, block_len, kv_width
    )
    return (summed, decode_pool)


def solution(mesh):
    in_specs = (
        P("dec", "seq", None),
        P(),
        P(),
        P(None, "dec"),
        P(None, "dec"),
        P("dec", None),
        P("seq", "dec", None, None),
        P("seq", None, "dec", None, None),
        P("seq", None, "dec", None, None),
    )
    out_specs = (P("dec", "seq", None), P("seq", "dec", None, None, None, None, None))
    return jax.shard_map(local, mesh=mesh, in_specs=in_specs, out_specs=out_specs, check_vma=False)
```

```python
import functools

import jax
import jax.numpy as jnp
from jax import lax
from jax.experimental import pallas as pl
from jax.experimental.pallas import tpu as pltpu
from jax.sharding import PartitionSpec as P

HD = 64
NEW_TOK = 512


EPSILON = 1e-06
ROPE_BASE = 10000.0


def rotate(values, angles):
    half_dim = values.shape[-1] // 2
    first_half = values[..., :half_dim]
    second_half = values[..., half_dim:]
    cosine = jnp.cos(angles)
    sine_part = jnp.sin(angles)
    return jnp.concatenate(
        [
            first_half * cosine - second_half * sine_part,
            second_half * cosine + first_half * sine_part,
        ],
        axis=-1,
    )


def route_blocks(dispatch_table, block_data):
    layers = dispatch_table.shape[0]
    same_layer = jnp.eye(layers, dtype=dispatch_table.dtype)
    spread = dispatch_table[:, :, :, None, :] * same_layer[:, None, None, :, None]
    moved_blocks = jnp.einsum(
        "locms,msbw->olcbw", spread, block_data, preferred_element_type=jnp.float32
    ).astype(jnp.bfloat16)
    shape = moved_blocks.shape
    return moved_blocks.reshape(shape[0], shape[1] * shape[2] * shape[3], shape[4])


def swap_halves(values, half):
    lane = lax.broadcasted_iota(jnp.int32, values.shape, 1)
    width = values.shape[1]
    wanted = jnp.where((lane % (2 * half)) < half, lane + half, lane - half)
    ahead = pltpu.roll(values, half, 1)
    behind = pltpu.roll(values, width - half, 1)
    ahead_lane = pltpu.roll(lane, half, 1)
    return jnp.where(ahead_lane == wanted, ahead, behind)


def project_kernel(
    x_ref, gain_ref, wq_ref, wkv_ref, cq_ref, sq_ref, ckv_ref, skv_ref, q_out, kv_out, kt_out
):
    widened = x_ref[...].astype(jnp.float32)
    scale = lax.rsqrt(jnp.mean(widened * widened, axis=-1, keepdims=True) + EPSILON)
    x = (widened * scale * gain_ref[...]).astype(jnp.bfloat16)
    query = jnp.dot(x, wq_ref[...], preferred_element_type=jnp.float32)
    repeat = lambda ref, cols: jnp.concatenate([ref[...]] * (cols // ref.shape[1]), axis=1)
    q_cols, kv_cols = query.shape[1], wkv_ref.shape[1]
    q_out[...] = (
        query * repeat(cq_ref, q_cols) + swap_halves(query, HD // 2) * repeat(sq_ref, q_cols)
    ).astype(q_out.dtype)
    key_value = jnp.dot(x, wkv_ref[...], preferred_element_type=jnp.float32)
    rotated = key_value * repeat(ckv_ref, kv_cols) + swap_halves(key_value, HD // 2) * repeat(
        skv_ref, kv_cols
    )
    width = kv_out.shape[2]
    for head_index in range(kv_out.shape[0]):
        block = rotated[:, head_index * width : (head_index + 1) * width].astype(kv_out.dtype)
        kv_out[head_index] = block
        kt_out[head_index] = block[:, :HD].astype(jnp.float32).T.astype(kt_out.dtype)


def project(x, gain, w_query, w_keyval, cos_q, sin_q, cos_kv, sin_kv, tile=256):
    tokens, depth = x.shape
    q_cols, kv_cols = w_query.shape[1], w_keyval.shape[1]
    heads = kv_cols // (2 * HD)
    row_spec = lambda cols: pl.BlockSpec((tile, cols), lambda i: (i, 0))
    return pl.pallas_call(
        project_kernel,
        out_shape=(
            jax.ShapeDtypeStruct((tokens, q_cols), jnp.bfloat16),
            jax.ShapeDtypeStruct((heads, tokens, 2 * HD), jnp.bfloat16),
            jax.ShapeDtypeStruct((heads, HD, tokens), jnp.bfloat16),
        ),
        grid=(tokens // tile,),
        in_specs=[
            row_spec(depth),
            pl.BlockSpec((depth,), lambda i: (0,)),
            pl.BlockSpec((depth, q_cols), lambda i: (0, 0)),
            pl.BlockSpec((depth, kv_cols), lambda i: (0, 0)),
            row_spec(cos_q.shape[1]),
            row_spec(sin_q.shape[1]),
            row_spec(cos_kv.shape[1]),
            row_spec(sin_kv.shape[1]),
        ],
        out_specs=(
            row_spec(q_cols),
            pl.BlockSpec((heads, tile, 2 * HD), lambda i: (0, i, 0)),
            pl.BlockSpec((heads, HD, tile), lambda i: (0, 0, i)),
        ),
        cost_estimate=pl.CostEstimate(
            flops=2 * tokens * depth * (q_cols + kv_cols),
            transcendentals=0,
            bytes_accessed=2 * (x.size + w_query.size + w_keyval.size)
            + 4 * (cos_q.size + sin_q.size + cos_kv.size + sin_kv.size),
        ),
    )(x, gain, w_query, w_keyval, cos_q, sin_q, cos_kv, sin_kv)


def attend_tile(length_ref, q_ref, kt_ref, kv_ref, ktf_ref, kvf_ref, ctx_ref, *, tile, scale, group, tile_index):
    span = kt_ref.shape[2]
    fresh = min(ktf_ref.shape[2], (tile_index + 1) * tile)
    pair = 2 * HD
    slot = lax.broadcasted_iota(jnp.int32, (1, span), 1)
    cached_bias = jnp.where(slot < length_ref[0], 0.0, -jnp.inf).astype(jnp.float32)
    token = lax.broadcasted_iota(jnp.int32, (tile, fresh), 0) + tile_index * tile
    new_slot = lax.broadcasted_iota(jnp.int32, (tile, fresh), 1)
    fresh_bias = jnp.where(new_slot <= token, 0.0, -jnp.inf).astype(jnp.float32)
    lane = lax.broadcasted_iota(jnp.int32, (tile, pair), 1)
    for pair_index in range(q_ref.shape[1] // pair):
        both = q_ref[:, pair_index * pair : (pair_index + 1) * pair]
        halves = []
        for parity in range(2):
            head = (2 * pair_index + parity) // group
            lined = (both if parity == 0 else pltpu.roll(both, HD, 1))[:, :HD]
            lined = lined * jnp.asarray(scale, lined.dtype)
            old = jnp.dot(lined, kt_ref[head], preferred_element_type=jnp.float32) + cached_bias
            new = jnp.dot(lined, ktf_ref[head][:, :fresh], preferred_element_type=jnp.float32) + fresh_bias
            row_max = jnp.maximum(
                jnp.max(old, axis=-1, keepdims=True), jnp.max(new, axis=-1, keepdims=True)
            )
            old_w = jnp.exp(old - row_max)
            new_w = jnp.exp(new - row_max)
            row_total = jnp.sum(old_w, axis=-1, keepdims=True) + jnp.sum(
                new_w, axis=-1, keepdims=True
            )
            mixed = jnp.dot(
                old_w.astype(jnp.bfloat16), kv_ref[head], preferred_element_type=jnp.float32
            ) + jnp.dot(new_w.astype(jnp.bfloat16), kvf_ref[head][:fresh], preferred_element_type=jnp.float32)
            halves.append((mixed, row_total))
        (even, even_total), (odd, odd_total) = halves
        joined = jnp.where(lane < HD, pltpu.roll(even, HD, 1) / even_total, odd / odd_total)
        ctx_ref[:, pair_index * pair : (pair_index + 1) * pair] = joined.astype(ctx_ref.dtype)


def attention_kernel(
    length_ref, q_ref, kt_ref, kv_ref, ktf_ref, kvf_ref, wo_ref, out_ref, ctx_ref, *, tile, scale, group, q_tiles
):
    tile_index = pl.program_id(0)
    for static_tile in range(q_tiles):

        @pl.when(tile_index == static_tile)
        def _():
            attend_tile(
                length_ref, q_ref, kt_ref, kv_ref, ktf_ref, kvf_ref, ctx_ref,
                tile=tile, scale=scale, group=group, tile_index=static_tile,
            )

    out_ref[...] = jnp.dot(ctx_ref[...], wo_ref[...], preferred_element_type=jnp.float32).astype(
        out_ref.dtype
    )


def attend(length, queries, keys_t, cache, fresh_keys_t, fresh, w_out, group, tile=256):
    tokens, q_cols = queries.shape
    span = cache.shape[1] + fresh.shape[1]
    model = w_out.shape[1]
    kernel = functools.partial(
        attention_kernel, tile=tile, scale=HD ** (-0.5), group=group, q_tiles=tokens // tile
    )
    flops = 4 * tokens * q_cols * span + 2 * tokens * q_cols * model
    whole = lambda shape: pl.BlockSpec(shape, lambda i, n: (0,) * len(shape))
    return pl.pallas_call(
        kernel,
        out_shape=jax.ShapeDtypeStruct((tokens, model), jnp.bfloat16),
        grid_spec=pltpu.PrefetchScalarGridSpec(
            num_scalar_prefetch=1,
            grid=(tokens // tile,),
            in_specs=[
                pl.BlockSpec((tile, q_cols), lambda i, n: (i, 0)),
                whole(keys_t.shape),
                whole(cache.shape),
                whole(fresh_keys_t.shape),
                whole(fresh.shape),
                whole(w_out.shape),
            ],
            out_specs=pl.BlockSpec((tile, model), lambda i, n: (i, 0)),
            scratch_shapes=[pltpu.VMEM((tile, q_cols), jnp.bfloat16)],
        ),
        cost_estimate=pl.CostEstimate(
            flops=flops,
            transcendentals=tokens * (q_cols // HD) * span,
            bytes_accessed=2
            * (queries.size + keys_t.size + cache.size + fresh_keys_t.size + fresh.size + w_out.size)
            + 2 * tokens * model,
        ),
    )(length, queries, keys_t, cache, fresh_keys_t, fresh, w_out)


def norm_kernel(x_ref, gain_ref, out_ref):
    widened = x_ref[...].astype(jnp.float32)
    scale = lax.rsqrt(jnp.mean(widened * widened, axis=-1, keepdims=True) + EPSILON)
    out_ref[...] = (widened * scale * gain_ref[...]).astype(out_ref.dtype)


def rms_norm(x, gain):
    return pl.pallas_call(
        norm_kernel,
        out_shape=jax.ShapeDtypeStruct(x.shape, jnp.bfloat16),
        cost_estimate=pl.CostEstimate(
            flops=4 * x.size, transcendentals=x.shape[0], bytes_accessed=4 * x.size
        ),
    )(x, gain)


def local(tokens, norm_gain, lengths, w_query, w_keyval, w_out, kv_cache, prior_kv, owners):
    query_cols = w_query.shape[1]
    heads_here = kv_cache.shape[1]
    layer_count = owners.shape[1]
    block_count = owners.shape[3]
    span_len = prior_kv.shape[3]
    block_len = span_len // block_count
    kv_width = 2 * HD
    rows_here = heads_here * block_count
    owner_count = lax.axis_size("seq")
    capacity = (rows_here + owner_count - 1) // owner_count
    req_length = lengths[lax.axis_index("seq")]
    slot_ids = jnp.arange(span_len, dtype=jnp.int32)
    zero_index = jnp.zeros((), jnp.int32)
    owner_rows = owners[0, :, :, :, 0].reshape(layer_count, rows_here)
    owner_hits = (owner_rows[:, :, None] == jnp.arange(owner_count, dtype=jnp.int32)).astype(
        jnp.int32
    )
    owner_rank = jnp.sum((jnp.cumsum(owner_hits, axis=1) - owner_hits) * owner_hits, axis=-1)
    slot_index = owner_rows * capacity + owner_rank
    dispatch = (
        slot_index[:, None, :] == jnp.arange(owner_count * capacity, dtype=jnp.int32)[None, :, None]
    ).astype(jnp.bfloat16)
    dispatch = dispatch.reshape(layer_count, owner_count, capacity, rows_here)
    live_mask = (slot_ids < req_length + NEW_TOK)[None, None, :, None]
    earlier = jnp.where(live_mask, prior_kv[0], jnp.zeros_like(prior_kv[0]))
    earlier_rows = earlier.reshape(layer_count - 1, rows_here, block_len, kv_width)
    received_early = lax.all_to_all(
        route_blocks(dispatch[: layer_count - 1], earlier_rows), "seq", 0, 0, tiled=True
    )
    portion = lax.all_gather(tokens, "dec", axis=0, tiled=True)
    flattened = portion.reshape(-1, portion.shape[-1])
    positions = (jnp.arange(NEW_TOK, dtype=jnp.int32) + req_length).astype(jnp.float32)
    inverse_freq = ROPE_BASE ** (-(jnp.arange(0, HD, 2, dtype=jnp.float32) / HD))
    angles = positions[:, None] * inverse_freq
    cosine, sine = jnp.cos(angles), jnp.sin(angles)
    signed_sine = jnp.concatenate([-sine, sine], axis=-1)
    head_cos = jnp.concatenate([cosine, cosine], axis=-1)
    cos_q = jnp.concatenate([head_cos, head_cos], axis=-1)
    sin_q = jnp.concatenate([signed_sine, signed_sine], axis=-1)
    cos_kv = jnp.concatenate([head_cos, jnp.ones_like(head_cos)], axis=-1)
    sin_kv = jnp.concatenate([signed_sine, jnp.zeros_like(signed_sine)], axis=-1)
    queries, fresh_rows, fresh_keys_t = project(
        flattened, norm_gain, w_query, w_keyval, cos_q, sin_q, cos_kv, sin_kv
    )
    received_early, queries = lax.optimization_barrier((received_early, queries))
    cached = kv_cache[0]
    padded = jnp.pad(cached, ((0, 0), (0, span_len - cached.shape[1]), (0, 0)))
    kept_cache = jnp.where((slot_ids < req_length)[None, :, None], padded, jnp.zeros_like(padded))
    assembled = lax.dynamic_update_slice(
        kept_cache, fresh_rows, (zero_index, req_length, zero_index)
    )
    group_size = query_cols // HD // heads_here
    product = attend(
        req_length.reshape(1),
        queries,
        jnp.transpose(cached[:, :, :HD], (0, 2, 1)),
        cached,
        fresh_keys_t,
        fresh_rows,
        w_out,
        group_size,
    )
    summed = lax.psum_scatter(
        product.reshape(NEW_TOK, 1, product.shape[-1]),
        "dec",
        scatter_dimension=0,
        tiled=True,
    )
    current_rows = assembled.reshape(1, rows_here, block_len, kv_width)
    received_last = lax.all_to_all(
        route_blocks(dispatch[layer_count - 1 :], current_rows), "seq", 0, 0, tiled=True
    )
    received = jnp.concatenate(
        [
            received_early.reshape(owner_count, layer_count - 1, capacity, block_len, kv_width),
            received_last.reshape(owner_count, 1, capacity, block_len, kv_width),
        ],
        axis=1,
    )
    decode_pool = jnp.transpose(received, (1, 0, 2, 3, 4)).reshape(
        1, 1, layer_count, owner_count, capacity, block_len, kv_width
    )
    return (summed, decode_pool)


def solution(mesh):
    in_specs = (
        P("dec", "seq", None),
        P(),
        P(),
        P(None, "dec"),
        P(None, "dec"),
        P("dec", None),
        P("seq", "dec", None, None),
        P("seq", None, "dec", None, None),
        P("seq", None, "dec", None, None),
    )
    out_specs = (P("dec", "seq", None), P("seq", "dec", None, None, None, None, None))
    return jax.shard_map(local, mesh=mesh, in_specs=in_specs, out_specs=out_specs, check_vma=False)
```

```python
import functools

import jax
import jax.numpy as jnp
from jax import lax
from jax.experimental import pallas as pl
from jax.experimental.pallas import tpu as pltpu
from jax.sharding import PartitionSpec as P

HD = 64
NEW_TOK = 512


EPSILON = 1e-06
ROPE_BASE = 10000.0


def rotate(values, angles):
    half_dim = values.shape[-1] // 2
    first_half = values[..., :half_dim]
    second_half = values[..., half_dim:]
    cosine = jnp.cos(angles)
    sine_part = jnp.sin(angles)
    return jnp.concatenate(
        [
            first_half * cosine - second_half * sine_part,
            second_half * cosine + first_half * sine_part,
        ],
        axis=-1,
    )


def route_blocks(dispatch_table, block_data):
    layers = dispatch_table.shape[0]
    same_layer = jnp.eye(layers, dtype=dispatch_table.dtype)
    spread = dispatch_table[:, :, :, None, :] * same_layer[:, None, None, :, None]
    moved_blocks = jnp.einsum(
        "locms,msbw->olcbw", spread, block_data, preferred_element_type=jnp.float32
    ).astype(jnp.bfloat16)
    shape = moved_blocks.shape
    return moved_blocks.reshape(shape[0], shape[1] * shape[2] * shape[3], shape[4])


def swap_halves(values, half):
    lane = lax.broadcasted_iota(jnp.int32, values.shape, 1)
    width = values.shape[1]
    wanted = jnp.where((lane % (2 * half)) < half, lane + half, lane - half)
    ahead = pltpu.roll(values, half, 1)
    behind = pltpu.roll(values, width - half, 1)
    ahead_lane = pltpu.roll(lane, half, 1)
    return jnp.where(ahead_lane == wanted, ahead, behind)


def project_kernel(
    x_ref, gain_ref, wq_ref, wkv_ref, cq_ref, sq_ref, ckv_ref, skv_ref, q_out, kv_out, kt_out
):
    widened = x_ref[...].astype(jnp.float32)
    scale = lax.rsqrt(jnp.mean(widened * widened, axis=-1, keepdims=True) + EPSILON)
    x = (widened * scale * gain_ref[...]).astype(jnp.bfloat16)
    query = jnp.dot(x, wq_ref[...], preferred_element_type=jnp.float32)
    repeat = lambda ref, cols: jnp.concatenate([ref[...]] * (cols // ref.shape[1]), axis=1)
    q_cols, kv_cols = query.shape[1], wkv_ref.shape[1]
    q_out[...] = (
        query * repeat(cq_ref, q_cols) + swap_halves(query, HD // 2) * repeat(sq_ref, q_cols)
    ).astype(q_out.dtype)
    key_value = jnp.dot(x, wkv_ref[...], preferred_element_type=jnp.float32)
    rotated = key_value * repeat(ckv_ref, kv_cols) + swap_halves(key_value, HD // 2) * repeat(
        skv_ref, kv_cols
    )
    width = kv_out.shape[2]
    for head_index in range(kv_out.shape[0]):
        block = rotated[:, head_index * width : (head_index + 1) * width].astype(kv_out.dtype)
        kv_out[head_index] = block
        kt_out[head_index] = block[:, :HD].astype(jnp.float32).T.astype(kt_out.dtype)


def project(x, gain, w_query, w_keyval, cos_q, sin_q, cos_kv, sin_kv, tile=256):
    tokens, depth = x.shape
    q_cols, kv_cols = w_query.shape[1], w_keyval.shape[1]
    heads = kv_cols // (2 * HD)
    row_spec = lambda cols: pl.BlockSpec((tile, cols), lambda i: (i, 0))
    return pl.pallas_call(
        project_kernel,
        out_shape=(
            jax.ShapeDtypeStruct((tokens, q_cols), jnp.bfloat16),
            jax.ShapeDtypeStruct((heads, tokens, 2 * HD), jnp.bfloat16),
            jax.ShapeDtypeStruct((heads, HD, tokens), jnp.bfloat16),
        ),
        grid=(tokens // tile,),
        in_specs=[
            row_spec(depth),
            pl.BlockSpec((depth,), lambda i: (0,)),
            pl.BlockSpec((depth, q_cols), lambda i: (0, 0)),
            pl.BlockSpec((depth, kv_cols), lambda i: (0, 0)),
            row_spec(cos_q.shape[1]),
            row_spec(sin_q.shape[1]),
            row_spec(cos_kv.shape[1]),
            row_spec(sin_kv.shape[1]),
        ],
        out_specs=(
            row_spec(q_cols),
            pl.BlockSpec((heads, tile, 2 * HD), lambda i: (0, i, 0)),
            pl.BlockSpec((heads, HD, tile), lambda i: (0, 0, i)),
        ),
        cost_estimate=pl.CostEstimate(
            flops=2 * tokens * depth * (q_cols + kv_cols),
            transcendentals=0,
            bytes_accessed=2 * (x.size + w_query.size + w_keyval.size)
            + 4 * (cos_q.size + sin_q.size + cos_kv.size + sin_kv.size),
        ),
    )(x, gain, w_query, w_keyval, cos_q, sin_q, cos_kv, sin_kv)


def attend_tile(length_ref, q_ref, kt_ref, kv_ref, ktf_ref, kvf_ref, ctx_ref, *, tile, scale, group, tile_index):
    span = kt_ref.shape[2]
    fresh = min(ktf_ref.shape[2], (tile_index + 1) * tile)
    pair = 2 * HD
    slot = lax.broadcasted_iota(jnp.int32, (1, span), 1)
    cached_bias = jnp.where(slot < length_ref[0], 0.0, -jnp.inf).astype(jnp.float32)
    token = lax.broadcasted_iota(jnp.int32, (tile, fresh), 0) + tile_index * tile
    new_slot = lax.broadcasted_iota(jnp.int32, (tile, fresh), 1)
    fresh_bias = jnp.where(new_slot <= token, 0.0, -jnp.inf).astype(jnp.float32)
    lane = lax.broadcasted_iota(jnp.int32, (tile, pair), 1)
    for pair_index in range(q_ref.shape[1] // pair):
        both = q_ref[:, pair_index * pair : (pair_index + 1) * pair]
        halves = []
        for parity in range(2):
            head = (2 * pair_index + parity) // group
            lined = (both if parity == 0 else pltpu.roll(both, HD, 1))[:, :HD]
            lined = lined * jnp.asarray(scale, lined.dtype)
            old = jnp.dot(lined, kt_ref[head], preferred_element_type=jnp.float32) + cached_bias
            new = jnp.dot(lined, ktf_ref[head][:, :fresh], preferred_element_type=jnp.float32) + fresh_bias
            row_max = jnp.maximum(
                jnp.max(old, axis=-1, keepdims=True), jnp.max(new, axis=-1, keepdims=True)
            )
            old_w = jnp.exp(old - row_max)
            new_w = jnp.exp(new - row_max)
            row_total = jnp.sum(old_w, axis=-1, keepdims=True) + jnp.sum(
                new_w, axis=-1, keepdims=True
            )
            mixed = jnp.dot(
                old_w.astype(jnp.bfloat16), kv_ref[head], preferred_element_type=jnp.float32
            ) + jnp.dot(new_w.astype(jnp.bfloat16), kvf_ref[head][:fresh], preferred_element_type=jnp.float32)
            halves.append((mixed, row_total))
        (even, even_total), (odd, odd_total) = halves
        joined = jnp.where(lane < HD, pltpu.roll(even, HD, 1) / even_total, odd / odd_total)
        ctx_ref[:, pair_index * pair : (pair_index + 1) * pair] = joined.astype(ctx_ref.dtype)


def attention_kernel(
    length_ref, q_ref, kt_ref, kv_ref, ktf_ref, kvf_ref, wo_ref, out_ref, ctx_ref, *, tile, scale, group, q_tiles
):
    tile_index = pl.program_id(0)
    for static_tile in range(q_tiles):

        @pl.when(tile_index == static_tile)
        def _():
            attend_tile(
                length_ref, q_ref, kt_ref, kv_ref, ktf_ref, kvf_ref, ctx_ref,
                tile=tile, scale=scale, group=group, tile_index=static_tile,
            )

    out_ref[...] = jnp.dot(ctx_ref[...], wo_ref[...], preferred_element_type=jnp.float32).astype(
        out_ref.dtype
    )


def attend(length, queries, keys_t, cache, fresh_keys_t, fresh, w_out, group, tile=256):
    tokens, q_cols = queries.shape
    span = cache.shape[1] + fresh.shape[1]
    model = w_out.shape[1]
    kernel = functools.partial(
        attention_kernel, tile=tile, scale=HD ** (-0.5), group=group, q_tiles=tokens // tile
    )
    flops = 4 * tokens * q_cols * span + 2 * tokens * q_cols * model
    whole = lambda shape: pl.BlockSpec(shape, lambda i, n: (0,) * len(shape))
    return pl.pallas_call(
        kernel,
        out_shape=jax.ShapeDtypeStruct((tokens, model), jnp.bfloat16),
        grid_spec=pltpu.PrefetchScalarGridSpec(
            num_scalar_prefetch=1,
            grid=(tokens // tile,),
            in_specs=[
                pl.BlockSpec((tile, q_cols), lambda i, n: (i, 0)),
                whole(keys_t.shape),
                whole(cache.shape),
                whole(fresh_keys_t.shape),
                whole(fresh.shape),
                whole(w_out.shape),
            ],
            out_specs=pl.BlockSpec((tile, model), lambda i, n: (i, 0)),
            scratch_shapes=[pltpu.VMEM((tile, q_cols), jnp.bfloat16)],
        ),
        cost_estimate=pl.CostEstimate(
            flops=flops,
            transcendentals=tokens * (q_cols // HD) * span,
            bytes_accessed=2
            * (queries.size + keys_t.size + cache.size + fresh_keys_t.size + fresh.size + w_out.size)
            + 2 * tokens * model,
        ),
    )(length, queries, keys_t, cache, fresh_keys_t, fresh, w_out)


def fused_kernel(
    length_ref, x_ref, gain_ref, wq_ref, wkv_ref, cq_ref, sq_ref, ckv_ref, skv_ref,
    kt_ref, kv_ref, wo_ref, out_ref, kv_out, kt_out, ktf_ref, kvf_ref, ctx_ref,
    *, tile, scale, group, q_tiles
):
    tile_index = pl.program_id(0)
    widened = x_ref[...].astype(jnp.float32)
    norm_scale = lax.rsqrt(jnp.mean(widened * widened, axis=-1, keepdims=True) + EPSILON)
    x = (widened * norm_scale * gain_ref[...]).astype(jnp.bfloat16)
    query = jnp.dot(x, wq_ref[...], preferred_element_type=jnp.float32)
    repeat = lambda ref, cols: jnp.concatenate([ref[...]] * (cols // ref.shape[1]), axis=1)
    q_cols, kv_cols = query.shape[1], wkv_ref.shape[1]
    queries = (
        query * repeat(cq_ref, q_cols) + swap_halves(query, HD // 2) * repeat(sq_ref, q_cols)
    ).astype(jnp.bfloat16)
    key_value = jnp.dot(x, wkv_ref[...], preferred_element_type=jnp.float32)
    rotated = key_value * repeat(ckv_ref, kv_cols) + swap_halves(key_value, HD // 2) * repeat(
        skv_ref, kv_cols
    )
    width = kv_out.shape[2]
    start = pl.multiple_of(tile_index * tile, tile)
    for head_index in range(kv_out.shape[0]):
        block = rotated[:, head_index * width : (head_index + 1) * width].astype(kv_out.dtype)
        keys_t = block[:, :HD].astype(jnp.float32).T.astype(kt_out.dtype)
        kv_out[head_index] = block
        kt_out[head_index] = keys_t
        kvf_ref[head_index, pl.ds(start, tile), :] = block
        ktf_ref[head_index, :, pl.ds(start, tile)] = keys_t
    for static_tile in range(q_tiles):

        @pl.when(tile_index == static_tile)
        def _():
            attend_tile(
                length_ref, queries, kt_ref, kv_ref, ktf_ref, kvf_ref, ctx_ref,
                tile=tile, scale=scale, group=group, tile_index=static_tile,
            )

    out_ref[...] = jnp.dot(ctx_ref[...], wo_ref[...], preferred_element_type=jnp.float32).astype(
        out_ref.dtype
    )


def project_attend(length, x, gain, w_query, w_keyval, cos_q, sin_q, cos_kv, sin_kv, keys_t, cache, w_out, group, tile=256):
    tokens, depth = x.shape
    q_cols, kv_cols = w_query.shape[1], w_keyval.shape[1]
    heads = kv_cols // (2 * HD)
    model = w_out.shape[1]
    span = cache.shape[1] + tokens
    kernel = functools.partial(
        fused_kernel, tile=tile, scale=HD ** (-0.5), group=group, q_tiles=tokens // tile
    )
    row_spec = lambda cols: pl.BlockSpec((tile, cols), lambda i, n: (i, 0))
    whole = lambda shape: pl.BlockSpec(shape, lambda i, n: (0,) * len(shape))
    return pl.pallas_call(
        kernel,
        out_shape=(
            jax.ShapeDtypeStruct((tokens, model), jnp.bfloat16),
            jax.ShapeDtypeStruct((heads, tokens, 2 * HD), jnp.bfloat16),
            jax.ShapeDtypeStruct((heads, HD, tokens), jnp.bfloat16),
        ),
        grid_spec=pltpu.PrefetchScalarGridSpec(
            num_scalar_prefetch=1,
            grid=(tokens // tile,),
            in_specs=[
                row_spec(depth),
                whole(gain.shape),
                whole(w_query.shape),
                whole(w_keyval.shape),
                row_spec(cos_q.shape[1]),
                row_spec(sin_q.shape[1]),
                row_spec(cos_kv.shape[1]),
                row_spec(sin_kv.shape[1]),
                whole(keys_t.shape),
                whole(cache.shape),
                whole(w_out.shape),
            ],
            out_specs=(
                row_spec(model),
                pl.BlockSpec((heads, tile, 2 * HD), lambda i, n: (0, i, 0)),
                pl.BlockSpec((heads, HD, tile), lambda i, n: (0, 0, i)),
            ),
            scratch_shapes=[
                pltpu.VMEM((heads, HD, tokens), jnp.bfloat16),
                pltpu.VMEM((heads, tokens, 2 * HD), jnp.bfloat16),
                pltpu.VMEM((tile, q_cols), jnp.bfloat16),
            ],
        ),
        cost_estimate=pl.CostEstimate(
            flops=2 * tokens * depth * (q_cols + kv_cols)
            + 4 * tokens * q_cols * span
            + 2 * tokens * q_cols * model,
            transcendentals=tokens * (q_cols // HD) * span,
            bytes_accessed=2 * (x.size + w_query.size + w_keyval.size + keys_t.size + cache.size)
            + 2 * (w_out.size + tokens * model),
        ),
    )(length, x, gain, w_query, w_keyval, cos_q, sin_q, cos_kv, sin_kv, keys_t, cache, w_out)


def norm_kernel(x_ref, gain_ref, out_ref):
    widened = x_ref[...].astype(jnp.float32)
    scale = lax.rsqrt(jnp.mean(widened * widened, axis=-1, keepdims=True) + EPSILON)
    out_ref[...] = (widened * scale * gain_ref[...]).astype(out_ref.dtype)


def rms_norm(x, gain):
    return pl.pallas_call(
        norm_kernel,
        out_shape=jax.ShapeDtypeStruct(x.shape, jnp.bfloat16),
        cost_estimate=pl.CostEstimate(
            flops=4 * x.size, transcendentals=x.shape[0], bytes_accessed=4 * x.size
        ),
    )(x, gain)


def local(tokens, norm_gain, lengths, w_query, w_keyval, w_out, kv_cache, prior_kv, owners):
    query_cols = w_query.shape[1]
    heads_here = kv_cache.shape[1]
    layer_count = owners.shape[1]
    block_count = owners.shape[3]
    span_len = prior_kv.shape[3]
    block_len = span_len // block_count
    kv_width = 2 * HD
    rows_here = heads_here * block_count
    owner_count = lax.axis_size("seq")
    capacity = (rows_here + owner_count - 1) // owner_count
    req_length = lengths[lax.axis_index("seq")]
    slot_ids = jnp.arange(span_len, dtype=jnp.int32)
    zero_index = jnp.zeros((), jnp.int32)
    owner_rows = owners[0, :, :, :, 0].reshape(layer_count, rows_here)
    owner_hits = (owner_rows[:, :, None] == jnp.arange(owner_count, dtype=jnp.int32)).astype(
        jnp.int32
    )
    owner_rank = jnp.sum((jnp.cumsum(owner_hits, axis=1) - owner_hits) * owner_hits, axis=-1)
    slot_index = owner_rows * capacity + owner_rank
    dispatch = (
        slot_index[:, None, :] == jnp.arange(owner_count * capacity, dtype=jnp.int32)[None, :, None]
    ).astype(jnp.bfloat16)
    dispatch = dispatch.reshape(layer_count, owner_count, capacity, rows_here)
    live_mask = (slot_ids < req_length + NEW_TOK)[None, None, :, None]
    earlier = jnp.where(live_mask, prior_kv[0], jnp.zeros_like(prior_kv[0]))
    earlier_rows = earlier.reshape(layer_count - 1, rows_here, block_len, kv_width)
    received_early = lax.all_to_all(
        route_blocks(dispatch[: layer_count - 1], earlier_rows), "seq", 0, 0, tiled=True
    )
    portion = lax.all_gather(tokens, "dec", axis=0, tiled=True)
    flattened = portion.reshape(-1, portion.shape[-1])
    positions = (jnp.arange(NEW_TOK, dtype=jnp.int32) + req_length).astype(jnp.float32)
    inverse_freq = ROPE_BASE ** (-(jnp.arange(0, HD, 2, dtype=jnp.float32) / HD))
    angles = positions[:, None] * inverse_freq
    cosine, sine = jnp.cos(angles), jnp.sin(angles)
    signed_sine = jnp.concatenate([-sine, sine], axis=-1)
    head_cos = jnp.concatenate([cosine, cosine], axis=-1)
    cos_q = jnp.concatenate([head_cos, head_cos], axis=-1)
    sin_q = jnp.concatenate([signed_sine, signed_sine], axis=-1)
    cos_kv = jnp.concatenate([head_cos, jnp.ones_like(head_cos)], axis=-1)
    sin_kv = jnp.concatenate([signed_sine, jnp.zeros_like(signed_sine)], axis=-1)
    cached = kv_cache[0]
    group_size = query_cols // HD // heads_here
    product, fresh_rows, fresh_keys_t = project_attend(
        req_length.reshape(1),
        flattened,
        norm_gain,
        w_query,
        w_keyval,
        cos_q,
        sin_q,
        cos_kv,
        sin_kv,
        jnp.transpose(cached[:, :, :HD], (0, 2, 1)),
        cached,
        w_out,
        group_size,
    )
    received_early, product = lax.optimization_barrier((received_early, product))
    padded = jnp.pad(cached, ((0, 0), (0, span_len - cached.shape[1]), (0, 0)))
    kept_cache = jnp.where((slot_ids < req_length)[None, :, None], padded, jnp.zeros_like(padded))
    assembled = lax.dynamic_update_slice(
        kept_cache, fresh_rows, (zero_index, req_length, zero_index)
    )
    summed = lax.psum_scatter(
        product.reshape(NEW_TOK, 1, product.shape[-1]),
        "dec",
        scatter_dimension=0,
        tiled=True,
    )
    current_rows = assembled.reshape(1, rows_here, block_len, kv_width)
    received_last = lax.all_to_all(
        route_blocks(dispatch[layer_count - 1 :], current_rows), "seq", 0, 0, tiled=True
    )
    received = jnp.concatenate(
        [
            received_early.reshape(owner_count, layer_count - 1, capacity, block_len, kv_width),
            received_last.reshape(owner_count, 1, capacity, block_len, kv_width),
        ],
        axis=1,
    )
    decode_pool = jnp.transpose(received, (1, 0, 2, 3, 4)).reshape(
        1, 1, layer_count, owner_count, capacity, block_len, kv_width
    )
    return (summed, decode_pool)


def solution(mesh):
    in_specs = (
        P("dec", "seq", None),
        P(),
        P(),
        P(None, "dec"),
        P(None, "dec"),
        P("dec", None),
        P("seq", "dec", None, None),
        P("seq", None, "dec", None, None),
        P("seq", None, "dec", None, None),
    )
    out_specs = (P("dec", "seq", None), P("seq", "dec", None, None, None, None, None))
    return jax.shard_map(local, mesh=mesh, in_specs=in_specs, out_specs=out_specs, check_vma=False)
```

```python
import functools

import jax
import jax.numpy as jnp
from jax import lax
from jax.experimental import pallas as pl
from jax.experimental.pallas import tpu as pltpu
from jax.sharding import PartitionSpec as P

HD = 64
NEW_TOK = 512


EPSILON = 1e-06
ROPE_BASE = 10000.0


def rotate(values, angles):
    half_dim = values.shape[-1] // 2
    first_half = values[..., :half_dim]
    second_half = values[..., half_dim:]
    cosine = jnp.cos(angles)
    sine_part = jnp.sin(angles)
    return jnp.concatenate(
        [
            first_half * cosine - second_half * sine_part,
            second_half * cosine + first_half * sine_part,
        ],
        axis=-1,
    )


def route_blocks(dispatch_table, block_data):
    layers = dispatch_table.shape[0]
    same_layer = jnp.eye(layers, dtype=dispatch_table.dtype)
    spread = dispatch_table[:, :, :, None, :] * same_layer[:, None, None, :, None]
    moved_blocks = jnp.einsum(
        "locms,msbw->olcbw", spread, block_data, preferred_element_type=jnp.float32
    ).astype(jnp.bfloat16)
    shape = moved_blocks.shape
    return moved_blocks.reshape(shape[0], shape[1] * shape[2] * shape[3], shape[4])


def swap_halves(values, half):
    lane = lax.broadcasted_iota(jnp.int32, values.shape, 1)
    width = values.shape[1]
    wanted = jnp.where((lane % (2 * half)) < half, lane + half, lane - half)
    ahead = pltpu.roll(values, half, 1)
    behind = pltpu.roll(values, width - half, 1)
    ahead_lane = pltpu.roll(lane, half, 1)
    return jnp.where(ahead_lane == wanted, ahead, behind)


def project_kernel(
    x_ref, gain_ref, wq_ref, wkv_ref, cq_ref, sq_ref, ckv_ref, skv_ref, q_out, kv_out, kt_out
):
    widened = x_ref[...].astype(jnp.float32)
    scale = lax.rsqrt(jnp.mean(widened * widened, axis=-1, keepdims=True) + EPSILON)
    x = (widened * scale * gain_ref[...]).astype(jnp.bfloat16)
    query = jnp.dot(x, wq_ref[...], preferred_element_type=jnp.float32)
    repeat = lambda ref, cols: jnp.concatenate([ref[...]] * (cols // ref.shape[1]), axis=1)
    q_cols, kv_cols = query.shape[1], wkv_ref.shape[1]
    q_out[...] = (
        query * repeat(cq_ref, q_cols) + swap_halves(query, HD // 2) * repeat(sq_ref, q_cols)
    ).astype(q_out.dtype)
    key_value = jnp.dot(x, wkv_ref[...], preferred_element_type=jnp.float32)
    rotated = key_value * repeat(ckv_ref, kv_cols) + swap_halves(key_value, HD // 2) * repeat(
        skv_ref, kv_cols
    )
    width = kv_out.shape[2]
    for head_index in range(kv_out.shape[0]):
        block = rotated[:, head_index * width : (head_index + 1) * width].astype(kv_out.dtype)
        kv_out[head_index] = block
        kt_out[head_index] = block[:, :HD].astype(jnp.float32).T.astype(kt_out.dtype)


def project(x, gain, w_query, w_keyval, cos_q, sin_q, cos_kv, sin_kv, tile=256):
    tokens, depth = x.shape
    q_cols, kv_cols = w_query.shape[1], w_keyval.shape[1]
    heads = kv_cols // (2 * HD)
    row_spec = lambda cols: pl.BlockSpec((tile, cols), lambda i: (i, 0))
    return pl.pallas_call(
        project_kernel,
        out_shape=(
            jax.ShapeDtypeStruct((tokens, q_cols), jnp.bfloat16),
            jax.ShapeDtypeStruct((heads, tokens, 2 * HD), jnp.bfloat16),
            jax.ShapeDtypeStruct((heads, HD, tokens), jnp.bfloat16),
        ),
        grid=(tokens // tile,),
        in_specs=[
            row_spec(depth),
            pl.BlockSpec((depth,), lambda i: (0,)),
            pl.BlockSpec((depth, q_cols), lambda i: (0, 0)),
            pl.BlockSpec((depth, kv_cols), lambda i: (0, 0)),
            row_spec(cos_q.shape[1]),
            row_spec(sin_q.shape[1]),
            row_spec(cos_kv.shape[1]),
            row_spec(sin_kv.shape[1]),
        ],
        out_specs=(
            row_spec(q_cols),
            pl.BlockSpec((heads, tile, 2 * HD), lambda i: (0, i, 0)),
            pl.BlockSpec((heads, HD, tile), lambda i: (0, 0, i)),
        ),
        cost_estimate=pl.CostEstimate(
            flops=2 * tokens * depth * (q_cols + kv_cols),
            transcendentals=0,
            bytes_accessed=2 * (x.size + w_query.size + w_keyval.size)
            + 4 * (cos_q.size + sin_q.size + cos_kv.size + sin_kv.size),
        ),
    )(x, gain, w_query, w_keyval, cos_q, sin_q, cos_kv, sin_kv)


def attend_tile(length_ref, q_ref, kt_ref, kv_ref, ktf_ref, kvf_ref, ctx_ref, *, tile, scale, group, tile_index):
    span = kt_ref.shape[2]
    fresh = min(ktf_ref.shape[2], (tile_index + 1) * tile)
    pair = 2 * HD
    slot = lax.broadcasted_iota(jnp.int32, (1, span), 1)
    cached_bias = jnp.where(slot < length_ref[0], 0.0, -jnp.inf).astype(jnp.float32)
    token = lax.broadcasted_iota(jnp.int32, (tile, fresh), 0) + tile_index * tile
    new_slot = lax.broadcasted_iota(jnp.int32, (tile, fresh), 1)
    fresh_bias = jnp.where(new_slot <= token, 0.0, -jnp.inf).astype(jnp.float32)
    lane = lax.broadcasted_iota(jnp.int32, (tile, pair), 1)
    for pair_index in range(q_ref.shape[1] // pair):
        both = q_ref[:, pair_index * pair : (pair_index + 1) * pair]
        halves = []
        for parity in range(2):
            head = (2 * pair_index + parity) // group
            lined = (both if parity == 0 else pltpu.roll(both, HD, 1))[:, :HD]
            lined = lined * jnp.asarray(scale, lined.dtype)
            old = jnp.dot(lined, kt_ref[head], preferred_element_type=jnp.float32) + cached_bias
            new = jnp.dot(lined, ktf_ref[head][:, :fresh], preferred_element_type=jnp.float32) + fresh_bias
            row_max = jnp.maximum(
                jnp.max(old, axis=-1, keepdims=True), jnp.max(new, axis=-1, keepdims=True)
            )
            old_w = jnp.exp(old - row_max)
            new_w = jnp.exp(new - row_max)
            row_total = jnp.sum(old_w, axis=-1, keepdims=True) + jnp.sum(
                new_w, axis=-1, keepdims=True
            )
            mixed = jnp.dot(
                old_w.astype(jnp.bfloat16), kv_ref[head], preferred_element_type=jnp.float32
            ) + jnp.dot(new_w.astype(jnp.bfloat16), kvf_ref[head][:fresh], preferred_element_type=jnp.float32)
            halves.append((mixed, row_total))
        (even, even_total), (odd, odd_total) = halves
        joined = jnp.where(lane < HD, pltpu.roll(even, HD, 1) / even_total, odd / odd_total)
        ctx_ref[:, pair_index * pair : (pair_index + 1) * pair] = joined.astype(ctx_ref.dtype)


def attention_kernel(
    length_ref, q_ref, kt_ref, kv_ref, ktf_ref, kvf_ref, wo_ref, out_ref, ctx_ref, *, tile, scale, group, q_tiles
):
    tile_index = pl.program_id(0)
    for static_tile in range(q_tiles):

        @pl.when(tile_index == static_tile)
        def _():
            attend_tile(
                length_ref, q_ref, kt_ref, kv_ref, ktf_ref, kvf_ref, ctx_ref,
                tile=tile, scale=scale, group=group, tile_index=static_tile,
            )

    out_ref[...] = jnp.dot(ctx_ref[...], wo_ref[...], preferred_element_type=jnp.float32).astype(
        out_ref.dtype
    )


def attend(length, queries, keys_t, cache, fresh_keys_t, fresh, w_out, group, tile=256):
    tokens, q_cols = queries.shape
    span = cache.shape[1] + fresh.shape[1]
    model = w_out.shape[1]
    kernel = functools.partial(
        attention_kernel, tile=tile, scale=HD ** (-0.5), group=group, q_tiles=tokens // tile
    )
    flops = 4 * tokens * q_cols * span + 2 * tokens * q_cols * model
    whole = lambda shape: pl.BlockSpec(shape, lambda i, n: (0,) * len(shape))
    return pl.pallas_call(
        kernel,
        out_shape=jax.ShapeDtypeStruct((tokens, model), jnp.bfloat16),
        grid_spec=pltpu.PrefetchScalarGridSpec(
            num_scalar_prefetch=1,
            grid=(tokens // tile,),
            in_specs=[
                pl.BlockSpec((tile, q_cols), lambda i, n: (i, 0)),
                whole(keys_t.shape),
                whole(cache.shape),
                whole(fresh_keys_t.shape),
                whole(fresh.shape),
                whole(w_out.shape),
            ],
            out_specs=pl.BlockSpec((tile, model), lambda i, n: (i, 0)),
            scratch_shapes=[pltpu.VMEM((tile, q_cols), jnp.bfloat16)],
        ),
        cost_estimate=pl.CostEstimate(
            flops=flops,
            transcendentals=tokens * (q_cols // HD) * span,
            bytes_accessed=2
            * (queries.size + keys_t.size + cache.size + fresh_keys_t.size + fresh.size + w_out.size)
            + 2 * tokens * model,
        ),
    )(length, queries, keys_t, cache, fresh_keys_t, fresh, w_out)


def fused_kernel(
    length_ref, x_ref, gain_ref, wq_ref, wkv_ref, cq_ref, sq_ref, ckv_ref, skv_ref,
    kt_hbm, kv_hbm, wo_hbm, out_ref, kv_out, kt_out, ktf_ref, kvf_ref, ctx_ref,
    kt_ref, kv_ref, wo_ref, sems,
    *, tile, scale, group, q_tiles
):
    tile_index = pl.program_id(0)
    copies = [
        pltpu.make_async_copy(source, target, sems.at[index])
        for index, (source, target) in enumerate(
            ((kt_hbm, kt_ref), (kv_hbm, kv_ref), (wo_hbm, wo_ref))
        )
    ]

    @pl.when(tile_index == 0)
    def _():
        for copy in copies:
            copy.start()

    widened = x_ref[...].astype(jnp.float32)
    norm_scale = lax.rsqrt(jnp.mean(widened * widened, axis=-1, keepdims=True) + EPSILON)
    x = (widened * norm_scale * gain_ref[...]).astype(jnp.bfloat16)
    query = jnp.dot(x, wq_ref[...], preferred_element_type=jnp.float32)
    repeat = lambda ref, cols: jnp.concatenate([ref[...]] * (cols // ref.shape[1]), axis=1)
    q_cols, kv_cols = query.shape[1], wkv_ref.shape[1]
    queries = (
        query * repeat(cq_ref, q_cols) + swap_halves(query, HD // 2) * repeat(sq_ref, q_cols)
    ).astype(jnp.bfloat16)
    key_value = jnp.dot(x, wkv_ref[...], preferred_element_type=jnp.float32)
    rotated = key_value * repeat(ckv_ref, kv_cols) + swap_halves(key_value, HD // 2) * repeat(
        skv_ref, kv_cols
    )
    width = kv_out.shape[2]
    start = pl.multiple_of(tile_index * tile, tile)
    for head_index in range(kv_out.shape[0]):
        block = rotated[:, head_index * width : (head_index + 1) * width].astype(kv_out.dtype)
        keys_t = block[:, :HD].astype(jnp.float32).T.astype(kt_out.dtype)
        kv_out[head_index] = block
        kt_out[head_index] = keys_t
        kvf_ref[head_index, pl.ds(start, tile), :] = block
        ktf_ref[head_index, :, pl.ds(start, tile)] = keys_t

    @pl.when(tile_index == 0)
    def _():
        for copy in copies:
            copy.wait()

    for static_tile in range(q_tiles):

        @pl.when(tile_index == static_tile)
        def _():
            attend_tile(
                length_ref, queries, kt_ref, kv_ref, ktf_ref, kvf_ref, ctx_ref,
                tile=tile, scale=scale, group=group, tile_index=static_tile,
            )

    out_ref[...] = jnp.dot(ctx_ref[...], wo_ref[...], preferred_element_type=jnp.float32).astype(
        out_ref.dtype
    )


def project_attend(length, x, gain, w_query, w_keyval, cos_q, sin_q, cos_kv, sin_kv, keys_t, cache, w_out, group, tile=256):
    tokens, depth = x.shape
    q_cols, kv_cols = w_query.shape[1], w_keyval.shape[1]
    heads = kv_cols // (2 * HD)
    model = w_out.shape[1]
    span = cache.shape[1] + tokens
    kernel = functools.partial(
        fused_kernel, tile=tile, scale=HD ** (-0.5), group=group, q_tiles=tokens // tile
    )
    row_spec = lambda cols: pl.BlockSpec((tile, cols), lambda i, n: (i, 0))
    whole = lambda shape: pl.BlockSpec(shape, lambda i, n: (0,) * len(shape))
    return pl.pallas_call(
        kernel,
        out_shape=(
            jax.ShapeDtypeStruct((tokens, model), jnp.bfloat16),
            jax.ShapeDtypeStruct((heads, tokens, 2 * HD), jnp.bfloat16),
            jax.ShapeDtypeStruct((heads, HD, tokens), jnp.bfloat16),
        ),
        grid_spec=pltpu.PrefetchScalarGridSpec(
            num_scalar_prefetch=1,
            grid=(tokens // tile,),
            in_specs=[
                row_spec(depth),
                whole(gain.shape),
                whole(w_query.shape),
                whole(w_keyval.shape),
                row_spec(cos_q.shape[1]),
                row_spec(sin_q.shape[1]),
                row_spec(cos_kv.shape[1]),
                row_spec(sin_kv.shape[1]),
                pl.BlockSpec(memory_space=pl.ANY),
                pl.BlockSpec(memory_space=pl.ANY),
                pl.BlockSpec(memory_space=pl.ANY),
            ],
            out_specs=(
                row_spec(model),
                pl.BlockSpec((heads, tile, 2 * HD), lambda i, n: (0, i, 0)),
                pl.BlockSpec((heads, HD, tile), lambda i, n: (0, 0, i)),
            ),
            scratch_shapes=[
                pltpu.VMEM((heads, HD, tokens), jnp.bfloat16),
                pltpu.VMEM((heads, tokens, 2 * HD), jnp.bfloat16),
                pltpu.VMEM((tile, q_cols), jnp.bfloat16),
                pltpu.VMEM(keys_t.shape, keys_t.dtype),
                pltpu.VMEM(cache.shape, cache.dtype),
                pltpu.VMEM(w_out.shape, w_out.dtype),
                pltpu.SemaphoreType.DMA((3,)),
            ],
        ),
        cost_estimate=pl.CostEstimate(
            flops=2 * tokens * depth * (q_cols + kv_cols)
            + 4 * tokens * q_cols * span
            + 2 * tokens * q_cols * model,
            transcendentals=tokens * (q_cols // HD) * span,
            bytes_accessed=2 * (x.size + w_query.size + w_keyval.size + keys_t.size + cache.size)
            + 2 * (w_out.size + tokens * model),
        ),
    )(length, x, gain, w_query, w_keyval, cos_q, sin_q, cos_kv, sin_kv, keys_t, cache, w_out)


def norm_kernel(x_ref, gain_ref, out_ref):
    widened = x_ref[...].astype(jnp.float32)
    scale = lax.rsqrt(jnp.mean(widened * widened, axis=-1, keepdims=True) + EPSILON)
    out_ref[...] = (widened * scale * gain_ref[...]).astype(out_ref.dtype)


def rms_norm(x, gain):
    return pl.pallas_call(
        norm_kernel,
        out_shape=jax.ShapeDtypeStruct(x.shape, jnp.bfloat16),
        cost_estimate=pl.CostEstimate(
            flops=4 * x.size, transcendentals=x.shape[0], bytes_accessed=4 * x.size
        ),
    )(x, gain)


def local(tokens, norm_gain, lengths, w_query, w_keyval, w_out, kv_cache, prior_kv, owners):
    query_cols = w_query.shape[1]
    heads_here = kv_cache.shape[1]
    layer_count = owners.shape[1]
    block_count = owners.shape[3]
    span_len = prior_kv.shape[3]
    block_len = span_len // block_count
    kv_width = 2 * HD
    rows_here = heads_here * block_count
    owner_count = lax.axis_size("seq")
    capacity = (rows_here + owner_count - 1) // owner_count
    req_length = lengths[lax.axis_index("seq")]
    slot_ids = jnp.arange(span_len, dtype=jnp.int32)
    zero_index = jnp.zeros((), jnp.int32)
    owner_rows = owners[0, :, :, :, 0].reshape(layer_count, rows_here)
    owner_hits = (owner_rows[:, :, None] == jnp.arange(owner_count, dtype=jnp.int32)).astype(
        jnp.int32
    )
    owner_rank = jnp.sum((jnp.cumsum(owner_hits, axis=1) - owner_hits) * owner_hits, axis=-1)
    slot_index = owner_rows * capacity + owner_rank
    dispatch = (
        slot_index[:, None, :] == jnp.arange(owner_count * capacity, dtype=jnp.int32)[None, :, None]
    ).astype(jnp.bfloat16)
    dispatch = dispatch.reshape(layer_count, owner_count, capacity, rows_here)
    live_mask = (slot_ids < req_length + NEW_TOK)[None, None, :, None]
    earlier = jnp.where(live_mask, prior_kv[0], jnp.zeros_like(prior_kv[0]))
    earlier_rows = earlier.reshape(layer_count - 1, rows_here, block_len, kv_width)
    received_early = lax.all_to_all(
        route_blocks(dispatch[: layer_count - 1], earlier_rows), "seq", 0, 0, tiled=True
    )
    portion = lax.all_gather(tokens, "dec", axis=0, tiled=True)
    flattened = portion.reshape(-1, portion.shape[-1])
    positions = (jnp.arange(NEW_TOK, dtype=jnp.int32) + req_length).astype(jnp.float32)
    inverse_freq = ROPE_BASE ** (-(jnp.arange(0, HD, 2, dtype=jnp.float32) / HD))
    angles = positions[:, None] * inverse_freq
    cosine, sine = jnp.cos(angles), jnp.sin(angles)
    signed_sine = jnp.concatenate([-sine, sine], axis=-1)
    head_cos = jnp.concatenate([cosine, cosine], axis=-1)
    cos_q = jnp.concatenate([head_cos, head_cos], axis=-1)
    sin_q = jnp.concatenate([signed_sine, signed_sine], axis=-1)
    cos_kv = jnp.concatenate([head_cos, jnp.ones_like(head_cos)], axis=-1)
    sin_kv = jnp.concatenate([signed_sine, jnp.zeros_like(signed_sine)], axis=-1)
    cached = kv_cache[0]
    group_size = query_cols // HD // heads_here
    product, fresh_rows, fresh_keys_t = project_attend(
        req_length.reshape(1),
        flattened,
        norm_gain,
        w_query,
        w_keyval,
        cos_q,
        sin_q,
        cos_kv,
        sin_kv,
        jnp.transpose(cached[:, :, :HD], (0, 2, 1)),
        cached,
        w_out,
        group_size,
    )
    received_early, product = lax.optimization_barrier((received_early, product))
    padded = jnp.pad(cached, ((0, 0), (0, span_len - cached.shape[1]), (0, 0)))
    kept_cache = jnp.where((slot_ids < req_length)[None, :, None], padded, jnp.zeros_like(padded))
    assembled = lax.dynamic_update_slice(
        kept_cache, fresh_rows, (zero_index, req_length, zero_index)
    )
    summed = lax.psum_scatter(
        product.reshape(NEW_TOK, 1, product.shape[-1]),
        "dec",
        scatter_dimension=0,
        tiled=True,
    )
    current_rows = assembled.reshape(1, rows_here, block_len, kv_width)
    received_last = lax.all_to_all(
        route_blocks(dispatch[layer_count - 1 :], current_rows), "seq", 0, 0, tiled=True
    )
    received = jnp.concatenate(
        [
            received_early.reshape(owner_count, layer_count - 1, capacity, block_len, kv_width),
            received_last.reshape(owner_count, 1, capacity, block_len, kv_width),
        ],
        axis=1,
    )
    decode_pool = jnp.transpose(received, (1, 0, 2, 3, 4)).reshape(
        1, 1, layer_count, owner_count, capacity, block_len, kv_width
    )
    return (summed, decode_pool)


def solution(mesh):
    in_specs = (
        P("dec", "seq", None),
        P(),
        P(),
        P(None, "dec"),
        P(None, "dec"),
        P("dec", None),
        P("seq", "dec", None, None),
        P("seq", None, "dec", None, None),
        P("seq", None, "dec", None, None),
    )
    out_specs = (P("dec", "seq", None), P("seq", "dec", None, None, None, None, None))
    return jax.shard_map(local, mesh=mesh, in_specs=in_specs, out_specs=out_specs, check_vma=False)
```

```python
import functools

import jax
import jax.numpy as jnp
from jax import lax
from jax.experimental import pallas as pl
from jax.experimental.pallas import tpu as pltpu
from jax.sharding import PartitionSpec as P

HD = 64
NEW_TOK = 512


EPSILON = 1e-06
ROPE_BASE = 10000.0


def rotate(values, angles):
    half_dim = values.shape[-1] // 2
    first_half = values[..., :half_dim]
    second_half = values[..., half_dim:]
    cosine = jnp.cos(angles)
    sine_part = jnp.sin(angles)
    return jnp.concatenate(
        [
            first_half * cosine - second_half * sine_part,
            second_half * cosine + first_half * sine_part,
        ],
        axis=-1,
    )


def route_blocks(dispatch_table, block_data):
    layers = dispatch_table.shape[0]
    same_layer = jnp.eye(layers, dtype=dispatch_table.dtype)
    spread = dispatch_table[:, :, :, None, :] * same_layer[:, None, None, :, None]
    moved_blocks = jnp.einsum(
        "locms,msbw->olcbw", spread, block_data, preferred_element_type=jnp.float32
    ).astype(jnp.bfloat16)
    shape = moved_blocks.shape
    return moved_blocks.reshape(shape[0], shape[1] * shape[2] * shape[3], shape[4])


def swap_halves(values, half):
    lane = lax.broadcasted_iota(jnp.int32, values.shape, 1)
    width = values.shape[1]
    wanted = jnp.where((lane % (2 * half)) < half, lane + half, lane - half)
    ahead = pltpu.roll(values, half, 1)
    behind = pltpu.roll(values, width - half, 1)
    ahead_lane = pltpu.roll(lane, half, 1)
    return jnp.where(ahead_lane == wanted, ahead, behind)


def project_kernel(
    x_ref, gain_ref, wq_ref, wkv_ref, cq_ref, sq_ref, ckv_ref, skv_ref, q_out, kv_out, kt_out
):
    widened = x_ref[...].astype(jnp.float32)
    scale = lax.rsqrt(jnp.mean(widened * widened, axis=-1, keepdims=True) + EPSILON)
    x = (widened * scale * gain_ref[...]).astype(jnp.bfloat16)
    query = jnp.dot(x, wq_ref[...], preferred_element_type=jnp.float32)
    repeat = lambda ref, cols: jnp.concatenate([ref[...]] * (cols // ref.shape[1]), axis=1)
    q_cols, kv_cols = query.shape[1], wkv_ref.shape[1]
    q_out[...] = (
        query * repeat(cq_ref, q_cols) + swap_halves(query, HD // 2) * repeat(sq_ref, q_cols)
    ).astype(q_out.dtype)
    key_value = jnp.dot(x, wkv_ref[...], preferred_element_type=jnp.float32)
    rotated = key_value * repeat(ckv_ref, kv_cols) + swap_halves(key_value, HD // 2) * repeat(
        skv_ref, kv_cols
    )
    width = kv_out.shape[2]
    for head_index in range(kv_out.shape[0]):
        block = rotated[:, head_index * width : (head_index + 1) * width].astype(kv_out.dtype)
        kv_out[head_index] = block
        kt_out[head_index] = block[:, :HD].astype(jnp.float32).T.astype(kt_out.dtype)


def project(x, gain, w_query, w_keyval, cos_q, sin_q, cos_kv, sin_kv, tile=256):
    tokens, depth = x.shape
    q_cols, kv_cols = w_query.shape[1], w_keyval.shape[1]
    heads = kv_cols // (2 * HD)
    row_spec = lambda cols: pl.BlockSpec((tile, cols), lambda i: (i, 0))
    return pl.pallas_call(
        project_kernel,
        out_shape=(
            jax.ShapeDtypeStruct((tokens, q_cols), jnp.bfloat16),
            jax.ShapeDtypeStruct((heads, tokens, 2 * HD), jnp.bfloat16),
            jax.ShapeDtypeStruct((heads, HD, tokens), jnp.bfloat16),
        ),
        grid=(tokens // tile,),
        in_specs=[
            row_spec(depth),
            pl.BlockSpec((depth,), lambda i: (0,)),
            pl.BlockSpec((depth, q_cols), lambda i: (0, 0)),
            pl.BlockSpec((depth, kv_cols), lambda i: (0, 0)),
            row_spec(cos_q.shape[1]),
            row_spec(sin_q.shape[1]),
            row_spec(cos_kv.shape[1]),
            row_spec(sin_kv.shape[1]),
        ],
        out_specs=(
            row_spec(q_cols),
            pl.BlockSpec((heads, tile, 2 * HD), lambda i: (0, i, 0)),
            pl.BlockSpec((heads, HD, tile), lambda i: (0, 0, i)),
        ),
        cost_estimate=pl.CostEstimate(
            flops=2 * tokens * depth * (q_cols + kv_cols),
            transcendentals=0,
            bytes_accessed=2 * (x.size + w_query.size + w_keyval.size)
            + 4 * (cos_q.size + sin_q.size + cos_kv.size + sin_kv.size),
        ),
    )(x, gain, w_query, w_keyval, cos_q, sin_q, cos_kv, sin_kv)


def attend_tile(length_ref, q_ref, kt_ref, kv_ref, ktf_ref, kvf_ref, ctx_ref, *, tile, scale, group, tile_index):
    span = kt_ref.shape[2]
    fresh = min(ktf_ref.shape[2], (tile_index + 1) * tile)
    pair = 2 * HD
    slot = lax.broadcasted_iota(jnp.int32, (1, span), 1)
    cached_bias = jnp.where(slot < length_ref[0], 0.0, -jnp.inf).astype(jnp.float32)
    token = lax.broadcasted_iota(jnp.int32, (tile, fresh), 0) + tile_index * tile
    new_slot = lax.broadcasted_iota(jnp.int32, (tile, fresh), 1)
    fresh_bias = jnp.where(new_slot <= token, 0.0, -jnp.inf).astype(jnp.float32)
    lane = lax.broadcasted_iota(jnp.int32, (tile, pair), 1)
    for pair_index in range(q_ref.shape[1] // pair):
        both = q_ref[:, pair_index * pair : (pair_index + 1) * pair]
        halves = []
        for parity in range(2):
            head = (2 * pair_index + parity) // group
            lined = (both if parity == 0 else pltpu.roll(both, HD, 1))[:, :HD]
            lined = lined * jnp.asarray(scale, lined.dtype)
            old = jnp.dot(lined, kt_ref[head], preferred_element_type=jnp.float32) + cached_bias
            new = jnp.dot(lined, ktf_ref[head][:, :fresh], preferred_element_type=jnp.float32) + fresh_bias
            row_max = jnp.maximum(
                jnp.max(old, axis=-1, keepdims=True), jnp.max(new, axis=-1, keepdims=True)
            )
            old_w = jnp.exp(old - row_max)
            new_w = jnp.exp(new - row_max)
            row_total = jnp.sum(old_w, axis=-1, keepdims=True) + jnp.sum(
                new_w, axis=-1, keepdims=True
            )
            mixed = jnp.dot(
                old_w.astype(jnp.bfloat16), kv_ref[head], preferred_element_type=jnp.float32
            ) + jnp.dot(new_w.astype(jnp.bfloat16), kvf_ref[head][:fresh], preferred_element_type=jnp.float32)
            halves.append((mixed, row_total))
        (even, even_total), (odd, odd_total) = halves
        joined = jnp.where(lane < HD, pltpu.roll(even, HD, 1) / even_total, odd / odd_total)
        ctx_ref[:, pair_index * pair : (pair_index + 1) * pair] = joined.astype(ctx_ref.dtype)


def attention_kernel(
    length_ref, q_ref, kt_ref, kv_ref, ktf_ref, kvf_ref, wo_ref, out_ref, ctx_ref, *, tile, scale, group, q_tiles
):
    tile_index = pl.program_id(0)
    for static_tile in range(q_tiles):

        @pl.when(tile_index == static_tile)
        def _():
            attend_tile(
                length_ref, q_ref, kt_ref, kv_ref, ktf_ref, kvf_ref, ctx_ref,
                tile=tile, scale=scale, group=group, tile_index=static_tile,
            )

    out_ref[...] = jnp.dot(ctx_ref[...], wo_ref[...], preferred_element_type=jnp.float32).astype(
        out_ref.dtype
    )


def attend(length, queries, keys_t, cache, fresh_keys_t, fresh, w_out, group, tile=256):
    tokens, q_cols = queries.shape
    span = cache.shape[1] + fresh.shape[1]
    model = w_out.shape[1]
    kernel = functools.partial(
        attention_kernel, tile=tile, scale=HD ** (-0.5), group=group, q_tiles=tokens // tile
    )
    flops = 4 * tokens * q_cols * span + 2 * tokens * q_cols * model
    whole = lambda shape: pl.BlockSpec(shape, lambda i, n: (0,) * len(shape))
    return pl.pallas_call(
        kernel,
        out_shape=jax.ShapeDtypeStruct((tokens, model), jnp.bfloat16),
        grid_spec=pltpu.PrefetchScalarGridSpec(
            num_scalar_prefetch=1,
            grid=(tokens // tile,),
            in_specs=[
                pl.BlockSpec((tile, q_cols), lambda i, n: (i, 0)),
                whole(keys_t.shape),
                whole(cache.shape),
                whole(fresh_keys_t.shape),
                whole(fresh.shape),
                whole(w_out.shape),
            ],
            out_specs=pl.BlockSpec((tile, model), lambda i, n: (i, 0)),
            scratch_shapes=[pltpu.VMEM((tile, q_cols), jnp.bfloat16)],
        ),
        cost_estimate=pl.CostEstimate(
            flops=flops,
            transcendentals=tokens * (q_cols // HD) * span,
            bytes_accessed=2
            * (queries.size + keys_t.size + cache.size + fresh_keys_t.size + fresh.size + w_out.size)
            + 2 * tokens * model,
        ),
    )(length, queries, keys_t, cache, fresh_keys_t, fresh, w_out)


def fused_kernel(
    length_ref, x_ref, gain_ref, wq_ref, wkv_ref, cq_ref, sq_ref, ckv_ref, skv_ref,
    kt_ref, kv_ref, wo_ref, out_ref, kv_out, kt_out, ktf_ref, kvf_ref, ctx_ref,
    *, tile, scale, group, q_tiles
):
    tile_index = pl.program_id(0)
    widened = x_ref[...].astype(jnp.float32)
    norm_scale = lax.rsqrt(jnp.mean(widened * widened, axis=-1, keepdims=True) + EPSILON)
    x = (widened * norm_scale * gain_ref[...]).astype(jnp.bfloat16)
    query = jnp.dot(x, wq_ref[...], preferred_element_type=jnp.float32)
    repeat = lambda ref, cols: jnp.concatenate([ref[...]] * (cols // ref.shape[1]), axis=1)
    q_cols, kv_cols = query.shape[1], wkv_ref.shape[1]
    queries = (
        query * repeat(cq_ref, q_cols) + swap_halves(query, HD // 2) * repeat(sq_ref, q_cols)
    ).astype(jnp.bfloat16)
    key_value = jnp.dot(x, wkv_ref[...], preferred_element_type=jnp.float32)
    rotated = key_value * repeat(ckv_ref, kv_cols) + swap_halves(key_value, HD // 2) * repeat(
        skv_ref, kv_cols
    )
    width = kv_out.shape[2]
    start = pl.multiple_of(tile_index * tile, tile)
    for head_index in range(kv_out.shape[0]):
        block = rotated[:, head_index * width : (head_index + 1) * width].astype(kv_out.dtype)
        keys_t = block[:, :HD].astype(jnp.float32).T.astype(kt_out.dtype)
        kv_out[head_index] = block
        kt_out[head_index] = keys_t
        kvf_ref[head_index, pl.ds(start, tile), :] = block
        ktf_ref[head_index, :, pl.ds(start, tile)] = keys_t
    for static_tile in range(q_tiles):

        @pl.when(tile_index == static_tile)
        def _():
            attend_tile(
                length_ref, queries, kt_ref, kv_ref, ktf_ref, kvf_ref, ctx_ref,
                tile=tile, scale=scale, group=group, tile_index=static_tile,
            )

    out_ref[...] = jnp.dot(ctx_ref[...], wo_ref[...], preferred_element_type=jnp.float32).astype(
        out_ref.dtype
    )


def project_attend(length, x, gain, w_query, w_keyval, cos_q, sin_q, cos_kv, sin_kv, keys_t, cache, w_out, group, tile=128):
    tokens, depth = x.shape
    q_cols, kv_cols = w_query.shape[1], w_keyval.shape[1]
    heads = kv_cols // (2 * HD)
    model = w_out.shape[1]
    span = cache.shape[1] + tokens
    kernel = functools.partial(
        fused_kernel, tile=tile, scale=HD ** (-0.5), group=group, q_tiles=tokens // tile
    )
    row_spec = lambda cols: pl.BlockSpec((tile, cols), lambda i, n: (i, 0))
    whole = lambda shape: pl.BlockSpec(shape, lambda i, n: (0,) * len(shape))
    return pl.pallas_call(
        kernel,
        out_shape=(
            jax.ShapeDtypeStruct((tokens, model), jnp.bfloat16),
            jax.ShapeDtypeStruct((heads, tokens, 2 * HD), jnp.bfloat16),
            jax.ShapeDtypeStruct((heads, HD, tokens), jnp.bfloat16),
        ),
        grid_spec=pltpu.PrefetchScalarGridSpec(
            num_scalar_prefetch=1,
            grid=(tokens // tile,),
            in_specs=[
                row_spec(depth),
                whole(gain.shape),
                whole(w_query.shape),
                whole(w_keyval.shape),
                row_spec(cos_q.shape[1]),
                row_spec(sin_q.shape[1]),
                row_spec(cos_kv.shape[1]),
                row_spec(sin_kv.shape[1]),
                whole(keys_t.shape),
                whole(cache.shape),
                whole(w_out.shape),
            ],
            out_specs=(
                row_spec(model),
                pl.BlockSpec((heads, tile, 2 * HD), lambda i, n: (0, i, 0)),
                pl.BlockSpec((heads, HD, tile), lambda i, n: (0, 0, i)),
            ),
            scratch_shapes=[
                pltpu.VMEM((heads, HD, tokens), jnp.bfloat16),
                pltpu.VMEM((heads, tokens, 2 * HD), jnp.bfloat16),
                pltpu.VMEM((tile, q_cols), jnp.bfloat16),
            ],
        ),
        cost_estimate=pl.CostEstimate(
            flops=2 * tokens * depth * (q_cols + kv_cols)
            + 4 * tokens * q_cols * span
            + 2 * tokens * q_cols * model,
            transcendentals=tokens * (q_cols // HD) * span,
            bytes_accessed=2 * (x.size + w_query.size + w_keyval.size + keys_t.size + cache.size)
            + 2 * (w_out.size + tokens * model),
        ),
    )(length, x, gain, w_query, w_keyval, cos_q, sin_q, cos_kv, sin_kv, keys_t, cache, w_out)


def norm_kernel(x_ref, gain_ref, out_ref):
    widened = x_ref[...].astype(jnp.float32)
    scale = lax.rsqrt(jnp.mean(widened * widened, axis=-1, keepdims=True) + EPSILON)
    out_ref[...] = (widened * scale * gain_ref[...]).astype(out_ref.dtype)


def rms_norm(x, gain):
    return pl.pallas_call(
        norm_kernel,
        out_shape=jax.ShapeDtypeStruct(x.shape, jnp.bfloat16),
        cost_estimate=pl.CostEstimate(
            flops=4 * x.size, transcendentals=x.shape[0], bytes_accessed=4 * x.size
        ),
    )(x, gain)


def local(tokens, norm_gain, lengths, w_query, w_keyval, w_out, kv_cache, prior_kv, owners):
    query_cols = w_query.shape[1]
    heads_here = kv_cache.shape[1]
    layer_count = owners.shape[1]
    block_count = owners.shape[3]
    span_len = prior_kv.shape[3]
    block_len = span_len // block_count
    kv_width = 2 * HD
    rows_here = heads_here * block_count
    owner_count = lax.axis_size("seq")
    capacity = (rows_here + owner_count - 1) // owner_count
    req_length = lengths[lax.axis_index("seq")]
    slot_ids = jnp.arange(span_len, dtype=jnp.int32)
    zero_index = jnp.zeros((), jnp.int32)
    owner_rows = owners[0, :, :, :, 0].reshape(layer_count, rows_here)
    owner_hits = (owner_rows[:, :, None] == jnp.arange(owner_count, dtype=jnp.int32)).astype(
        jnp.int32
    )
    owner_rank = jnp.sum((jnp.cumsum(owner_hits, axis=1) - owner_hits) * owner_hits, axis=-1)
    slot_index = owner_rows * capacity + owner_rank
    dispatch = (
        slot_index[:, None, :] == jnp.arange(owner_count * capacity, dtype=jnp.int32)[None, :, None]
    ).astype(jnp.bfloat16)
    dispatch = dispatch.reshape(layer_count, owner_count, capacity, rows_here)
    live_mask = (slot_ids < req_length + NEW_TOK)[None, None, :, None]
    earlier = jnp.where(live_mask, prior_kv[0], jnp.zeros_like(prior_kv[0]))
    earlier_rows = earlier.reshape(layer_count - 1, rows_here, block_len, kv_width)
    received_early = lax.all_to_all(
        route_blocks(dispatch[: layer_count - 1], earlier_rows), "seq", 0, 0, tiled=True
    )
    portion = lax.all_gather(tokens, "dec", axis=0, tiled=True)
    flattened = portion.reshape(-1, portion.shape[-1])
    positions = (jnp.arange(NEW_TOK, dtype=jnp.int32) + req_length).astype(jnp.float32)
    inverse_freq = ROPE_BASE ** (-(jnp.arange(0, HD, 2, dtype=jnp.float32) / HD))
    angles = positions[:, None] * inverse_freq
    cosine, sine = jnp.cos(angles), jnp.sin(angles)
    signed_sine = jnp.concatenate([-sine, sine], axis=-1)
    head_cos = jnp.concatenate([cosine, cosine], axis=-1)
    cos_q = jnp.concatenate([head_cos, head_cos], axis=-1)
    sin_q = jnp.concatenate([signed_sine, signed_sine], axis=-1)
    cos_kv = jnp.concatenate([head_cos, jnp.ones_like(head_cos)], axis=-1)
    sin_kv = jnp.concatenate([signed_sine, jnp.zeros_like(signed_sine)], axis=-1)
    cached = kv_cache[0]
    group_size = query_cols // HD // heads_here
    product, fresh_rows, fresh_keys_t = project_attend(
        req_length.reshape(1),
        flattened,
        norm_gain,
        w_query,
        w_keyval,
        cos_q,
        sin_q,
        cos_kv,
        sin_kv,
        jnp.transpose(cached[:, :, :HD], (0, 2, 1)),
        cached,
        w_out,
        group_size,
    )
    received_early, product = lax.optimization_barrier((received_early, product))
    padded = jnp.pad(cached, ((0, 0), (0, span_len - cached.shape[1]), (0, 0)))
    kept_cache = jnp.where((slot_ids < req_length)[None, :, None], padded, jnp.zeros_like(padded))
    assembled = lax.dynamic_update_slice(
        kept_cache, fresh_rows, (zero_index, req_length, zero_index)
    )
    summed = lax.psum_scatter(
        product.reshape(NEW_TOK, 1, product.shape[-1]),
        "dec",
        scatter_dimension=0,
        tiled=True,
    )
    current_rows = assembled.reshape(1, rows_here, block_len, kv_width)
    received_last = lax.all_to_all(
        route_blocks(dispatch[layer_count - 1 :], current_rows), "seq", 0, 0, tiled=True
    )
    received = jnp.concatenate(
        [
            received_early.reshape(owner_count, layer_count - 1, capacity, block_len, kv_width),
            received_last.reshape(owner_count, 1, capacity, block_len, kv_width),
        ],
        axis=1,
    )
    decode_pool = jnp.transpose(received, (1, 0, 2, 3, 4)).reshape(
        1, 1, layer_count, owner_count, capacity, block_len, kv_width
    )
    return (summed, decode_pool)


def solution(mesh):
    in_specs = (
        P("dec", "seq", None),
        P(),
        P(),
        P(None, "dec"),
        P(None, "dec"),
        P("dec", None),
        P("seq", "dec", None, None),
        P("seq", None, "dec", None, None),
        P("seq", None, "dec", None, None),
    )
    out_specs = (P("dec", "seq", None), P("seq", "dec", None, None, None, None, None))
    return jax.shard_map(local, mesh=mesh, in_specs=in_specs, out_specs=out_specs, check_vma=False)
```
